32 devices in a mesh: stn: 16 (over z, y, core), blk: 2 (over x).
Axes of the slice: x: 2, y: 2, z: 4, core: 2. Of those that a mesh axis runs over, the one named last changes fastest.
Arguments:
- samples: int32 [2, 512, 65536], P(None, 'stn', 'blk'), may hold values from -128 to 127, as said below
- fir_taps: float32 [8, 1024], replicated, may hold values from -2 to 2
- station_order: int32 [512], replicated, may hold values from 0 to 511, each once
Outputs:
- coherence: bfloat16 [2, 1024, 512, 512], P(None, 'stn', 'blk')
The draws below stay inside these ranges and needn't reach their ends.
Inputs may be any that keep to these rules, and one draw needn't show every extreme that they name: `samples`: quantized voltages, real parts in row 0 and imaginary parts in row 1 of the leading dimension. `station_order`: each station number appears exactly once.
All inputs are finite; a program needn't handle non-finite values.
Results may differ from the reference program's by a relative error of at most 0.0033.
Values may be sent and summed in bfloat16 or wider, within the bound.
No kernel may reach another device: no remote copies, remote signals or barrier semaphores. Data moves between devices by JAX's collectives and lax.ppermute only.
A program may use at most 128 MiB of HBM per device.

```python
import math
import jax
import jax.numpy as jnp
from jax import lax

STATIONS = 512
CHANNELS = 1024
TAPS = 8
SPECTRA = 64


source_count = 8


def draw_samples(key, part):
    gain_key = jax.random.fold_in(key, 101)
    signal_key = jax.random.fold_in(key, 202)
    noise_key = jax.random.fold_in(key, 303)
    level_key = jax.random.fold_in(key, 404)
    station_gain = jax.random.randint(gain_key, (STATIONS, source_count), -2, 3)
    signals = jax.random.randint(signal_key, (2, source_count, SPECTRA * CHANNELS), -8, 9)
    noise_level = jax.random.randint(level_key, (STATIONS, 1), 1, 5)
    noise_part = jax.random.randint(noise_key, (2, STATIONS, SPECTRA * CHANNELS), -40, 41)
    noise_part = noise_part * noise_level[None, :, :] // 4
    mixture = jnp.einsum('as,pst->pat', station_gain, signals) + noise_part
    return jnp.clip(mixture, -128, 127).astype(jnp.int32)


def noise(key, dims, deviation, reach, kind=jnp.bfloat16):
    return jnp.clip(deviation * jax.random.normal(key, dims, jnp.float32), -reach, reach).astype(kind)


def setup_inputs(seed: int = 0) -> dict:
    arg_keys = jax.random.split(jax.random.key(seed), 4)
    return {
        "samples": draw_samples(jax.random.fold_in(arg_keys[3], 71), 0),
        "fir_taps": noise(arg_keys[1], (TAPS, CHANNELS), TAPS ** -0.5, 2.0, jnp.float32),
        "station_order": jax.random.permutation(arg_keys[2], STATIONS).astype(jnp.int32),
    }


epsilon = 1e-06

def dft_tables(channels):
    channel_index = jnp.arange(channels, dtype=jnp.int32)
    phase_index = channel_index[:, None] * channel_index[None, :] % channels
    angle_table = phase_index.astype(jnp.float32) * (2.0 * math.pi / channels)
    return (jnp.cos(angle_table).astype(jnp.bfloat16), jnp.sin(angle_table).astype(jnp.bfloat16))

def station_spectra(block_samples, fir_taps, cosine_table, sine_table):
    block_width = block_samples.shape[1]
    frames = block_samples.astype(jnp.float32).reshape(2, block_width, SPECTRA, CHANNELS)
    padded = jnp.concatenate([jnp.zeros((2, block_width, TAPS - 1, CHANNELS), jnp.float32), frames], axis=2)
    filtered = fir_taps[0] * padded[:, :, 0:SPECTRA]
    for tap_index in range(1, TAPS):
        filtered = filtered + fir_taps[tap_index] * padded[:, :, tap_index:tap_index + SPECTRA]
    filtered = lax.optimization_barrier(filtered.astype(jnp.bfloat16)).astype(jnp.float32)
    cosine_part = jnp.einsum('kc,pasc->pksa', cosine_table.astype(jnp.float32), filtered, precision=lax.Precision.HIGHEST)
    sine_part = jnp.einsum('kc,pasc->pksa', sine_table.astype(jnp.float32), filtered, precision=lax.Precision.HIGHEST)
    real_part = cosine_part[0] + sine_part[1]
    imag_part = cosine_part[1] - sine_part[0]
    return jnp.stack([real_part, imag_part]).astype(jnp.bfloat16)

def reference(samples, fir_taps, station_order):
    cosine_table, sine_table = dft_tables(CHANNELS)
    block_width = 16

    def one_block(block_index):
        block_samples = lax.dynamic_slice_in_dim(samples, block_index * block_width, block_width, 1)
        return station_spectra(block_samples, fir_taps, cosine_table, sine_table)
    blocks = lax.map(one_block, jnp.arange(STATIONS // block_width, dtype=jnp.int32))
    spectra = jnp.transpose(blocks, (1, 2, 3, 0, 4)).reshape(2, CHANNELS, SPECTRA, STATIONS)
    ordered = jnp.take(spectra, station_order, axis=3)
    group_width = 16

    def one_group(group_index):
        group_data = lax.dynamic_slice_in_dim(ordered, group_index * group_width, group_width, 1).astype(jnp.float32)
        real_vis = jnp.einsum('pksa,pksb->kab', group_data, group_data, precision=lax.Precision.HIGHEST)
        imag_vis = jnp.einsum('ksa,ksb->kab', group_data[1], group_data[0], precision=lax.Precision.HIGHEST) - jnp.einsum('ksa,ksb->kab', group_data[0], group_data[1], precision=lax.Precision.HIGHEST)
        power_sum = lax.optimization_barrier(jnp.sum(group_data * group_data, axis=(0, 2)))
        scale_row = lax.rsqrt(power_sum + epsilon)
        visibility = jnp.stack([real_vis, imag_vis])
        return (visibility * scale_row[None, :, :, None] * scale_row[None, :, None, :]).astype(jnp.bfloat16)
    groups = lax.map(one_group, jnp.arange(CHANNELS // group_width, dtype=jnp.int32))
    return jnp.transpose(groups, (1, 0, 2, 3, 4)).reshape(2, CHANNELS, STATIONS, STATIONS)
```

```python
import math

import jax
import jax.numpy as jnp
from jax import lax
from jax.experimental import pallas as pl
from jax.sharding import PartitionSpec as P

epsilon = 1e-06


def passed_along(value, axis, steps):
    count = lax.axis_size(axis)
    initial, last = (max(0, -steps), min(count, count - steps))
    return lax.ppermute(value, axis, [(source, source + steps) for source in range(initial, last)])


def chunk_count(local_channels):
    for count in (4, 2):
        if local_channels % count == 0:
            return count
    return 1


def dft_weights(channels, groups, chunks):
    local = channels // groups
    width = local // chunks
    chunk = lax.broadcasted_iota(jnp.int32, (chunks, groups, width, channels), 0)
    group = lax.broadcasted_iota(jnp.int32, (chunks, groups, width, channels), 1)
    inner = lax.broadcasted_iota(jnp.int32, (chunks, groups, width, channels), 2)
    column = lax.broadcasted_iota(jnp.int32, (chunks, groups, width, channels), 3)
    column = lax.optimization_barrier(column)
    row = group * local + chunk * width + inner
    phase_index = row * column % channels
    angle = phase_index.astype(jnp.float32) * (2.0 * math.pi / channels)
    cosine = jnp.cos(angle).astype(jnp.bfloat16)
    sine = jnp.sin(angle).astype(jnp.bfloat16)
    real_rows = jnp.stack([cosine, sine], axis=3)
    imag_rows = jnp.stack([-sine, cosine], axis=3)
    return jnp.stack([real_rows, imag_rows], axis=1)


def correlate_kernel(rows_ref, cols_ref, *refs):
    out_ref = refs[-1]
    row_real = rows_ref[0, 0]
    row_imag = rows_ref[0, 1]
    column_real = cols_ref[0, 0]
    column_imag = cols_ref[1, 0]

    def product(left, right):
        return jnp.dot(left, right, preferred_element_type=jnp.float32)

    real_vis = product(row_real, column_real) + product(row_imag, column_imag)
    imag_vis = product(row_imag, column_real) - product(row_real, column_imag)
    column_real = column_real.astype(jnp.float32)
    column_imag = column_imag.astype(jnp.float32)
    row_real = row_real.astype(jnp.float32)
    row_imag = row_imag.astype(jnp.float32)
    column_power = jnp.sum(column_real * column_real + column_imag * column_imag, axis=0, keepdims=True)
    row_power = jnp.sum(row_real * row_real + row_imag * row_imag, axis=1, keepdims=True)
    scale_row = lax.rsqrt(row_power + epsilon)
    scale_column = lax.rsqrt(column_power + epsilon)
    out_ref[0, 0] = (real_vis * scale_row * scale_column).astype(out_ref.dtype)
    out_ref[1, 0] = (imag_vis * scale_row * scale_column).astype(out_ref.dtype)


def correlate_chunk(rows_t, columns, previous, offset, local_channels):
    width, _, row_count, spectra = rows_t.shape
    stations = columns.shape[3]
    in_specs = [
        pl.BlockSpec((1, 2, row_count, spectra), lambda k: (k, 0, 0, 0)),
        pl.BlockSpec((2, 1, spectra, stations), lambda k: (0, k, 0, 0)),
    ]
    operands = [rows_t, columns]
    aliases = {}
    if previous is not None:
        in_specs.append(pl.BlockSpec(memory_space=pl.ANY))
        operands.append(previous)
        aliases = {2: 0}
    return pl.pallas_call(
        correlate_kernel,
        grid=(width,),
        in_specs=in_specs,
        out_specs=pl.BlockSpec((2, 1, row_count, stations), lambda k: (0, offset + k, 0, 0)),
        out_shape=jax.ShapeDtypeStruct((2, local_channels, row_count, stations), jnp.bfloat16),
        input_output_aliases=aliases,
    )(*operands)


def per_device(samples, fir_taps, station_order):
    tap_count = fir_taps.shape[0]
    channels = fir_taps.shape[1]
    stations_local = samples.shape[1]
    spectra_local = samples.shape[2] // channels
    stations = station_order.shape[0]
    groups = lax.axis_size("stn")
    blocks = lax.axis_size("blk")
    local_channels = channels // groups
    row_count = stations // blocks
    chunks = chunk_count(local_channels)
    width = local_channels // chunks

    frames = samples.reshape(2, stations_local, spectra_local, channels)
    earlier = frames[:, :, spectra_local - (tap_count - 1) :, :].astype(jnp.bfloat16)
    earlier = passed_along(earlier, "blk", 1)
    extended = jnp.concatenate([earlier.astype(jnp.float32), frames.astype(jnp.float32)], axis=2)
    filtered = fir_taps[0] * extended[:, :, 0:spectra_local]
    for tap_index in range(1, tap_count):
        filtered = (
            filtered + fir_taps[tap_index] * extended[:, :, tap_index : tap_index + spectra_local]
        )
    filtered = filtered.astype(jnp.bfloat16)

    weights = dft_weights(channels, groups, chunks)
    selector = (
        station_order[None, :] == jnp.arange(stations, dtype=jnp.int32)[:, None]
    ).astype(jnp.bfloat16)
    selector = selector.reshape(groups, stations_local, stations)
    row_start = lax.axis_index("blk") * row_count

    result = None
    for chunk in range(chunks):
        spectra = jnp.einsum(
            "igkpc,pasc->igksa", weights[chunk], filtered, preferred_element_type=jnp.float32
        ).astype(jnp.bfloat16)
        turned = lax.all_to_all(spectra, "stn", split_axis=1, concat_axis=1, tiled=True)
        ordered = jnp.einsum(
            "igksa,gar->iksr", turned, selector, preferred_element_type=jnp.float32
        ).astype(jnp.bfloat16)
        gathered = lax.all_gather(ordered, "blk", axis=2, tiled=True)
        row_block = lax.dynamic_slice_in_dim(gathered, row_start, row_count, 3)
        rows_t = jnp.transpose(row_block, (1, 0, 3, 2))
        result = correlate_chunk(rows_t, gathered, result, chunk * width, local_channels)
    return result


def solution(mesh):
    placed = (P(None, "stn", "blk"), P(), P())
    return jax.shard_map(
        per_device,
        mesh=mesh,
        in_specs=placed,
        out_specs=P(None, "stn", "blk", None),
        check_vma=False,
    )
```

```python
import math

import jax
import ml_dtypes
import numpy as np
import jax.numpy as jnp
from jax import lax
from jax.experimental import pallas as pl
from jax.sharding import PartitionSpec as P

epsilon = 1e-06


def passed_along(value, axis, steps):
    count = lax.axis_size(axis)
    initial, last = (max(0, -steps), min(count, count - steps))
    return lax.ppermute(value, axis, [(source, source + steps) for source in range(initial, last)])


def chunk_count(local_channels):
    for count in (4, 2):
        if local_channels % count == 0:
            return count
    return 1


def dft_weights(channels, groups, chunks):
    local = channels // groups
    width = local // chunks
    chunk = np.arange(chunks).reshape(chunks, 1, 1, 1)
    group = np.arange(groups).reshape(1, groups, 1, 1)
    inner = np.arange(width).reshape(1, 1, width, 1)
    column = np.arange(channels).reshape(1, 1, 1, channels)
    row = group * local + chunk * width + inner
    phase_index = (row * column % channels).astype(np.float32)
    angle = phase_index * np.float32(2.0 * math.pi / channels)
    cosine = np.cos(angle).astype(ml_dtypes.bfloat16)
    sine = np.sin(angle).astype(ml_dtypes.bfloat16)
    table = np.concatenate([cosine, sine], axis=3)
    return jnp.asarray(table.reshape(chunks, groups * width, 2 * channels))


def fir_kernel(taps_ref, halo_ref, frames_ref, out_ref):
    tap_count = taps_ref.shape[0]
    spectra = frames_ref.shape[2]
    channels = frames_ref.shape[3]
    filtered = []
    for part in range(2):
        extended = jnp.concatenate(
            [halo_ref[part, 0].astype(jnp.float32), frames_ref[part, 0].astype(jnp.float32)], axis=0
        )
        total = taps_ref[0:1, :] * extended[0:spectra]
        for tap_index in range(1, tap_count):
            total = total + taps_ref[tap_index : tap_index + 1, :] * extended[tap_index : tap_index + spectra]
        filtered.append(total.astype(jnp.bfloat16))
    out_ref[0, 0, :, 0:channels] = filtered[0]
    out_ref[0, 0, :, channels:] = filtered[1]
    out_ref[1, 0, :, 0:channels] = filtered[1]
    out_ref[1, 0, :, channels:] = -filtered[0]


def filter_frames(fir_taps, earlier, frames):
    tap_count, channels = fir_taps.shape
    _, stations_local, spectra, _ = frames.shape
    return pl.pallas_call(
        fir_kernel,
        grid=(stations_local,),
        in_specs=[
            pl.BlockSpec((tap_count, channels), lambda a: (0, 0)),
            pl.BlockSpec((2, 1, tap_count - 1, channels), lambda a: (0, a, 0, 0)),
            pl.BlockSpec((2, 1, spectra, channels), lambda a: (0, a, 0, 0)),
        ],
        out_specs=pl.BlockSpec((2, 1, spectra, 2 * channels), lambda a: (0, a, 0, 0)),
        out_shape=jax.ShapeDtypeStruct((2, stations_local, spectra, 2 * channels), jnp.bfloat16),
    )(fir_taps, earlier, frames)


def correlate_kernel(rows_ref, cols_ref, *refs):
    out_ref = refs[-1]
    row_count = out_ref.shape[2]
    left = rows_ref[0]
    right = cols_ref[0]
    product = jnp.dot(left, right, preferred_element_type=jnp.float32)
    right = right.astype(jnp.float32)
    rows = left[0:row_count].astype(jnp.float32)
    column_power = jnp.sum(right * right, axis=0, keepdims=True)
    row_power = jnp.sum(rows * rows, axis=1, keepdims=True)
    scale_row = lax.rsqrt(row_power + epsilon)
    scale_column = lax.rsqrt(column_power + epsilon)
    out_ref[0, 0] = (product[0:row_count] * scale_row * scale_column).astype(out_ref.dtype)
    out_ref[1, 0] = (product[row_count:] * scale_row * scale_column).astype(out_ref.dtype)


def correlate_chunk(left, right, previous, offset, local_channels):
    width, double_rows, depth = left.shape
    row_count = double_rows // 2
    stations = right.shape[2]
    in_specs = [
        pl.BlockSpec((1, double_rows, depth), lambda k: (k, 0, 0)),
        pl.BlockSpec((1, depth, stations), lambda k: (k, 0, 0)),
    ]
    operands = [left, right]
    aliases = {}
    if previous is not None:
        in_specs.append(pl.BlockSpec(memory_space=pl.ANY))
        operands.append(previous)
        aliases = {2: 0}
    return pl.pallas_call(
        correlate_kernel,
        grid=(width,),
        in_specs=in_specs,
        out_specs=pl.BlockSpec((2, 1, row_count, stations), lambda k: (0, offset + k, 0, 0)),
        out_shape=jax.ShapeDtypeStruct((2, local_channels, row_count, stations), jnp.bfloat16),
        input_output_aliases=aliases,
    )(*operands)


def per_device(samples, fir_taps, station_order):
    tap_count = fir_taps.shape[0]
    channels = fir_taps.shape[1]
    stations_local = samples.shape[1]
    spectra_local = samples.shape[2] // channels
    stations = station_order.shape[0]
    groups = lax.axis_size("stn")
    blocks = lax.axis_size("blk")
    local_channels = channels // groups
    row_count = stations // blocks
    chunks = chunk_count(local_channels)
    width = local_channels // chunks

    frames = samples.reshape(2, stations_local, spectra_local, channels)
    earlier = frames[:, :, spectra_local - (tap_count - 1) :, :].astype(jnp.bfloat16)
    earlier = passed_along(earlier, "blk", 1)
    filtered = filter_frames(fir_taps, earlier, frames)
    filtered = filtered.reshape(2 * stations_local * spectra_local, 2 * channels)

    weights = dft_weights(channels, groups, chunks)
    selector = (
        station_order[None, :] == jnp.arange(stations, dtype=jnp.int32)[:, None]
    ).astype(jnp.bfloat16)
    selector = selector.reshape(groups, stations_local, stations)
    row_start = lax.axis_index("blk") * row_count

    def correlate(chunk, gathered, result):
        gathered = gathered.reshape(width, 2, -1, stations)
        row_block = lax.dynamic_slice_in_dim(gathered, row_start, row_count, 3)
        direct = jnp.transpose(row_block, (0, 3, 1, 2))
        swapped = jnp.stack([direct[:, :, 1], -direct[:, :, 0]], axis=2)
        left = jnp.concatenate([direct, swapped], axis=1).reshape(width, 2 * row_count, -1)
        right = gathered.reshape(width, -1, stations)
        return correlate_chunk(left, right, result, chunk * width, local_channels)

    result = None
    pending = []
    for chunk in range(chunks):
        spectra = jnp.einsum(
            "kj,nj->kn", weights[chunk], filtered, preferred_element_type=jnp.float32
        ).astype(jnp.bfloat16)
        spectra = spectra.reshape(groups, width, 2 * stations_local * spectra_local)
        turned = lax.all_to_all(spectra, "stn", split_axis=0, concat_axis=0, tiled=True)
        turned = turned.reshape(groups, width, 2, stations_local, spectra_local)
        ordered = jnp.einsum(
            "gkias,gar->kisr", turned, selector, preferred_element_type=jnp.float32
        ).astype(jnp.bfloat16)
        ordered = ordered.reshape(width * 2, spectra_local, stations)
        if chunk >= 2:
            ordered, result = lax.optimization_barrier((ordered, result))
        pending.append(lax.all_gather(ordered, "blk", axis=1, tiled=True))
        if chunk >= 1:
            result = correlate(chunk - 1, pending[chunk - 1], result)
    result = correlate(chunks - 1, pending[chunks - 1], result)
    return result


def solution(mesh):
    placed = (P(None, "stn", "blk"), P(), P())
    return jax.shard_map(
        per_device,
        mesh=mesh,
        in_specs=placed,
        out_specs=P(None, "stn", "blk", None),
        check_vma=False,
    )
```

```python
import math

import jax
import ml_dtypes
import numpy as np
import jax.numpy as jnp
from jax import lax
from jax.experimental import pallas as pl
from jax.sharding import PartitionSpec as P

epsilon = 1e-06


def passed_along(value, axis, steps):
    count = lax.axis_size(axis)
    initial, last = (max(0, -steps), min(count, count - steps))
    return lax.ppermute(value, axis, [(source, source + steps) for source in range(initial, last)])


def gathered_along(value, axis, dimension):
    count = lax.axis_size(axis)
    parts = [value]
    for shift in range(1, count):
        pairs = [(source, (source + shift) % count) for source in range(count)]
        parts.append(lax.ppermute(value, axis, pairs))
    return jnp.concatenate(parts, axis=dimension)


def chunk_count(local_channels):
    for count in (4, 2):
        if local_channels % count == 0:
            return count
    return 1


def dft_weights(channels, groups, chunks):
    local = channels // groups
    width = local // chunks
    chunk = np.arange(chunks).reshape(chunks, 1, 1, 1)
    group = np.arange(groups).reshape(1, groups, 1, 1)
    inner = np.arange(width).reshape(1, 1, width, 1)
    column = np.arange(channels).reshape(1, 1, 1, channels)
    row = group * local + chunk * width + inner
    phase_index = (row * column % channels).astype(np.float32)
    angle = phase_index * np.float32(2.0 * math.pi / channels)
    cosine = np.cos(angle).astype(ml_dtypes.bfloat16)
    sine = np.sin(angle).astype(ml_dtypes.bfloat16)
    table = np.concatenate([cosine, sine], axis=3)
    return jnp.asarray(table.reshape(chunks, groups * width, 2 * channels))


def fir_kernel(taps_ref, halo_ref, frames_ref, out_ref):
    tap_count = taps_ref.shape[0]
    spectra = frames_ref.shape[2]
    channels = frames_ref.shape[3]
    filtered = []
    for part in range(2):
        extended = jnp.concatenate(
            [halo_ref[part, 0].astype(jnp.float32), frames_ref[part, 0].astype(jnp.float32)], axis=0
        )
        total = taps_ref[0:1, :] * extended[0:spectra]
        for tap_index in range(1, tap_count):
            total = total + taps_ref[tap_index : tap_index + 1, :] * extended[tap_index : tap_index + spectra]
        filtered.append(total.astype(jnp.bfloat16))
    out_ref[0, 0, :, 0:channels] = filtered[0]
    out_ref[0, 0, :, channels:] = filtered[1]
    out_ref[1, 0, :, 0:channels] = filtered[1]
    out_ref[1, 0, :, channels:] = -filtered[0]


def filter_frames(fir_taps, earlier, frames):
    tap_count, channels = fir_taps.shape
    _, stations_local, spectra, _ = frames.shape
    return pl.pallas_call(
        fir_kernel,
        grid=(stations_local,),
        in_specs=[
            pl.BlockSpec((tap_count, channels), lambda a: (0, 0)),
            pl.BlockSpec((2, 1, tap_count - 1, channels), lambda a: (0, a, 0, 0)),
            pl.BlockSpec((2, 1, spectra, channels), lambda a: (0, a, 0, 0)),
        ],
        out_specs=pl.BlockSpec((2, 1, spectra, 2 * channels), lambda a: (0, a, 0, 0)),
        out_shape=jax.ShapeDtypeStruct((2, stations_local, spectra, 2 * channels), jnp.bfloat16),
    )(fir_taps, earlier, frames)


def correlate_kernel(rows_ref, cols_ref, *refs):
    out_ref = refs[-1]
    row_count = out_ref.shape[2]
    left = rows_ref[0]
    right = cols_ref[0]
    product = jnp.dot(left, right, preferred_element_type=jnp.float32)
    right = right.astype(jnp.float32)
    rows = left[0:row_count].astype(jnp.float32)
    column_power = jnp.sum(right * right, axis=0, keepdims=True)
    row_power = jnp.sum(rows * rows, axis=1, keepdims=True)
    scale_row = lax.rsqrt(row_power + epsilon)
    scale_column = lax.rsqrt(column_power + epsilon)
    out_ref[0, 0] = (product[0:row_count] * scale_row * scale_column).astype(out_ref.dtype)
    out_ref[1, 0] = (product[row_count:] * scale_row * scale_column).astype(out_ref.dtype)


def correlate_chunk(left, right, previous, offset, local_channels):
    width, double_rows, depth = left.shape
    row_count = double_rows // 2
    stations = right.shape[2]
    in_specs = [
        pl.BlockSpec((1, double_rows, depth), lambda k: (k, 0, 0)),
        pl.BlockSpec((1, depth, stations), lambda k: (k, 0, 0)),
    ]
    operands = [left, right]
    aliases = {}
    if previous is not None:
        in_specs.append(pl.BlockSpec(memory_space=pl.ANY))
        operands.append(previous)
        aliases = {2: 0}
    return pl.pallas_call(
        correlate_kernel,
        grid=(width,),
        in_specs=in_specs,
        out_specs=pl.BlockSpec((2, 1, row_count, stations), lambda k: (0, offset + k, 0, 0)),
        out_shape=jax.ShapeDtypeStruct((2, local_channels, row_count, stations), jnp.bfloat16),
        input_output_aliases=aliases,
    )(*operands)


def per_device(samples, fir_taps, station_order):
    tap_count = fir_taps.shape[0]
    channels = fir_taps.shape[1]
    stations_local = samples.shape[1]
    spectra_local = samples.shape[2] // channels
    stations = station_order.shape[0]
    groups = lax.axis_size("stn")
    blocks = lax.axis_size("blk")
    local_channels = channels // groups
    row_count = stations // blocks
    chunks = chunk_count(local_channels)
    width = local_channels // chunks

    frames = samples.reshape(2, stations_local, spectra_local, channels)
    earlier = frames[:, :, spectra_local - (tap_count - 1) :, :].astype(jnp.bfloat16)
    earlier = passed_along(earlier, "blk", 1)
    filtered = filter_frames(fir_taps, earlier, frames)
    filtered = filtered.reshape(2 * stations_local * spectra_local, 2 * channels)

    weights = dft_weights(channels, groups, chunks)
    selector = (
        station_order[None, :] == jnp.arange(stations, dtype=jnp.int32)[:, None]
    ).astype(jnp.bfloat16)
    selector = selector.reshape(groups, stations_local, stations)
    row_start = lax.axis_index("blk") * row_count

    def correlate(chunk, gathered, result):
        gathered = gathered.reshape(width, 2, -1, stations)
        row_block = lax.dynamic_slice_in_dim(gathered, row_start, row_count, 3)
        direct = jnp.transpose(row_block, (0, 3, 1, 2))
        swapped = jnp.stack([direct[:, :, 1], -direct[:, :, 0]], axis=2)
        left = jnp.concatenate([direct, swapped], axis=1).reshape(width, 2 * row_count, -1)
        right = gathered.reshape(width, -1, stations)
        return correlate_chunk(left, right, result, chunk * width, local_channels)

    result = None
    pending = []
    for chunk in range(chunks):
        spectra = jnp.einsum(
            "kj,nj->kn", weights[chunk], filtered, preferred_element_type=jnp.float32
        ).astype(jnp.bfloat16)
        spectra = spectra.reshape(groups, width, 2 * stations_local * spectra_local)
        turned = lax.all_to_all(spectra, "stn", split_axis=0, concat_axis=0, tiled=True)
        turned = turned.reshape(groups, width, 2, stations_local, spectra_local)
        ordered = jnp.einsum(
            "gkias,gar->kisr", turned, selector, preferred_element_type=jnp.float32
        ).astype(jnp.bfloat16)
        ordered = ordered.reshape(width * 2, spectra_local, stations)
        pending.append(gathered_along(ordered, "blk", 1))
        if chunk >= 1:
            result = correlate(chunk - 1, pending[chunk - 1], result)
    result = correlate(chunks - 1, pending[chunks - 1], result)
    return result


def solution(mesh):
    placed = (P(None, "stn", "blk"), P(), P())
    return jax.shard_map(
        per_device,
        mesh=mesh,
        in_specs=placed,
        out_specs=P(None, "stn", "blk", None),
        check_vma=False,
    )
```

```python
import math

import jax
import ml_dtypes
import numpy as np
import jax.numpy as jnp
from jax import lax
from jax.experimental import pallas as pl
from jax.sharding import PartitionSpec as P

epsilon = 1e-06


def passed_along(value, axis, steps):
    count = lax.axis_size(axis)
    initial, last = (max(0, -steps), min(count, count - steps))
    return lax.ppermute(value, axis, [(source, source + steps) for source in range(initial, last)])


def gathered_along(value, axis, dimension):
    count = lax.axis_size(axis)
    parts = [value]
    for shift in range(1, count):
        pairs = [(source, (source + shift) % count) for source in range(count)]
        parts.append(lax.ppermute(value, axis, pairs))
    return jnp.concatenate(parts, axis=dimension)


def chunk_count(local_channels):
    for count in (4, 2):
        if local_channels % count == 0:
            return count
    return 1


def dft_weights(channels, groups, chunks):
    local = channels // groups
    width = local // chunks
    chunk = np.arange(chunks).reshape(chunks, 1, 1, 1)
    group = np.arange(groups).reshape(1, groups, 1, 1)
    inner = np.arange(width).reshape(1, 1, width, 1)
    column = np.arange(channels).reshape(1, 1, 1, channels)
    row = group * local + chunk * width + inner
    phase_index = (row * column % channels).astype(np.float32)
    angle = phase_index * np.float32(2.0 * math.pi / channels)
    cosine = np.cos(angle).astype(ml_dtypes.bfloat16)
    sine = np.sin(angle).astype(ml_dtypes.bfloat16)
    table = np.concatenate([cosine, sine], axis=3)
    return jnp.asarray(table.reshape(chunks, groups * width, 2 * channels))


def fir_kernel(taps_ref, halo_ref, frames_ref, out_ref):
    tap_count = taps_ref.shape[0]
    spectra = frames_ref.shape[2]
    channels = frames_ref.shape[3]
    filtered = []
    for part in range(2):
        extended = jnp.concatenate(
            [halo_ref[part, 0].astype(jnp.float32), frames_ref[part, 0].astype(jnp.float32)], axis=0
        )
        total = taps_ref[0:1, :] * extended[0:spectra]
        for tap_index in range(1, tap_count):
            total = total + taps_ref[tap_index : tap_index + 1, :] * extended[tap_index : tap_index + spectra]
        filtered.append(total.astype(jnp.bfloat16))
    out_ref[0, 0, :, 0:channels] = filtered[0]
    out_ref[0, 0, :, channels:] = filtered[1]
    out_ref[1, 0, :, 0:channels] = filtered[1]
    out_ref[1, 0, :, channels:] = -filtered[0]


def filter_frames(fir_taps, earlier, frames):
    tap_count, channels = fir_taps.shape
    _, stations_local, spectra, _ = frames.shape
    return pl.pallas_call(
        fir_kernel,
        grid=(stations_local,),
        in_specs=[
            pl.BlockSpec((tap_count, channels), lambda a: (0, 0)),
            pl.BlockSpec((2, 1, tap_count - 1, channels), lambda a: (0, a, 0, 0)),
            pl.BlockSpec((2, 1, spectra, channels), lambda a: (0, a, 0, 0)),
        ],
        out_specs=pl.BlockSpec((2, 1, spectra, 2 * channels), lambda a: (0, a, 0, 0)),
        out_shape=jax.ShapeDtypeStruct((2, stations_local, spectra, 2 * channels), jnp.bfloat16),
        cost_estimate=pl.CostEstimate(
            flops=4 * tap_count * frames.size,
            transcendentals=0,
            bytes_accessed=4 * frames.size + 4 * frames.size,
        ),
    )(fir_taps, earlier, frames)


def correlate_kernel(rows_ref, cols_ref, *refs):
    out_ref = refs[-1]
    row_count = out_ref.shape[2]
    left = rows_ref[0]
    right = cols_ref[0]
    product = jnp.dot(left, right, preferred_element_type=jnp.float32)
    right = right.astype(jnp.float32)
    rows = left[0:row_count].astype(jnp.float32)
    column_power = jnp.sum(right * right, axis=0, keepdims=True)
    row_power = jnp.sum(rows * rows, axis=1, keepdims=True)
    scale_row = lax.rsqrt(row_power + epsilon)
    scale_column = lax.rsqrt(column_power + epsilon)
    out_ref[0, 0] = (product[0:row_count] * scale_row * scale_column).astype(out_ref.dtype)
    out_ref[1, 0] = (product[row_count:] * scale_row * scale_column).astype(out_ref.dtype)


def correlate_chunk(left, right, previous, offset, local_channels):
    width, double_rows, depth = left.shape
    row_count = double_rows // 2
    stations = right.shape[2]
    in_specs = [
        pl.BlockSpec((1, double_rows, depth), lambda k: (k, 0, 0)),
        pl.BlockSpec((1, depth, stations), lambda k: (k, 0, 0)),
    ]
    operands = [left, right]
    aliases = {}
    if previous is not None:
        in_specs.append(pl.BlockSpec(memory_space=pl.ANY))
        operands.append(previous)
        aliases = {2: 0}
    return pl.pallas_call(
        correlate_kernel,
        grid=(width,),
        in_specs=in_specs,
        out_specs=pl.BlockSpec((2, 1, row_count, stations), lambda k: (0, offset + k, 0, 0)),
        out_shape=jax.ShapeDtypeStruct((2, local_channels, row_count, stations), jnp.bfloat16),
        input_output_aliases=aliases,
        cost_estimate=pl.CostEstimate(
            flops=2 * width * double_rows * depth * stations,
            transcendentals=width * (row_count + stations),
            bytes_accessed=2 * (left.size + right.size + width * double_rows * stations),
        ),
    )(*operands)


def per_device(samples, fir_taps, station_order):
    tap_count = fir_taps.shape[0]
    channels = fir_taps.shape[1]
    stations_local = samples.shape[1]
    spectra_local = samples.shape[2] // channels
    stations = station_order.shape[0]
    groups = lax.axis_size("stn")
    blocks = lax.axis_size("blk")
    local_channels = channels // groups
    row_count = stations // blocks
    chunks = chunk_count(local_channels)
    width = local_channels // chunks

    frames = samples.reshape(2, stations_local, spectra_local, channels)
    earlier = frames[:, :, spectra_local - (tap_count - 1) :, :].astype(jnp.bfloat16)
    earlier = passed_along(earlier, "blk", 1)
    filtered = filter_frames(fir_taps, earlier, frames)
    filtered = filtered.reshape(2 * stations_local * spectra_local, 2 * channels)

    weights = dft_weights(channels, groups, chunks)
    selector = (
        station_order[None, :] == jnp.arange(stations, dtype=jnp.int32)[:, None]
    ).astype(jnp.bfloat16)
    selector = selector.reshape(groups, stations_local, stations)
    row_start = lax.axis_index("blk") * row_count

    def correlate(chunk, gathered, result):
        gathered = gathered.reshape(width, 2, -1, stations)
        row_block = lax.dynamic_slice_in_dim(gathered, row_start, row_count, 3)
        direct = jnp.transpose(row_block, (0, 3, 1, 2))
        swapped = jnp.stack([direct[:, :, 1], -direct[:, :, 0]], axis=2)
        left = jnp.concatenate([direct, swapped], axis=1).reshape(width, 2 * row_count, -1)
        right = gathered.reshape(width, -1, stations)
        return correlate_chunk(left, right, result, chunk * width, local_channels)

    result = None
    pending = []
    for chunk in range(chunks):
        spectra = jnp.einsum(
            "kj,nj->kn", weights[chunk], filtered, preferred_element_type=jnp.float32
        ).astype(jnp.bfloat16)
        spectra = spectra.reshape(groups, width, 2 * stations_local * spectra_local)
        turned = lax.all_to_all(spectra, "stn", split_axis=0, concat_axis=0, tiled=True)
        turned = turned.reshape(groups, width, 2, stations_local, spectra_local)
        ordered = jnp.einsum(
            "gkias,gar->kisr", turned, selector, preferred_element_type=jnp.float32
        ).astype(jnp.bfloat16)
        ordered = ordered.reshape(width * 2, spectra_local, stations)
        if 2 * chunk < chunks:
            pending.append(lax.all_gather(ordered, "blk", axis=1, tiled=True))
        else:
            pending.append(gathered_along(ordered, "blk", 1))
        if chunk >= 1:
            result = correlate(chunk - 1, pending[chunk - 1], result)
    result = correlate(chunks - 1, pending[chunks - 1], result)
    return result


def solution(mesh):
    placed = (P(None, "stn", "blk"), P(), P())
    return jax.shard_map(
        per_device,
        mesh=mesh,
        in_specs=placed,
        out_specs=P(None, "stn", "blk", None),
        check_vma=False,
    )
```

```python
import math

import jax
import ml_dtypes
import numpy as np
import jax.numpy as jnp
from jax import lax
from jax.experimental import pallas as pl
from jax.sharding import PartitionSpec as P

epsilon = 1e-06


def passed_along(value, axis, steps):
    count = lax.axis_size(axis)
    initial, last = (max(0, -steps), min(count, count - steps))
    return lax.ppermute(value, axis, [(source, source + steps) for source in range(initial, last)])


def gathered_along(value, axis, dimension):
    count = lax.axis_size(axis)
    parts = [value]
    for shift in range(1, count):
        pairs = [(source, (source + shift) % count) for source in range(count)]
        parts.append(lax.ppermute(value, axis, pairs))
    return jnp.concatenate(parts, axis=dimension)


def chunk_count(local_channels):
    for count in (4, 2):
        if local_channels % count == 0:
            return count
    return 1


def dft_weights(channels, groups, chunks):
    local = channels // groups
    width = local // chunks
    chunk = np.arange(chunks).reshape(chunks, 1, 1, 1)
    group = np.arange(groups).reshape(1, groups, 1, 1)
    inner = np.arange(width).reshape(1, 1, width, 1)
    column = np.arange(channels).reshape(1, 1, 1, channels)
    row = group * local + chunk * width + inner
    phase_index = (row * column % channels).astype(np.float32)
    angle = phase_index * np.float32(2.0 * math.pi / channels)
    cosine = np.cos(angle).astype(ml_dtypes.bfloat16)
    sine = np.sin(angle).astype(ml_dtypes.bfloat16)
    table = np.concatenate([cosine, sine], axis=3)
    return jnp.asarray(table.reshape(chunks, groups * width, 2 * channels))


def fir_kernel(taps_ref, halo_ref, frames_ref, out_ref):
    tap_count = taps_ref.shape[0]
    spectra = frames_ref.shape[2]
    channels = frames_ref.shape[3]
    filtered = []
    for part in range(2):
        extended = jnp.concatenate(
            [halo_ref[part, 0].astype(jnp.float32), frames_ref[part, 0].astype(jnp.float32)], axis=0
        )
        total = taps_ref[0:1, :] * extended[0:spectra]
        for tap_index in range(1, tap_count):
            total = total + taps_ref[tap_index : tap_index + 1, :] * extended[tap_index : tap_index + spectra]
        filtered.append(total.astype(jnp.bfloat16))
    out_ref[0, 0, :, 0:channels] = filtered[0]
    out_ref[0, 0, :, channels:] = filtered[1]
    out_ref[1, 0, :, 0:channels] = filtered[1]
    out_ref[1, 0, :, channels:] = -filtered[0]


def filter_frames(fir_taps, earlier, frames):
    tap_count, channels = fir_taps.shape
    _, stations_local, spectra, _ = frames.shape
    return pl.pallas_call(
        fir_kernel,
        grid=(stations_local,),
        in_specs=[
            pl.BlockSpec((tap_count, channels), lambda a: (0, 0)),
            pl.BlockSpec((2, 1, tap_count - 1, channels), lambda a: (0, a, 0, 0)),
            pl.BlockSpec((2, 1, spectra, channels), lambda a: (0, a, 0, 0)),
        ],
        out_specs=pl.BlockSpec((2, 1, spectra, 2 * channels), lambda a: (0, a, 0, 0)),
        out_shape=jax.ShapeDtypeStruct((2, stations_local, spectra, 2 * channels), jnp.bfloat16),
        cost_estimate=pl.CostEstimate(
            flops=4 * tap_count * frames.size,
            transcendentals=0,
            bytes_accessed=4 * frames.size + 4 * frames.size,
        ),
    )(fir_taps, earlier, frames)


def correlate_kernel(rows_ref, cols_ref, *refs):
    out_ref = refs[-1]
    row_count = out_ref.shape[2]
    left = rows_ref[0]
    right = cols_ref[0]
    product = jnp.dot(left, right, preferred_element_type=jnp.float32)
    right = right.astype(jnp.float32)
    rows = left[0:row_count].astype(jnp.float32)
    column_power = jnp.sum(right * right, axis=0, keepdims=True)
    row_power = jnp.sum(rows * rows, axis=1, keepdims=True)
    scale_row = lax.rsqrt(row_power + epsilon)
    scale_column = lax.rsqrt(column_power + epsilon)
    out_ref[0, 0] = (product[0:row_count] * scale_row * scale_column).astype(out_ref.dtype)
    out_ref[1, 0] = (product[row_count:] * scale_row * scale_column).astype(out_ref.dtype)


def correlate_chunk(left, right, previous, offset, local_channels):
    width, double_rows, depth = left.shape
    row_count = double_rows // 2
    stations = right.shape[2]
    in_specs = [
        pl.BlockSpec((1, double_rows, depth), lambda k: (k, 0, 0)),
        pl.BlockSpec((1, depth, stations), lambda k: (k, 0, 0)),
    ]
    operands = [left, right]
    aliases = {}
    if previous is not None:
        in_specs.append(pl.BlockSpec(memory_space=pl.ANY))
        operands.append(previous)
        aliases = {2: 0}
    return pl.pallas_call(
        correlate_kernel,
        grid=(width,),
        in_specs=in_specs,
        out_specs=pl.BlockSpec((2, 1, row_count, stations), lambda k: (0, offset + k, 0, 0)),
        out_shape=jax.ShapeDtypeStruct((2, local_channels, row_count, stations), jnp.bfloat16),
        input_output_aliases=aliases,
        cost_estimate=pl.CostEstimate(
            flops=2 * width * double_rows * depth * stations,
            transcendentals=width * (row_count + stations),
            bytes_accessed=2 * (left.size + right.size + width * double_rows * stations),
        ),
    )(*operands)


def per_device(samples, fir_taps, station_order):
    tap_count = fir_taps.shape[0]
    channels = fir_taps.shape[1]
    stations_local = samples.shape[1]
    spectra_local = samples.shape[2] // channels
    stations = station_order.shape[0]
    groups = lax.axis_size("stn")
    blocks = lax.axis_size("blk")
    local_channels = channels // groups
    row_count = stations // blocks
    chunks = chunk_count(local_channels)
    width = local_channels // chunks

    frames = samples.reshape(2, stations_local, spectra_local, channels)
    earlier = frames[:, :, spectra_local - (tap_count - 1) :, :].astype(jnp.bfloat16)
    earlier = passed_along(earlier, "blk", 1)
    filtered = filter_frames(fir_taps, earlier, frames)
    filtered = filtered.reshape(2 * stations_local * spectra_local, 2 * channels)

    weights = dft_weights(channels, groups, chunks)
    selector = (
        station_order[None, :] == jnp.arange(stations, dtype=jnp.int32)[:, None]
    ).astype(jnp.bfloat16)
    selector = selector.reshape(groups, stations_local, stations)
    row_start = lax.axis_index("blk") * row_count

    def correlate(chunk, gathered, result):
        gathered = gathered.reshape(width, 2, -1, stations)
        row_block = lax.dynamic_slice_in_dim(gathered, row_start, row_count, 3)
        direct = jnp.transpose(row_block, (0, 3, 1, 2))
        swapped = jnp.stack([direct[:, :, 1], -direct[:, :, 0]], axis=2)
        left = jnp.concatenate([direct, swapped], axis=1).reshape(width, 2 * row_count, -1)
        right = gathered.reshape(width, -1, stations)
        return correlate_chunk(left, right, result, chunk * width, local_channels)

    result = None
    pending = []
    for chunk in range(chunks):
        source = filtered
        if chunk >= 2:
            result = correlate(chunk - 2, pending[chunk - 2], result)
            source, result = lax.optimization_barrier((filtered, result))
        spectra = jnp.einsum(
            "kj,nj->kn", weights[chunk], source, preferred_element_type=jnp.float32
        ).astype(jnp.bfloat16)
        spectra = spectra.reshape(groups, width, 2 * stations_local * spectra_local)
        turned = lax.all_to_all(spectra, "stn", split_axis=0, concat_axis=0, tiled=True)
        turned = turned.reshape(groups, width, 2, stations_local, spectra_local)
        ordered = jnp.einsum(
            "gkias,gar->kisr", turned, selector, preferred_element_type=jnp.float32
        ).astype(jnp.bfloat16)
        ordered = ordered.reshape(width * 2, spectra_local, stations)
        pending.append(gathered_along(ordered, "blk", 1))
    for chunk in range(max(0, chunks - 2), chunks):
        result = correlate(chunk, pending[chunk], result)
    return result


def solution(mesh):
    placed = (P(None, "stn", "blk"), P(), P())
    return jax.shard_map(
        per_device,
        mesh=mesh,
        in_specs=placed,
        out_specs=P(None, "stn", "blk", None),
        check_vma=False,
    )
```

```python
import math

import jax
import ml_dtypes
import numpy as np
import jax.numpy as jnp
from jax import lax
from jax.experimental import pallas as pl
from jax.sharding import PartitionSpec as P

epsilon = 1e-06


def passed_along(value, axis, steps):
    count = lax.axis_size(axis)
    initial, last = (max(0, -steps), min(count, count - steps))
    return lax.ppermute(value, axis, [(source, source + steps) for source in range(initial, last)])


def gathered_along(value, axis, dimension):
    count = lax.axis_size(axis)
    parts = [value]
    for shift in range(1, count):
        pairs = [(source, (source + shift) % count) for source in range(count)]
        parts.append(lax.ppermute(value, axis, pairs))
    return jnp.concatenate(parts, axis=dimension)


def chunk_count(local_channels):
    for count in (4, 2):
        if local_channels % count == 0:
            return count
    return 1


def dft_weights(channels, groups, chunks):
    local = channels // groups
    width = local // chunks
    chunk = np.arange(chunks).reshape(chunks, 1, 1, 1)
    group = np.arange(groups).reshape(1, groups, 1, 1)
    inner = np.arange(width).reshape(1, 1, width, 1)
    column = np.arange(channels).reshape(1, 1, 1, channels)
    row = group * local + chunk * width + inner
    phase_index = (row * column % channels).astype(np.float32)
    angle = phase_index * np.float32(2.0 * math.pi / channels)
    cosine = np.cos(angle).astype(ml_dtypes.bfloat16)
    sine = np.sin(angle).astype(ml_dtypes.bfloat16)
    table = np.concatenate([cosine, sine], axis=3)
    return jnp.asarray(table.reshape(chunks, groups * width, 2 * channels))


def fir_rows(taps_ref, extended, count):
    total = taps_ref[0:1, :] * extended[0:count]
    for tap_index in range(1, taps_ref.shape[0]):
        total = total + taps_ref[tap_index : tap_index + 1, :] * extended[tap_index : tap_index + count]
    return total.astype(jnp.bfloat16)


def fir_store(out_ref, filtered, channels):
    out_ref[0, 0, :, 0:channels] = filtered[0]
    out_ref[0, 0, :, channels:] = filtered[1]
    out_ref[1, 0, :, 0:channels] = filtered[1]
    out_ref[1, 0, :, channels:] = -filtered[0]


def fir_kernel(taps_ref, frames_ref, out_ref):
    halo = taps_ref.shape[0] - 1
    spectra = frames_ref.shape[2]
    channels = frames_ref.shape[3]
    filtered = []
    for part in range(2):
        frames = frames_ref[part, 0].astype(jnp.float32)
        extended = jnp.concatenate([jnp.zeros((halo, channels), jnp.float32), frames], axis=0)
        filtered.append(fir_rows(taps_ref, extended, spectra))
    fir_store(out_ref, filtered, channels)


def fir_edge_kernel(taps_ref, halo_ref, frames_ref, previous_ref, out_ref):
    count = frames_ref.shape[2]
    channels = frames_ref.shape[3]
    filtered = []
    for part in range(2):
        extended = jnp.concatenate(
            [halo_ref[part, 0].astype(jnp.float32), frames_ref[part, 0].astype(jnp.float32)], axis=0
        )
        filtered.append(fir_rows(taps_ref, extended, count))
    fir_store(out_ref, filtered, channels)


def filter_frames(fir_taps, earlier, frames):
    tap_count, channels = fir_taps.shape
    _, stations_local, spectra, _ = frames.shape
    out_shape = jax.ShapeDtypeStruct((2, stations_local, spectra, 2 * channels), jnp.bfloat16)
    whole = pl.pallas_call(
        fir_kernel,
        grid=(stations_local,),
        in_specs=[
            pl.BlockSpec((tap_count, channels), lambda a: (0, 0)),
            pl.BlockSpec((2, 1, spectra, channels), lambda a: (0, a, 0, 0)),
        ],
        out_specs=pl.BlockSpec((2, 1, spectra, 2 * channels), lambda a: (0, a, 0, 0)),
        out_shape=out_shape,
        cost_estimate=pl.CostEstimate(
            flops=4 * tap_count * frames.size,
            transcendentals=0,
            bytes_accessed=4 * frames.size + 4 * frames.size,
        ),
    )(fir_taps, frames)
    edge = 8
    return pl.pallas_call(
        fir_edge_kernel,
        grid=(stations_local,),
        in_specs=[
            pl.BlockSpec((tap_count, channels), lambda a: (0, 0)),
            pl.BlockSpec((2, 1, tap_count - 1, channels), lambda a: (0, a, 0, 0)),
            pl.BlockSpec((2, 1, edge, channels), lambda a: (0, a, 0, 0)),
            pl.BlockSpec(memory_space=pl.ANY),
        ],
        out_specs=pl.BlockSpec((2, 1, edge, 2 * channels), lambda a: (0, a, 0, 0)),
        out_shape=out_shape,
        input_output_aliases={3: 0},
        cost_estimate=pl.CostEstimate(
            flops=4 * tap_count * edge * frames.size // spectra,
            transcendentals=0,
            bytes_accessed=8 * edge * frames.size // spectra,
        ),
    )(fir_taps, earlier, frames, whole)


def correlate_kernel(rows_ref, cols_ref, *refs):
    out_ref = refs[-1]
    row_count = out_ref.shape[2]
    for index in range(out_ref.shape[1]):
        left = rows_ref[index]
        right = cols_ref[index]
        product = jnp.dot(left, right, preferred_element_type=jnp.float32)
        right = right.astype(jnp.float32)
        rows = left[0:row_count].astype(jnp.float32)
        column_power = jnp.sum(right * right, axis=0, keepdims=True)
        row_power = jnp.sum(rows * rows, axis=1, keepdims=True)
        scale_row = lax.rsqrt(row_power + epsilon)
        scale_column = lax.rsqrt(column_power + epsilon)
        out_ref[0, index] = (product[0:row_count] * scale_row * scale_column).astype(out_ref.dtype)
        out_ref[1, index] = (product[row_count:] * scale_row * scale_column).astype(out_ref.dtype)


def correlate_chunk(left, right, previous, offset, local_channels):
    width, double_rows, depth = left.shape
    row_count = double_rows // 2
    stations = right.shape[2]
    step = 4 if width % 4 == 0 and offset % 4 == 0 else 1
    in_specs = [
        pl.BlockSpec((step, double_rows, depth), lambda k: (k, 0, 0)),
        pl.BlockSpec((step, depth, stations), lambda k: (k, 0, 0)),
    ]
    operands = [left, right]
    aliases = {}
    if previous is not None:
        in_specs.append(pl.BlockSpec(memory_space=pl.ANY))
        operands.append(previous)
        aliases = {2: 0}
    return pl.pallas_call(
        correlate_kernel,
        grid=(width // step,),
        in_specs=in_specs,
        out_specs=pl.BlockSpec(
            (2, step, row_count, stations), lambda k: (0, offset // step + k, 0, 0)
        ),
        out_shape=jax.ShapeDtypeStruct((2, local_channels, row_count, stations), jnp.bfloat16),
        input_output_aliases=aliases,
        cost_estimate=pl.CostEstimate(
            flops=2 * width * double_rows * depth * stations,
            transcendentals=width * (row_count + stations),
            bytes_accessed=2 * (left.size + right.size + width * double_rows * stations),
        ),
    )(*operands)


def per_device(samples, fir_taps, station_order):
    tap_count = fir_taps.shape[0]
    channels = fir_taps.shape[1]
    stations_local = samples.shape[1]
    spectra_local = samples.shape[2] // channels
    stations = station_order.shape[0]
    groups = lax.axis_size("stn")
    blocks = lax.axis_size("blk")
    local_channels = channels // groups
    row_count = stations // blocks
    chunks = chunk_count(local_channels)
    width = local_channels // chunks

    frames = samples.reshape(2, stations_local, spectra_local, channels)
    earlier = frames[:, :, spectra_local - (tap_count - 1) :, :].astype(jnp.bfloat16)
    earlier = passed_along(earlier, "blk", 1)
    filtered = filter_frames(fir_taps, earlier, frames)
    filtered = filtered.reshape(2 * stations_local * spectra_local, 2 * channels)

    weights = dft_weights(channels, groups, chunks)
    selector = (
        station_order[None, :] == jnp.arange(stations, dtype=jnp.int32)[:, None]
    ).astype(jnp.bfloat16)
    selector = selector.reshape(groups, stations_local, stations)
    row_start = lax.axis_index("blk") * row_count

    def correlate(chunk, gathered, result):
        gathered = gathered.reshape(width, 2, -1, stations)
        row_block = lax.dynamic_slice_in_dim(gathered, row_start, row_count, 3)
        direct = jnp.transpose(row_block, (0, 3, 1, 2))
        swapped = jnp.stack([direct[:, :, 1], -direct[:, :, 0]], axis=2)
        left = jnp.concatenate([direct, swapped], axis=1).reshape(width, 2 * row_count, -1)
        right = gathered.reshape(width, -1, stations)
        return correlate_chunk(left, right, result, chunk * width, local_channels)

    result = None
    pending = []
    for chunk in range(chunks):
        source = filtered
        if chunk >= 2:
            result = correlate(chunk - 2, pending[chunk - 2], result)
            source, result = lax.optimization_barrier((filtered, result))
        spectra = jnp.einsum(
            "kj,nj->kn", weights[chunk], source, preferred_element_type=jnp.float32
        ).astype(jnp.bfloat16)
        spectra = spectra.reshape(groups, width, 2 * stations_local * spectra_local)
        turned = lax.all_to_all(spectra, "stn", split_axis=0, concat_axis=0, tiled=True)
        turned = turned.reshape(groups, width, 2, stations_local, spectra_local)
        ordered = jnp.einsum(
            "gkias,gar->kisr", turned, selector, preferred_element_type=jnp.float32
        ).astype(jnp.bfloat16)
        ordered = ordered.reshape(width * 2, spectra_local, stations)
        pending.append(gathered_along(ordered, "blk", 1))
    for chunk in range(max(0, chunks - 2), chunks):
        result = correlate(chunk, pending[chunk], result)
    return result


def solution(mesh):
    placed = (P(None, "stn", "blk"), P(), P())
    return jax.shard_map(
        per_device,
        mesh=mesh,
        in_specs=placed,
        out_specs=P(None, "stn", "blk", None),
        check_vma=False,
    )
```

```python
import math

import jax
import ml_dtypes
import numpy as np
import jax.numpy as jnp
from jax import lax
from jax.experimental import pallas as pl
from jax.experimental.pallas import tpu as pltpu
from jax.sharding import PartitionSpec as P

epsilon = 1e-06


def passed_along(value, axis, steps):
    count = lax.axis_size(axis)
    initial, last = (max(0, -steps), min(count, count - steps))
    return lax.ppermute(value, axis, [(source, source + steps) for source in range(initial, last)])


def gathered_along(value, axis, dimension):
    count = lax.axis_size(axis)
    parts = [value]
    for shift in range(1, count):
        pairs = [(source, (source + shift) % count) for source in range(count)]
        parts.append(lax.ppermute(value, axis, pairs))
    return jnp.concatenate(parts, axis=dimension)


def chunk_count(local_channels):
    for count in (4, 2):
        if local_channels % count == 0:
            return count
    return 1


def dft_weights(channels, groups, chunks):
    local = channels // groups
    width = local // chunks
    chunk = np.arange(chunks).reshape(chunks, 1, 1, 1)
    group = np.arange(groups).reshape(1, groups, 1, 1)
    inner = np.arange(width).reshape(1, 1, width, 1)
    column = np.arange(channels).reshape(1, 1, 1, channels)
    row = group * local + chunk * width + inner
    phase_index = (row * column % channels).astype(np.float32)
    angle = phase_index * np.float32(2.0 * math.pi / channels)
    cosine = np.cos(angle).astype(ml_dtypes.bfloat16)
    sine = np.sin(angle).astype(ml_dtypes.bfloat16)
    table = np.concatenate([cosine, sine], axis=3)
    return jnp.asarray(table.reshape(chunks, groups * width, 2 * channels))


def fir_rows(taps_ref, extended, count):
    total = taps_ref[0:1, :] * extended[0:count]
    for tap_index in range(1, taps_ref.shape[0]):
        total = total + taps_ref[tap_index : tap_index + 1, :] * extended[tap_index : tap_index + count]
    return total.astype(jnp.bfloat16)


def fir_store(out_ref, station, filtered, channels):
    out_ref[0, station, :, 0:channels] = filtered[0]
    out_ref[0, station, :, channels:] = filtered[1]
    out_ref[1, station, :, 0:channels] = filtered[1]
    out_ref[1, station, :, channels:] = -filtered[0]


def fir_kernel(taps_ref, frames_ref, out_ref):
    halo = taps_ref.shape[0] - 1
    spectra = frames_ref.shape[2]
    channels = frames_ref.shape[3]

    def body(station, carry):
        filtered = []
        for part in range(2):
            frames = frames_ref[part, station].astype(jnp.float32)
            extended = jnp.concatenate([jnp.zeros((halo, channels), jnp.float32), frames], axis=0)
            filtered.append(fir_rows(taps_ref, extended, spectra))
        fir_store(out_ref, station, filtered, channels)
        return carry

    lax.fori_loop(0, frames_ref.shape[1], body, 0)


def fir_edge_kernel(taps_ref, halo_ref, frames_ref, previous_ref, out_ref):
    count = frames_ref.shape[2]
    channels = frames_ref.shape[3]

    def body(station, carry):
        filtered = []
        for part in range(2):
            extended = jnp.concatenate(
                [
                    halo_ref[part, station].astype(jnp.float32),
                    frames_ref[part, station].astype(jnp.float32),
                ],
                axis=0,
            )
            filtered.append(fir_rows(taps_ref, extended, count))
        fir_store(out_ref, station, filtered, channels)
        return carry

    lax.fori_loop(0, frames_ref.shape[1], body, 0)


def filter_frames(fir_taps, earlier, frames):
    tap_count, channels = fir_taps.shape
    _, stations_local, spectra, _ = frames.shape
    out_shape = jax.ShapeDtypeStruct((2, stations_local, spectra, 2 * channels), jnp.bfloat16)
    group = 4 if stations_local % 4 == 0 else 1
    whole = pl.pallas_call(
        fir_kernel,
        grid=(stations_local // group,),
        in_specs=[
            pl.BlockSpec((tap_count, channels), lambda a: (0, 0)),
            pl.BlockSpec((2, group, spectra, channels), lambda a: (0, a, 0, 0)),
        ],
        out_specs=pl.BlockSpec((2, group, spectra, 2 * channels), lambda a: (0, a, 0, 0)),
        out_shape=out_shape,
        cost_estimate=pl.CostEstimate(
            flops=4 * tap_count * frames.size,
            transcendentals=0,
            bytes_accessed=2 * frames.size + 4 * frames.size,
        ),
    )(fir_taps, frames)
    edge = 8
    return pl.pallas_call(
        fir_edge_kernel,
        grid=(1,),
        in_specs=[
            pl.BlockSpec((tap_count, channels), lambda a: (0, 0)),
            pl.BlockSpec((2, stations_local, tap_count - 1, channels), lambda a: (0, 0, 0, 0)),
            pl.BlockSpec((2, stations_local, edge, channels), lambda a: (0, 0, 0, 0)),
            pl.BlockSpec(memory_space=pl.ANY),
        ],
        out_specs=pl.BlockSpec((2, stations_local, edge, 2 * channels), lambda a: (0, 0, 0, 0)),
        out_shape=out_shape,
        input_output_aliases={3: 0},
        cost_estimate=pl.CostEstimate(
            flops=4 * tap_count * edge * frames.size // spectra,
            transcendentals=0,
            bytes_accessed=8 * edge * frames.size // spectra,
        ),
    )(fir_taps, earlier, frames, whole)


def correlate_kernel(rows_ref, cols_ref, *refs):
    out_ref = refs[-1]
    row_count = out_ref.shape[2]
    for index in range(out_ref.shape[1]):
        left = rows_ref[index]
        right = cols_ref[index]
        product = jnp.dot(left, right, preferred_element_type=jnp.float32)
        right = right.astype(jnp.float32)
        rows = left[0:row_count].astype(jnp.float32)
        column_power = jnp.sum(right * right, axis=0, keepdims=True)
        row_power = jnp.sum(rows * rows, axis=1, keepdims=True)
        scale_row = lax.rsqrt(row_power + epsilon)
        scale_column = lax.rsqrt(column_power + epsilon)
        out_ref[0, index] = (product[0:row_count] * scale_row * scale_column).astype(out_ref.dtype)
        out_ref[1, index] = (product[row_count:] * scale_row * scale_column).astype(out_ref.dtype)


def correlate_chunk(left, right, previous, offset, local_channels):
    width, double_rows, depth = left.shape
    row_count = double_rows // 2
    stations = right.shape[2]
    step = 4 if width % 4 == 0 and offset % 4 == 0 else 1
    in_specs = [
        pl.BlockSpec((step, double_rows, depth), lambda k: (k, 0, 0)),
        pl.BlockSpec((step, depth, stations), lambda k: (k, 0, 0)),
    ]
    operands = [left, right]
    aliases = {}
    if previous is not None:
        in_specs.append(pl.BlockSpec(memory_space=pl.ANY))
        operands.append(previous)
        aliases = {2: 0}
    return pl.pallas_call(
        correlate_kernel,
        grid=(width // step,),
        in_specs=in_specs,
        out_specs=pl.BlockSpec(
            (2, step, row_count, stations), lambda k: (0, offset // step + k, 0, 0)
        ),
        out_shape=jax.ShapeDtypeStruct((2, local_channels, row_count, stations), jnp.bfloat16),
        input_output_aliases=aliases,
        cost_estimate=pl.CostEstimate(
            flops=2 * width * double_rows * depth * stations,
            transcendentals=width * (row_count + stations),
            bytes_accessed=2 * (left.size + right.size + width * double_rows * stations),
        ),
    )(*operands)


def correlate_rows_kernel(block_ref, rows_ref, cols_ref, *refs):
    out_ref = refs[-1]
    half = cols_ref.shape[1] // 2
    contract_first = (((0,), (0,)), ((), ()))
    for index in range(out_ref.shape[1]):
        rows = rows_ref[index]
        right = cols_ref[index]
        swapped = jnp.concatenate([rows[half:], -rows[:half]], axis=0)
        real_vis = lax.dot_general(rows, right, contract_first, preferred_element_type=jnp.float32)
        imag_vis = lax.dot_general(swapped, right, contract_first, preferred_element_type=jnp.float32)
        right = right.astype(jnp.float32)
        rows = rows.astype(jnp.float32)
        column_power = jnp.sum(right * right, axis=0, keepdims=True)
        row_power = jnp.sum(jnp.transpose(rows * rows), axis=1, keepdims=True)
        scale_row = lax.rsqrt(row_power + epsilon)
        scale_column = lax.rsqrt(column_power + epsilon)
        out_ref[0, index] = (real_vis * scale_row * scale_column).astype(out_ref.dtype)
        out_ref[1, index] = (imag_vis * scale_row * scale_column).astype(out_ref.dtype)


def correlate_rows_chunk(right, block, row_count, previous, offset, local_channels):
    width, depth, stations = right.shape
    step = 4 if width % 4 == 0 and offset % 4 == 0 else 1
    in_specs = [
        pl.BlockSpec((step, depth, row_count), lambda k, b: (k, 0, b[0])),
        pl.BlockSpec((step, depth, stations), lambda k, b: (k, 0, 0)),
    ]
    operands = [block, right, right]
    aliases = {}
    if previous is not None:
        in_specs.append(pl.BlockSpec(memory_space=pl.ANY))
        operands.append(previous)
        aliases = {3: 0}
    grid_spec = pltpu.PrefetchScalarGridSpec(
        num_scalar_prefetch=1,
        grid=(width // step,),
        in_specs=in_specs,
        out_specs=pl.BlockSpec(
            (2, step, row_count, stations), lambda k, b: (0, offset // step + k, 0, 0)
        ),
    )
    return pl.pallas_call(
        correlate_rows_kernel,
        grid_spec=grid_spec,
        out_shape=jax.ShapeDtypeStruct((2, local_channels, row_count, stations), jnp.bfloat16),
        input_output_aliases=aliases,
        cost_estimate=pl.CostEstimate(
            flops=4 * width * row_count * depth * stations,
            transcendentals=width * (row_count + stations),
            bytes_accessed=2 * (right.size + width * depth * row_count + 2 * width * row_count * stations),
        ),
    )(*operands)


def per_device(samples, fir_taps, station_order):
    tap_count = fir_taps.shape[0]
    channels = fir_taps.shape[1]
    stations_local = samples.shape[1]
    spectra_local = samples.shape[2] // channels
    stations = station_order.shape[0]
    groups = lax.axis_size("stn")
    blocks = lax.axis_size("blk")
    local_channels = channels // groups
    row_count = stations // blocks
    chunks = chunk_count(local_channels)
    width = local_channels // chunks

    frames = samples.astype(jnp.bfloat16).reshape(2, stations_local, spectra_local, channels)
    earlier = frames[:, :, spectra_local - (tap_count - 1) :, :]
    earlier = passed_along(earlier, "blk", 1)
    filtered = filter_frames(fir_taps, earlier, frames)
    filtered = filtered.reshape(2 * stations_local * spectra_local, 2 * channels)

    weights = dft_weights(channels, groups, chunks)
    selector = (
        station_order[None, :] == jnp.arange(stations, dtype=jnp.int32)[:, None]
    ).astype(jnp.bfloat16)
    selector = selector.reshape(groups, stations_local, stations)
    row_start = lax.axis_index("blk") * row_count

    block_index = jnp.reshape(lax.axis_index("blk"), (1,)).astype(jnp.int32)

    def correlate(chunk, gathered, result):
        if row_count % 128 == 0:
            right = gathered.reshape(width, -1, stations)
            return correlate_rows_chunk(
                right, block_index, row_count, result, chunk * width, local_channels
            )
        gathered = gathered.reshape(width, 2, -1, stations)
        row_block = lax.dynamic_slice_in_dim(gathered, row_start, row_count, 3)
        direct = jnp.transpose(row_block, (0, 3, 1, 2))
        swapped = jnp.stack([direct[:, :, 1], -direct[:, :, 0]], axis=2)
        left = jnp.concatenate([direct, swapped], axis=1).reshape(width, 2 * row_count, -1)
        right = gathered.reshape(width, -1, stations)
        return correlate_chunk(left, right, result, chunk * width, local_channels)

    result = None
    pending = []
    for chunk in range(chunks):
        source = filtered
        if chunk >= 2:
            result = correlate(chunk - 2, pending[chunk - 2], result)
            source, result = lax.optimization_barrier((filtered, result))
        spectra = jnp.einsum(
            "kj,nj->kn", weights[chunk], source, preferred_element_type=jnp.float32
        ).astype(jnp.bfloat16)
        spectra = spectra.reshape(groups, width, 2 * stations_local * spectra_local)
        turned = lax.all_to_all(spectra, "stn", split_axis=0, concat_axis=0, tiled=True)
        turned = turned.reshape(groups, width, 2, stations_local, spectra_local)
        ordered = jnp.einsum(
            "gkias,gar->kisr", turned, selector, preferred_element_type=jnp.float32
        ).astype(jnp.bfloat16)
        ordered = ordered.reshape(width * 2, spectra_local, stations)
        pending.append(gathered_along(ordered, "blk", 1))
    for chunk in range(max(0, chunks - 2), chunks):
        result = correlate(chunk, pending[chunk], result)
    return result


def solution(mesh):
    placed = (P(None, "stn", "blk"), P(), P())
    return jax.shard_map(
        per_device,
        mesh=mesh,
        in_specs=placed,
        out_specs=P(None, "stn", "blk", None),
        check_vma=False,
    )
```

```python
import math

import jax
import ml_dtypes
import numpy as np
import jax.numpy as jnp
from jax import lax
from jax.experimental import pallas as pl
from jax.experimental.pallas import tpu as pltpu
from jax.sharding import PartitionSpec as P

epsilon = 1e-06


def passed_along(value, axis, steps):
    count = lax.axis_size(axis)
    initial, last = (max(0, -steps), min(count, count - steps))
    return lax.ppermute(value, axis, [(source, source + steps) for source in range(initial, last)])


def gathered_along(value, axis):
    count = lax.axis_size(axis)
    parts = [value]
    for shift in range(1, count):
        pairs = [(source, (source + shift) % count) for source in range(count)]
        parts.append(lax.ppermute(value, axis, pairs))
    return parts


def chunk_count(local_channels):
    for count in (4, 2):
        if local_channels % count == 0:
            return count
    return 1


def dft_weights(channels, groups, chunks):
    local = channels // groups
    width = local // chunks
    chunk = np.arange(chunks).reshape(chunks, 1, 1, 1)
    group = np.arange(groups).reshape(1, groups, 1, 1)
    inner = np.arange(width).reshape(1, 1, width, 1)
    column = np.arange(channels).reshape(1, 1, 1, channels)
    row = group * local + chunk * width + inner
    phase_index = (row * column % channels).astype(np.float32)
    angle = phase_index * np.float32(2.0 * math.pi / channels)
    cosine = np.cos(angle).astype(ml_dtypes.bfloat16)
    sine = np.sin(angle).astype(ml_dtypes.bfloat16)
    table = np.concatenate([cosine, sine], axis=3)
    return jnp.asarray(table.reshape(chunks, groups * width, 2 * channels))


def fir_rows(taps_ref, extended, count):
    total = taps_ref[0:1, :] * extended[0:count]
    for tap_index in range(1, taps_ref.shape[0]):
        total = total + taps_ref[tap_index : tap_index + 1, :] * extended[tap_index : tap_index + count]
    return total.astype(jnp.bfloat16)


def fir_store(out_ref, station, filtered, channels):
    out_ref[0, station, :, 0:channels] = filtered[0]
    out_ref[0, station, :, channels:] = filtered[1]
    out_ref[1, station, :, 0:channels] = filtered[1]
    out_ref[1, station, :, channels:] = -filtered[0]


def fir_kernel(taps_ref, frames_ref, out_ref):
    halo = taps_ref.shape[0] - 1
    spectra = frames_ref.shape[2]
    channels = frames_ref.shape[3]

    def body(station, carry):
        filtered = []
        for part in range(2):
            frames = frames_ref[part, station].astype(jnp.float32)
            extended = jnp.concatenate([jnp.zeros((halo, channels), jnp.float32), frames], axis=0)
            filtered.append(fir_rows(taps_ref, extended, spectra))
        fir_store(out_ref, station, filtered, channels)
        return carry

    lax.fori_loop(0, frames_ref.shape[1], body, 0)


def fir_edge_kernel(taps_ref, halo_ref, frames_ref, previous_ref, out_ref):
    count = frames_ref.shape[2]
    channels = frames_ref.shape[3]

    def body(station, carry):
        filtered = []
        for part in range(2):
            extended = jnp.concatenate(
                [
                    halo_ref[part, station].astype(jnp.float32),
                    frames_ref[part, station].astype(jnp.float32),
                ],
                axis=0,
            )
            filtered.append(fir_rows(taps_ref, extended, count))
        fir_store(out_ref, station, filtered, channels)
        return carry

    lax.fori_loop(0, frames_ref.shape[1], body, 0)


def filter_frames(fir_taps, earlier, frames):
    tap_count, channels = fir_taps.shape
    _, stations_local, spectra, _ = frames.shape
    out_shape = jax.ShapeDtypeStruct((2, stations_local, spectra, 2 * channels), jnp.bfloat16)
    group = 4 if stations_local % 4 == 0 else 1
    whole = pl.pallas_call(
        fir_kernel,
        grid=(stations_local // group,),
        in_specs=[
            pl.BlockSpec((tap_count, channels), lambda a: (0, 0)),
            pl.BlockSpec((2, group, spectra, channels), lambda a: (0, a, 0, 0)),
        ],
        out_specs=pl.BlockSpec((2, group, spectra, 2 * channels), lambda a: (0, a, 0, 0)),
        out_shape=out_shape,
        cost_estimate=pl.CostEstimate(
            flops=4 * tap_count * frames.size,
            transcendentals=0,
            bytes_accessed=2 * frames.size + 4 * frames.size,
        ),
    )(fir_taps, frames)
    edge = 8
    edge_group = stations_local // 4 if stations_local % 4 == 0 else stations_local
    return pl.pallas_call(
        fir_edge_kernel,
        grid=(stations_local // edge_group,),
        in_specs=[
            pl.BlockSpec((tap_count, channels), lambda a: (0, 0)),
            pl.BlockSpec((2, edge_group, tap_count - 1, channels), lambda a: (0, a, 0, 0)),
            pl.BlockSpec((2, edge_group, edge, channels), lambda a: (0, a, 0, 0)),
            pl.BlockSpec(memory_space=pl.ANY),
        ],
        out_specs=pl.BlockSpec((2, edge_group, edge, 2 * channels), lambda a: (0, a, 0, 0)),
        out_shape=out_shape,
        input_output_aliases={3: 0},
        cost_estimate=pl.CostEstimate(
            flops=4 * tap_count * edge * frames.size // spectra,
            transcendentals=0,
            bytes_accessed=8 * edge * frames.size // spectra,
        ),
    )(fir_taps, earlier, frames, whole)


def correlate_kernel(rows_ref, cols_ref, *refs):
    out_ref = refs[-1]
    row_count = out_ref.shape[2]
    for index in range(out_ref.shape[1]):
        left = rows_ref[index]
        right = cols_ref[index]
        product = jnp.dot(left, right, preferred_element_type=jnp.float32)
        right = right.astype(jnp.float32)
        rows = left[0:row_count].astype(jnp.float32)
        column_power = jnp.sum(right * right, axis=0, keepdims=True)
        row_power = jnp.sum(rows * rows, axis=1, keepdims=True)
        scale_row = lax.rsqrt(row_power + epsilon)
        scale_column = lax.rsqrt(column_power + epsilon)
        out_ref[0, index] = (product[0:row_count] * scale_row * scale_column).astype(out_ref.dtype)
        out_ref[1, index] = (product[row_count:] * scale_row * scale_column).astype(out_ref.dtype)


def correlate_chunk(left, right, previous, offset, local_channels):
    width, double_rows, depth = left.shape
    row_count = double_rows // 2
    stations = right.shape[2]
    step = 4 if width % 4 == 0 and offset % 4 == 0 else 1
    in_specs = [
        pl.BlockSpec((step, double_rows, depth), lambda k: (k, 0, 0)),
        pl.BlockSpec((step, depth, stations), lambda k: (k, 0, 0)),
    ]
    operands = [left, right]
    aliases = {}
    if previous is not None:
        in_specs.append(pl.BlockSpec(memory_space=pl.ANY))
        operands.append(previous)
        aliases = {2: 0}
    return pl.pallas_call(
        correlate_kernel,
        grid=(width // step,),
        in_specs=in_specs,
        out_specs=pl.BlockSpec(
            (2, step, row_count, stations), lambda k: (0, offset // step + k, 0, 0)
        ),
        out_shape=jax.ShapeDtypeStruct((2, local_channels, row_count, stations), jnp.bfloat16),
        input_output_aliases=aliases,
        cost_estimate=pl.CostEstimate(
            flops=2 * width * double_rows * depth * stations,
            transcendentals=width * (row_count + stations),
            bytes_accessed=2 * (left.size + right.size + width * double_rows * stations),
        ),
    )(*operands)


def correlate_rows_kernel(block_ref, *refs):
    out_ref = refs[-1]
    pieces = (len(refs) - 1) // 2
    rows_refs = refs[0:pieces]
    cols_refs = refs[pieces : 2 * pieces]
    contract_first = (((0,), (0,)), ((), ()))
    for index in range(out_ref.shape[1]):
        rows = jnp.concatenate(
            [ref[index, part] for part in range(2) for ref in rows_refs], axis=0
        )
        right = jnp.concatenate(
            [ref[index, part] for part in range(2) for ref in cols_refs], axis=0
        )
        half = rows.shape[0] // 2
        swapped = jnp.concatenate([rows[half:], -rows[:half]], axis=0)
        real_vis = lax.dot_general(rows, right, contract_first, preferred_element_type=jnp.float32)
        imag_vis = lax.dot_general(swapped, right, contract_first, preferred_element_type=jnp.float32)
        right = right.astype(jnp.float32)
        rows = rows.astype(jnp.float32)
        column_power = jnp.sum(right * right, axis=0, keepdims=True)
        row_power = jnp.sum(jnp.transpose(rows * rows), axis=1, keepdims=True)
        scale_row = lax.rsqrt(row_power + epsilon)
        scale_column = lax.rsqrt(column_power + epsilon)
        out_ref[0, index] = (real_vis * scale_row * scale_column).astype(out_ref.dtype)
        out_ref[1, index] = (imag_vis * scale_row * scale_column).astype(out_ref.dtype)


def correlate_rows_chunk(parts, block, row_count, previous, offset, local_channels):
    width, _, spectra, stations = parts[0].shape
    step = 4 if width % 4 == 0 and offset % 4 == 0 else 1
    rows_spec = pl.BlockSpec((step, 2, spectra, row_count), lambda k, b: (k, 0, 0, b[0]))
    cols_spec = pl.BlockSpec((step, 2, spectra, stations), lambda k, b: (k, 0, 0, 0))
    in_specs = [rows_spec] * len(parts) + [cols_spec] * len(parts)
    operands = [block] + list(parts) + list(parts)
    aliases = {}
    if previous is not None:
        in_specs.append(pl.BlockSpec(memory_space=pl.ANY))
        operands.append(previous)
        aliases = {len(operands) - 1: 0}
    grid_spec = pltpu.PrefetchScalarGridSpec(
        num_scalar_prefetch=1,
        grid=(width // step,),
        in_specs=in_specs,
        out_specs=pl.BlockSpec(
            (2, step, row_count, stations), lambda k, b: (0, offset // step + k, 0, 0)
        ),
    )
    depth = 2 * spectra * len(parts)
    return pl.pallas_call(
        correlate_rows_kernel,
        grid_spec=grid_spec,
        out_shape=jax.ShapeDtypeStruct((2, local_channels, row_count, stations), jnp.bfloat16),
        input_output_aliases=aliases,
        cost_estimate=pl.CostEstimate(
            flops=4 * width * row_count * depth * stations,
            transcendentals=width * (row_count + stations),
            bytes_accessed=2 * width * depth * (stations + row_count)
            + 4 * width * row_count * stations,
        ),
    )(*operands)


def per_device(samples, fir_taps, station_order):
    tap_count = fir_taps.shape[0]
    channels = fir_taps.shape[1]
    stations_local = samples.shape[1]
    spectra_local = samples.shape[2] // channels
    stations = station_order.shape[0]
    groups = lax.axis_size("stn")
    blocks = lax.axis_size("blk")
    local_channels = channels // groups
    row_count = stations // blocks
    chunks = chunk_count(local_channels)
    width = local_channels // chunks

    earlier = samples[:, :, (spectra_local - (tap_count - 1)) * channels :].astype(jnp.bfloat16)
    earlier = earlier.reshape(2, stations_local, tap_count - 1, channels)
    frames = samples.astype(jnp.bfloat16).reshape(2, stations_local, spectra_local, channels)
    earlier = passed_along(earlier, "blk", 1)
    filtered = filter_frames(fir_taps, earlier, frames)
    filtered = filtered.reshape(2 * stations_local * spectra_local, 2 * channels)

    weights = dft_weights(channels, groups, chunks)
    selector = (
        station_order[None, :] == jnp.arange(stations, dtype=jnp.int32)[:, None]
    ).astype(jnp.bfloat16)
    selector = selector.reshape(groups, stations_local, stations)
    row_start = lax.axis_index("blk") * row_count

    block_index = jnp.reshape(lax.axis_index("blk"), (1,)).astype(jnp.int32)

    def correlate(chunk, parts, result):
        parts = [part.reshape(width, 2, spectra_local, stations) for part in parts]
        if row_count % 128 == 0:
            return correlate_rows_chunk(
                parts, block_index, row_count, result, chunk * width, local_channels
            )
        gathered = jnp.concatenate(parts, axis=2)
        row_block = lax.dynamic_slice_in_dim(gathered, row_start, row_count, 3)
        direct = jnp.transpose(row_block, (0, 3, 1, 2))
        swapped = jnp.stack([direct[:, :, 1], -direct[:, :, 0]], axis=2)
        left = jnp.concatenate([direct, swapped], axis=1).reshape(width, 2 * row_count, -1)
        right = gathered.reshape(width, -1, stations)
        return correlate_chunk(left, right, result, chunk * width, local_channels)

    result = None
    pending = []
    for chunk in range(chunks):
        source = filtered
        if chunk >= 2:
            result = correlate(chunk - 2, pending[chunk - 2], result)
            source, result = lax.optimization_barrier((filtered, result))
        spectra = jnp.einsum(
            "kj,nj->kn", weights[chunk], source, preferred_element_type=jnp.float32
        ).astype(jnp.bfloat16)
        spectra = spectra.reshape(groups, width, 2 * stations_local * spectra_local)
        turned = lax.all_to_all(spectra, "stn", split_axis=0, concat_axis=0, tiled=True)
        turned = turned.reshape(groups, width, 2, stations_local, spectra_local)
        ordered = jnp.einsum(
            "gkias,gar->kisr", turned, selector, preferred_element_type=jnp.float32
        ).astype(jnp.bfloat16)
        ordered = ordered.reshape(width * 2, spectra_local, stations)
        pending.append(gathered_along(ordered, "blk"))
    for chunk in range(max(0, chunks - 2), chunks):
        result = correlate(chunk, pending[chunk], result)
    return result


def solution(mesh):
    placed = (P(None, "stn", "blk"), P(), P())
    return jax.shard_map(
        per_device,
        mesh=mesh,
        in_specs=placed,
        out_specs=P(None, "stn", "blk", None),
        check_vma=False,
    )
```

```python
import math

import jax
import ml_dtypes
import numpy as np
import jax.numpy as jnp
from jax import lax
from jax.experimental import pallas as pl
from jax.experimental.pallas import tpu as pltpu
from jax.sharding import PartitionSpec as P

epsilon = 1e-06


def passed_along(value, axis, steps):
    count = lax.axis_size(axis)
    initial, last = (max(0, -steps), min(count, count - steps))
    return lax.ppermute(value, axis, [(source, source + steps) for source in range(initial, last)])


def gathered_along(value, axis):
    count = lax.axis_size(axis)
    parts = [value]
    for shift in range(1, count):
        pairs = [(source, (source + shift) % count) for source in range(count)]
        parts.append(lax.ppermute(value, axis, pairs))
    return parts


def chunk_count(local_channels):
    for count in (4, 2):
        if local_channels % count == 0:
            return count
    return 1


def dft_weights(channels, groups, chunks):
    local = channels // groups
    width = local // chunks
    chunk = np.arange(chunks).reshape(chunks, 1, 1, 1)
    group = np.arange(groups).reshape(1, groups, 1, 1)
    inner = np.arange(width).reshape(1, 1, width, 1)
    column = np.arange(channels).reshape(1, 1, 1, channels)
    row = group * local + chunk * width + inner
    phase_index = (row * column % channels).astype(np.float32)
    angle = phase_index * np.float32(2.0 * math.pi / channels)
    cosine = np.cos(angle).astype(ml_dtypes.bfloat16)
    sine = np.sin(angle).astype(ml_dtypes.bfloat16)
    table = np.concatenate([cosine, sine], axis=3)
    return jnp.asarray(table.reshape(chunks, groups * width, 2 * channels))


def fir_rows(taps_ref, extended, count):
    total = taps_ref[0:1, :] * extended[0:count]
    for tap_index in range(1, taps_ref.shape[0]):
        total = total + taps_ref[tap_index : tap_index + 1, :] * extended[tap_index : tap_index + count]
    return total.astype(jnp.bfloat16)


def fir_store(out_ref, station, filtered, channels):
    out_ref[0, station, :, 0:channels] = filtered[0]
    out_ref[0, station, :, channels:] = filtered[1]
    out_ref[1, station, :, 0:channels] = filtered[1]
    out_ref[1, station, :, channels:] = -filtered[0]


def fir_kernel(taps_ref, frames_ref, out_ref):
    halo = taps_ref.shape[0] - 1
    spectra = frames_ref.shape[2]
    channels = frames_ref.shape[3]

    def body(station, carry):
        filtered = []
        for part in range(2):
            frames = frames_ref[part, station].astype(jnp.float32)
            extended = jnp.concatenate([jnp.zeros((halo, channels), jnp.float32), frames], axis=0)
            filtered.append(fir_rows(taps_ref, extended, spectra))
        fir_store(out_ref, station, filtered, channels)
        return carry

    lax.fori_loop(0, frames_ref.shape[1], body, 0)


def fir_edge_kernel(taps_ref, halo_ref, frames_ref, previous_ref, out_ref):
    count = frames_ref.shape[2]
    channels = frames_ref.shape[3]

    def body(station, carry):
        filtered = []
        for part in range(2):
            extended = jnp.concatenate(
                [
                    halo_ref[part, station].astype(jnp.float32),
                    frames_ref[part, station].astype(jnp.float32),
                ],
                axis=0,
            )
            filtered.append(fir_rows(taps_ref, extended, count))
        fir_store(out_ref, station, filtered, channels)
        return carry

    lax.fori_loop(0, frames_ref.shape[1], body, 0)


def filter_frames(fir_taps, earlier, frames):
    tap_count, channels = fir_taps.shape
    _, stations_local, spectra, _ = frames.shape
    out_shape = jax.ShapeDtypeStruct((2, stations_local, spectra, 2 * channels), jnp.bfloat16)
    group = 4 if stations_local % 4 == 0 else 1
    whole = pl.pallas_call(
        fir_kernel,
        grid=(stations_local // group,),
        in_specs=[
            pl.BlockSpec((tap_count, channels), lambda a: (0, 0)),
            pl.BlockSpec((2, group, spectra, channels), lambda a: (0, a, 0, 0)),
        ],
        out_specs=pl.BlockSpec((2, group, spectra, 2 * channels), lambda a: (0, a, 0, 0)),
        out_shape=out_shape,
        cost_estimate=pl.CostEstimate(
            flops=4 * tap_count * frames.size,
            transcendentals=0,
            bytes_accessed=2 * frames.size + 4 * frames.size,
        ),
    )(fir_taps, frames)
    edge = 8
    edge_group = stations_local // 4 if stations_local % 4 == 0 else stations_local
    return pl.pallas_call(
        fir_edge_kernel,
        grid=(stations_local // edge_group,),
        in_specs=[
            pl.BlockSpec((tap_count, channels), lambda a: (0, 0)),
            pl.BlockSpec((2, edge_group, tap_count - 1, channels), lambda a: (0, a, 0, 0)),
            pl.BlockSpec((2, edge_group, edge, channels), lambda a: (0, a, 0, 0)),
            pl.BlockSpec(memory_space=pl.ANY),
        ],
        out_specs=pl.BlockSpec((2, edge_group, edge, 2 * channels), lambda a: (0, a, 0, 0)),
        out_shape=out_shape,
        input_output_aliases={3: 0},
        cost_estimate=pl.CostEstimate(
            flops=4 * tap_count * edge * frames.size // spectra,
            transcendentals=0,
            bytes_accessed=8 * edge * frames.size // spectra,
        ),
    )(fir_taps, earlier, frames, whole)


def correlate_kernel(rows_ref, cols_ref, *refs):
    out_ref = refs[-1]
    row_count = out_ref.shape[2]
    for index in range(out_ref.shape[1]):
        left = rows_ref[index]
        right = cols_ref[index]
        product = jnp.dot(left, right, preferred_element_type=jnp.float32)
        right = right.astype(jnp.float32)
        rows = left[0:row_count].astype(jnp.float32)
        column_power = jnp.sum(right * right, axis=0, keepdims=True)
        row_power = jnp.sum(rows * rows, axis=1, keepdims=True)
        scale_row = lax.rsqrt(row_power + epsilon)
        scale_column = lax.rsqrt(column_power + epsilon)
        out_ref[0, index] = (product[0:row_count] * scale_row * scale_column).astype(out_ref.dtype)
        out_ref[1, index] = (product[row_count:] * scale_row * scale_column).astype(out_ref.dtype)


def correlate_chunk(left, right, previous, offset, local_channels):
    width, double_rows, depth = left.shape
    row_count = double_rows // 2
    stations = right.shape[2]
    step = 4 if width % 4 == 0 and offset % 4 == 0 else 1
    in_specs = [
        pl.BlockSpec((step, double_rows, depth), lambda k: (k, 0, 0)),
        pl.BlockSpec((step, depth, stations), lambda k: (k, 0, 0)),
    ]
    operands = [left, right]
    aliases = {}
    if previous is not None:
        in_specs.append(pl.BlockSpec(memory_space=pl.ANY))
        operands.append(previous)
        aliases = {2: 0}
    return pl.pallas_call(
        correlate_kernel,
        grid=(width // step,),
        in_specs=in_specs,
        out_specs=pl.BlockSpec(
            (2, step, row_count, stations), lambda k: (0, offset // step + k, 0, 0)
        ),
        out_shape=jax.ShapeDtypeStruct((2, local_channels, row_count, stations), jnp.bfloat16),
        input_output_aliases=aliases,
        cost_estimate=pl.CostEstimate(
            flops=2 * width * double_rows * depth * stations,
            transcendentals=width * (row_count + stations),
            bytes_accessed=2 * (left.size + right.size + width * double_rows * stations),
        ),
    )(*operands)


def correlate_rows_kernel(block_ref, *refs):
    out_ref = refs[-1]
    pieces = (len(refs) - 1) // 2
    rows_refs = refs[0:pieces]
    cols_refs = refs[pieces : 2 * pieces]
    contract_first = (((0,), (0,)), ((), ()))
    for index in range(out_ref.shape[1]):
        rows = jnp.concatenate(
            [ref[index, part] for part in range(2) for ref in rows_refs], axis=0
        )
        right = jnp.concatenate(
            [ref[index, part] for part in range(2) for ref in cols_refs], axis=0
        )
        half = rows.shape[0] // 2
        swapped = jnp.concatenate([rows[half:], -rows[:half]], axis=0)
        real_vis = lax.dot_general(rows, right, contract_first, preferred_element_type=jnp.float32)
        imag_vis = lax.dot_general(swapped, right, contract_first, preferred_element_type=jnp.float32)
        right = right.astype(jnp.float32)
        rows = rows.astype(jnp.float32)
        column_power = jnp.sum(right * right, axis=0, keepdims=True)
        row_power = jnp.sum(jnp.transpose(rows * rows), axis=1, keepdims=True)
        scale_row = lax.rsqrt(row_power + epsilon)
        scale_column = lax.rsqrt(column_power + epsilon)
        out_ref[0, index] = (real_vis * scale_row * scale_column).astype(out_ref.dtype)
        out_ref[1, index] = (imag_vis * scale_row * scale_column).astype(out_ref.dtype)


def correlate_rows_chunk(parts, block, row_count, previous, offset, local_channels):
    width, _, spectra, stations = parts[0].shape
    step = 4 if width % 4 == 0 and offset % 4 == 0 else 1
    rows_spec = pl.BlockSpec((step, 2, spectra, row_count), lambda k, b: (k, 0, 0, b[0]))
    cols_spec = pl.BlockSpec((step, 2, spectra, stations), lambda k, b: (k, 0, 0, 0))
    in_specs = [rows_spec] * len(parts) + [cols_spec] * len(parts)
    operands = [block] + list(parts) + list(parts)
    aliases = {}
    if previous is not None:
        in_specs.append(pl.BlockSpec(memory_space=pl.ANY))
        operands.append(previous)
        aliases = {len(operands) - 1: 0}
    grid_spec = pltpu.PrefetchScalarGridSpec(
        num_scalar_prefetch=1,
        grid=(width // step,),
        in_specs=in_specs,
        out_specs=pl.BlockSpec(
            (2, step, row_count, stations), lambda k, b: (0, offset // step + k, 0, 0)
        ),
    )
    depth = 2 * spectra * len(parts)
    return pl.pallas_call(
        correlate_rows_kernel,
        grid_spec=grid_spec,
        out_shape=jax.ShapeDtypeStruct((2, local_channels, row_count, stations), jnp.bfloat16),
        input_output_aliases=aliases,
        cost_estimate=pl.CostEstimate(
            flops=4 * width * row_count * depth * stations,
            transcendentals=width * (row_count + stations),
            bytes_accessed=2 * width * depth * (stations + row_count)
            + 4 * width * row_count * stations,
        ),
    )(*operands)


def per_device(samples, fir_taps, station_order):
    tap_count = fir_taps.shape[0]
    channels = fir_taps.shape[1]
    stations_local = samples.shape[1]
    spectra_local = samples.shape[2] // channels
    stations = station_order.shape[0]
    groups = lax.axis_size("stn")
    blocks = lax.axis_size("blk")
    local_channels = channels // groups
    row_count = stations // blocks
    chunks = chunk_count(local_channels)
    width = local_channels // chunks

    earlier = samples[:, :, (spectra_local - (tap_count - 1)) * channels :].astype(jnp.bfloat16)
    earlier = earlier.reshape(2, stations_local, tap_count - 1, channels)
    frames = samples.astype(jnp.bfloat16).reshape(2, stations_local, spectra_local, channels)
    earlier = passed_along(earlier, "blk", 1)
    filtered = filter_frames(fir_taps, earlier, frames)
    filtered = filtered.reshape(2 * stations_local * spectra_local, 2 * channels)

    weights = dft_weights(channels, groups, chunks)
    selector = (
        station_order[None, :] == jnp.arange(stations, dtype=jnp.int32)[:, None]
    ).astype(jnp.bfloat16)
    selector = selector.reshape(groups, stations_local, stations)
    row_start = lax.axis_index("blk") * row_count

    block_index = jnp.reshape(lax.axis_index("blk"), (1,)).astype(jnp.int32)

    def correlate(chunk, parts, result):
        parts = [part.reshape(width, 2, spectra_local, stations) for part in parts]
        if row_count % 128 == 0:
            return correlate_rows_chunk(
                parts, block_index, row_count, result, chunk * width, local_channels
            )
        gathered = jnp.concatenate(parts, axis=2)
        row_block = lax.dynamic_slice_in_dim(gathered, row_start, row_count, 3)
        direct = jnp.transpose(row_block, (0, 3, 1, 2))
        swapped = jnp.stack([direct[:, :, 1], -direct[:, :, 0]], axis=2)
        left = jnp.concatenate([direct, swapped], axis=1).reshape(width, 2 * row_count, -1)
        right = gathered.reshape(width, -1, stations)
        return correlate_chunk(left, right, result, chunk * width, local_channels)

    def reorder(turned):
        turned = turned.reshape(groups, width, 2, stations_local, spectra_local)
        ordered = jnp.einsum(
            "gkias,gar->kisr", turned, selector, preferred_element_type=jnp.float32
        ).astype(jnp.bfloat16)
        return ordered.reshape(width * 2, spectra_local, stations)

    result = None
    pending = []
    turned = None
    for chunk in range(chunks):
        source = filtered
        if chunk >= 2:
            result = correlate(chunk - 2, pending[chunk - 2], result)
            source, result = lax.optimization_barrier((filtered, result))
        spectra = jnp.einsum(
            "kj,nj->kn", weights[chunk], source, preferred_element_type=jnp.float32
        ).astype(jnp.bfloat16)
        spectra = spectra.reshape(groups, width, 2 * stations_local * spectra_local)
        if chunk >= 1:
            ordered = reorder(turned)
            spectra, ordered = lax.optimization_barrier((spectra, ordered))
            pending.append(gathered_along(ordered, "blk"))
        turned = lax.all_to_all(spectra, "stn", split_axis=0, concat_axis=0, tiled=True)
    pending.append(gathered_along(reorder(turned), "blk"))
    for chunk in range(max(0, chunks - 2), chunks):
        result = correlate(chunk, pending[chunk], result)
    return result


def solution(mesh):
    placed = (P(None, "stn", "blk"), P(), P())
    return jax.shard_map(
        per_device,
        mesh=mesh,
        in_specs=placed,
        out_specs=P(None, "stn", "blk", None),
        check_vma=False,
    )
```

```python
import math

import jax
import ml_dtypes
import numpy as np
import jax.numpy as jnp
from jax import lax
from jax.experimental import pallas as pl
from jax.experimental.pallas import tpu as pltpu
from jax.sharding import PartitionSpec as P

epsilon = 1e-06


def passed_along(value, axis, steps):
    count = lax.axis_size(axis)
    initial, last = (max(0, -steps), min(count, count - steps))
    return lax.ppermute(value, axis, [(source, source + steps) for source in range(initial, last)])


def gathered_along(value, axis):
    count = lax.axis_size(axis)
    parts = [value]
    for shift in range(1, count):
        pairs = [(source, (source + shift) % count) for source in range(count)]
        parts.append(lax.ppermute(value, axis, pairs))
    return parts


def chunk_count(local_channels):
    for count in (4, 2):
        if local_channels % count == 0:
            return count
    return 1


def dft_weights(channels, groups, chunks):
    local = channels // groups
    width = local // chunks
    chunk = np.arange(chunks).reshape(chunks, 1, 1, 1)
    group = np.arange(groups).reshape(1, groups, 1, 1)
    inner = np.arange(width).reshape(1, 1, width, 1)
    column = np.arange(channels).reshape(1, 1, 1, channels)
    row = group * local + chunk * width + inner
    phase_index = (row * column % channels).astype(np.float32)
    angle = phase_index * np.float32(2.0 * math.pi / channels)
    cosine = np.cos(angle).astype(ml_dtypes.bfloat16)
    sine = np.sin(angle).astype(ml_dtypes.bfloat16)
    table = np.concatenate([cosine, sine], axis=3)
    return jnp.asarray(table.reshape(chunks, groups * width, 2 * channels))


def fir_rows(taps_ref, extended, count):
    total = taps_ref[0:1, :] * extended[0:count]
    for tap_index in range(1, taps_ref.shape[0]):
        total = total + taps_ref[tap_index : tap_index + 1, :] * extended[tap_index : tap_index + count]
    return total.astype(jnp.bfloat16)


def fir_store(out_ref, station, filtered, channels):
    out_ref[0, station, :, 0:channels] = filtered[0]
    out_ref[0, station, :, channels:] = filtered[1]
    out_ref[1, station, :, 0:channels] = filtered[1]
    out_ref[1, station, :, channels:] = -filtered[0]


def fir_kernel(taps_ref, frames_ref, out_ref):
    halo = taps_ref.shape[0] - 1
    spectra = frames_ref.shape[2]
    channels = frames_ref.shape[3]

    def body(station, carry):
        filtered = []
        for part in range(2):
            frames = frames_ref[part, station].astype(jnp.float32)
            extended = jnp.concatenate([jnp.zeros((halo, channels), jnp.float32), frames], axis=0)
            filtered.append(fir_rows(taps_ref, extended, spectra))
        fir_store(out_ref, station, filtered, channels)
        return carry

    lax.fori_loop(0, frames_ref.shape[1], body, 0)


def fir_edge_kernel(taps_ref, halo_ref, frames_ref, previous_ref, out_ref):
    count = frames_ref.shape[2]
    channels = frames_ref.shape[3]

    def body(station, carry):
        filtered = []
        for part in range(2):
            extended = jnp.concatenate(
                [
                    halo_ref[part, station].astype(jnp.float32),
                    frames_ref[part, station].astype(jnp.float32),
                ],
                axis=0,
            )
            filtered.append(fir_rows(taps_ref, extended, count))
        fir_store(out_ref, station, filtered, channels)
        return carry

    lax.fori_loop(0, frames_ref.shape[1], body, 0)


def filter_frames(fir_taps, earlier, frames):
    tap_count, channels = fir_taps.shape
    _, stations_local, spectra, _ = frames.shape
    out_shape = jax.ShapeDtypeStruct((2, stations_local, spectra, 2 * channels), jnp.bfloat16)
    group = 4 if stations_local % 4 == 0 else 1
    whole = pl.pallas_call(
        fir_kernel,
        grid=(stations_local // group,),
        in_specs=[
            pl.BlockSpec((tap_count, channels), lambda a: (0, 0)),
            pl.BlockSpec((2, group, spectra, channels), lambda a: (0, a, 0, 0)),
        ],
        out_specs=pl.BlockSpec((2, group, spectra, 2 * channels), lambda a: (0, a, 0, 0)),
        out_shape=out_shape,
        cost_estimate=pl.CostEstimate(
            flops=4 * tap_count * frames.size,
            transcendentals=0,
            bytes_accessed=2 * frames.size + 4 * frames.size,
        ),
    )(fir_taps, frames)
    edge = 8
    edge_group = stations_local // 4 if stations_local % 4 == 0 else stations_local
    return pl.pallas_call(
        fir_edge_kernel,
        grid=(stations_local // edge_group,),
        in_specs=[
            pl.BlockSpec((tap_count, channels), lambda a: (0, 0)),
            pl.BlockSpec((2, edge_group, tap_count - 1, channels), lambda a: (0, a, 0, 0)),
            pl.BlockSpec((2, edge_group, edge, channels), lambda a: (0, a, 0, 0)),
            pl.BlockSpec(memory_space=pl.ANY),
        ],
        out_specs=pl.BlockSpec((2, edge_group, edge, 2 * channels), lambda a: (0, a, 0, 0)),
        out_shape=out_shape,
        input_output_aliases={3: 0},
        cost_estimate=pl.CostEstimate(
            flops=4 * tap_count * edge * frames.size // spectra,
            transcendentals=0,
            bytes_accessed=8 * edge * frames.size // spectra,
        ),
    )(fir_taps, earlier, frames, whole)


def correlate_kernel(rows_ref, cols_ref, *refs):
    out_ref = refs[-1]
    row_count = out_ref.shape[2]
    for index in range(out_ref.shape[1]):
        left = rows_ref[index]
        right = cols_ref[index]
        product = jnp.dot(left, right, preferred_element_type=jnp.float32)
        right = right.astype(jnp.float32)
        rows = left[0:row_count].astype(jnp.float32)
        column_power = jnp.sum(right * right, axis=0, keepdims=True)
        row_power = jnp.sum(rows * rows, axis=1, keepdims=True)
        scale_row = lax.rsqrt(row_power + epsilon)
        scale_column = lax.rsqrt(column_power + epsilon)
        out_ref[0, index] = (product[0:row_count] * scale_row * scale_column).astype(out_ref.dtype)
        out_ref[1, index] = (product[row_count:] * scale_row * scale_column).astype(out_ref.dtype)


def correlate_chunk(left, right, previous, offset, local_channels):
    width, double_rows, depth = left.shape
    row_count = double_rows // 2
    stations = right.shape[2]
    step = 4 if width % 4 == 0 and offset % 4 == 0 else 1
    in_specs = [
        pl.BlockSpec((step, double_rows, depth), lambda k: (k, 0, 0)),
        pl.BlockSpec((step, depth, stations), lambda k: (k, 0, 0)),
    ]
    operands = [left, right]
    aliases = {}
    if previous is not None:
        in_specs.append(pl.BlockSpec(memory_space=pl.ANY))
        operands.append(previous)
        aliases = {2: 0}
    return pl.pallas_call(
        correlate_kernel,
        grid=(width // step,),
        in_specs=in_specs,
        out_specs=pl.BlockSpec(
            (2, step, row_count, stations), lambda k: (0, offset // step + k, 0, 0)
        ),
        out_shape=jax.ShapeDtypeStruct((2, local_channels, row_count, stations), jnp.bfloat16),
        input_output_aliases=aliases,
        cost_estimate=pl.CostEstimate(
            flops=2 * width * double_rows * depth * stations,
            transcendentals=width * (row_count + stations),
            bytes_accessed=2 * (left.size + right.size + width * double_rows * stations),
        ),
    )(*operands)


def correlate_rows_kernel(block_ref, *refs):
    out_ref = refs[-1]
    pieces = (len(refs) - 1) // 2
    rows_refs = refs[0:pieces]
    cols_refs = refs[pieces : 2 * pieces]
    contract_first = (((0,), (0,)), ((), ()))
    for index in range(out_ref.shape[1]):
        rows = jnp.concatenate(
            [ref[index, part] for part in range(2) for ref in rows_refs], axis=0
        )
        right = jnp.concatenate(
            [ref[index, part] for part in range(2) for ref in cols_refs], axis=0
        )
        half = rows.shape[0] // 2
        swapped = jnp.concatenate([rows[half:], -rows[:half]], axis=0)
        real_vis = lax.dot_general(rows, right, contract_first, preferred_element_type=jnp.float32)
        imag_vis = lax.dot_general(swapped, right, contract_first, preferred_element_type=jnp.float32)
        right = right.astype(jnp.float32)
        rows = rows.astype(jnp.float32)
        column_power = jnp.sum(right * right, axis=0, keepdims=True)
        row_power = jnp.sum(jnp.transpose(rows * rows), axis=1, keepdims=True)
        scale_row = lax.rsqrt(row_power + epsilon)
        scale_column = lax.rsqrt(column_power + epsilon)
        out_ref[0, index] = (real_vis * scale_row * scale_column).astype(out_ref.dtype)
        out_ref[1, index] = (imag_vis * scale_row * scale_column).astype(out_ref.dtype)


def correlate_rows_chunk(parts, block, row_count, previous, offset, local_channels):
    width, _, spectra, stations = parts[0].shape
    step = 4 if width % 4 == 0 and offset % 4 == 0 else 1
    rows_spec = pl.BlockSpec((step, 2, spectra, row_count), lambda k, b: (k, 0, 0, b[0]))
    cols_spec = pl.BlockSpec((step, 2, spectra, stations), lambda k, b: (k, 0, 0, 0))
    in_specs = [rows_spec] * len(parts) + [cols_spec] * len(parts)
    operands = [block] + list(parts) + list(parts)
    aliases = {}
    if previous is not None:
        in_specs.append(pl.BlockSpec(memory_space=pl.ANY))
        operands.append(previous)
        aliases = {len(operands) - 1: 0}
    grid_spec = pltpu.PrefetchScalarGridSpec(
        num_scalar_prefetch=1,
        grid=(width // step,),
        in_specs=in_specs,
        out_specs=pl.BlockSpec(
            (2, step, row_count, stations), lambda k, b: (0, offset // step + k, 0, 0)
        ),
    )
    depth = 2 * spectra * len(parts)
    return pl.pallas_call(
        correlate_rows_kernel,
        grid_spec=grid_spec,
        out_shape=jax.ShapeDtypeStruct((2, local_channels, row_count, stations), jnp.bfloat16),
        input_output_aliases=aliases,
        cost_estimate=pl.CostEstimate(
            flops=4 * width * row_count * depth * stations,
            transcendentals=width * (row_count + stations),
            bytes_accessed=2 * width * depth * (stations + row_count)
            + 4 * width * row_count * stations,
        ),
    )(*operands)


def per_device(samples, fir_taps, station_order):
    tap_count = fir_taps.shape[0]
    channels = fir_taps.shape[1]
    stations_local = samples.shape[1]
    spectra_local = samples.shape[2] // channels
    stations = station_order.shape[0]
    groups = lax.axis_size("stn")
    blocks = lax.axis_size("blk")
    local_channels = channels // groups
    row_count = stations // blocks
    chunks = chunk_count(local_channels)
    width = local_channels // chunks

    earlier = samples[:, :, (spectra_local - (tap_count - 1)) * channels :].astype(jnp.bfloat16)
    earlier = earlier.reshape(2, stations_local, tap_count - 1, channels)
    frames = samples.astype(jnp.bfloat16).reshape(2, stations_local, spectra_local, channels)
    earlier = passed_along(earlier, "blk", 1)
    filtered = filter_frames(fir_taps, earlier, frames)
    filtered = filtered.reshape(2 * stations_local * spectra_local, 2 * channels)

    weights = dft_weights(channels, groups, chunks)
    selector = (
        station_order[None, :] == jnp.arange(stations, dtype=jnp.int32)[:, None]
    ).astype(jnp.bfloat16)
    selector = selector.reshape(groups, stations_local, stations)
    row_start = lax.axis_index("blk") * row_count

    block_index = jnp.reshape(lax.axis_index("blk"), (1,)).astype(jnp.int32)

    def correlate(chunk, parts, result):
        parts = [part.reshape(width, 2, spectra_local, stations) for part in parts]
        if row_count % 128 == 0:
            return correlate_rows_chunk(
                parts, block_index, row_count, result, chunk * width, local_channels
            )
        gathered = jnp.concatenate(parts, axis=2)
        row_block = lax.dynamic_slice_in_dim(gathered, row_start, row_count, 3)
        direct = jnp.transpose(row_block, (0, 3, 1, 2))
        swapped = jnp.stack([direct[:, :, 1], -direct[:, :, 0]], axis=2)
        left = jnp.concatenate([direct, swapped], axis=1).reshape(width, 2 * row_count, -1)
        right = gathered.reshape(width, -1, stations)
        return correlate_chunk(left, right, result, chunk * width, local_channels)

    def reorder(turned):
        turned = turned.reshape(groups, width, 2, stations_local, spectra_local)
        ordered = jnp.einsum(
            "gkias,gar->kisr", turned, selector, preferred_element_type=jnp.float32
        ).astype(jnp.bfloat16)
        return ordered.reshape(width * 2, spectra_local, stations)

    result = None
    pending = []
    reordered = []
    for chunk in range(chunks):
        source = filtered
        if chunk >= 2:
            parts, following = lax.optimization_barrier((pending[chunk - 2], reordered[chunk - 1]))
            pending.append(gathered_along(following, "blk"))
            result = correlate(chunk - 2, parts, result)
            source, result = lax.optimization_barrier((filtered, result))
        spectra = jnp.einsum(
            "kj,nj->kn", weights[chunk], source, preferred_element_type=jnp.float32
        ).astype(jnp.bfloat16)
        spectra = spectra.reshape(groups, width, 2 * stations_local * spectra_local)
        turned = lax.all_to_all(spectra, "stn", split_axis=0, concat_axis=0, tiled=True)
        reordered.append(reorder(turned))
        if chunk == 0:
            pending.append(gathered_along(reordered[0], "blk"))
    if chunks >= 2:
        parts, following = lax.optimization_barrier((pending[chunks - 2], reordered[chunks - 1]))
        pending.append(gathered_along(following, "blk"))
        result = correlate(chunks - 2, parts, result)
    result = correlate(chunks - 1, pending[chunks - 1], result)
    return result


def solution(mesh):
    placed = (P(None, "stn", "blk"), P(), P())
    return jax.shard_map(
        per_device,
        mesh=mesh,
        in_specs=placed,
        out_specs=P(None, "stn", "blk", None),
        check_vma=False,
    )
```

```python
import math

import jax
import ml_dtypes
import numpy as np
import jax.numpy as jnp
from jax import lax
from jax.experimental import pallas as pl
from jax.experimental.pallas import tpu as pltpu
from jax.sharding import PartitionSpec as P

epsilon = 1e-06


def passed_along(value, axis, steps):
    count = lax.axis_size(axis)
    initial, last = (max(0, -steps), min(count, count - steps))
    return lax.ppermute(value, axis, [(source, source + steps) for source in range(initial, last)])


def gathered_along(value, axis, dimension):
    count = lax.axis_size(axis)
    parts = [value]
    for shift in range(1, count):
        pairs = [(source, (source + shift) % count) for source in range(count)]
        parts.append(lax.ppermute(value, axis, pairs))
    return jnp.concatenate(parts, axis=dimension)


def chunk_count(local_channels):
    for count in (4, 2):
        if local_channels % count == 0:
            return count
    return 1


def dft_weights(channels, groups, chunks):
    local = channels // groups
    width = local // chunks
    chunk = np.arange(chunks).reshape(chunks, 1, 1, 1)
    group = np.arange(groups).reshape(1, groups, 1, 1)
    inner = np.arange(width).reshape(1, 1, width, 1)
    column = np.arange(channels).reshape(1, 1, 1, channels)
    row = group * local + chunk * width + inner
    phase_index = (row * column % channels).astype(np.float32)
    angle = phase_index * np.float32(2.0 * math.pi / channels)
    cosine = np.cos(angle).astype(ml_dtypes.bfloat16)
    sine = np.sin(angle).astype(ml_dtypes.bfloat16)
    table = np.concatenate([cosine, sine], axis=3)
    return jnp.asarray(table.reshape(chunks, groups * width, 2 * channels))


def fir_rows(taps_ref, extended, count):
    total = taps_ref[0:1, :] * extended[0:count]
    for tap_index in range(1, taps_ref.shape[0]):
        total = total + taps_ref[tap_index : tap_index + 1, :] * extended[tap_index : tap_index + count]
    return total.astype(jnp.bfloat16)


def fir_store(out_ref, station, filtered, channels):
    out_ref[0, station, :, 0:channels] = filtered[0]
    out_ref[0, station, :, channels:] = filtered[1]
    out_ref[1, station, :, 0:channels] = filtered[1]
    out_ref[1, station, :, channels:] = -filtered[0]


def fir_kernel(taps_ref, frames_ref, out_ref):
    halo = taps_ref.shape[0] - 1
    spectra = frames_ref.shape[2]
    channels = frames_ref.shape[3]

    def body(station, carry):
        filtered = []
        for part in range(2):
            frames = frames_ref[part, station].astype(jnp.float32)
            extended = jnp.concatenate([jnp.zeros((halo, channels), jnp.float32), frames], axis=0)
            filtered.append(fir_rows(taps_ref, extended, spectra))
        fir_store(out_ref, station, filtered, channels)
        return carry

    lax.fori_loop(0, frames_ref.shape[1], body, 0)


def fir_edge_kernel(taps_ref, halo_ref, frames_ref, previous_ref, out_ref):
    count = frames_ref.shape[2]
    channels = frames_ref.shape[3]

    def body(station, carry):
        filtered = []
        for part in range(2):
            extended = jnp.concatenate(
                [
                    halo_ref[part, station].astype(jnp.float32),
                    frames_ref[part, station].astype(jnp.float32),
                ],
                axis=0,
            )
            filtered.append(fir_rows(taps_ref, extended, count))
        fir_store(out_ref, station, filtered, channels)
        return carry

    lax.fori_loop(0, frames_ref.shape[1], body, 0)


def filter_frames(fir_taps, earlier, frames):
    tap_count, channels = fir_taps.shape
    _, stations_local, spectra, _ = frames.shape
    out_shape = jax.ShapeDtypeStruct((2, stations_local, spectra, 2 * channels), jnp.bfloat16)
    group = 4 if stations_local % 4 == 0 else 1
    whole = pl.pallas_call(
        fir_kernel,
        grid=(stations_local // group,),
        in_specs=[
            pl.BlockSpec((tap_count, channels), lambda a: (0, 0)),
            pl.BlockSpec((2, group, spectra, channels), lambda a: (0, a, 0, 0)),
        ],
        out_specs=pl.BlockSpec((2, group, spectra, 2 * channels), lambda a: (0, a, 0, 0)),
        out_shape=out_shape,
        cost_estimate=pl.CostEstimate(
            flops=4 * tap_count * frames.size,
            transcendentals=0,
            bytes_accessed=2 * frames.size + 4 * frames.size,
        ),
    )(fir_taps, frames)
    edge = 8
    edge_group = stations_local // 4 if stations_local % 4 == 0 else stations_local
    return pl.pallas_call(
        fir_edge_kernel,
        grid=(stations_local // edge_group,),
        in_specs=[
            pl.BlockSpec((tap_count, channels), lambda a: (0, 0)),
            pl.BlockSpec((2, edge_group, tap_count - 1, channels), lambda a: (0, a, 0, 0)),
            pl.BlockSpec((2, edge_group, edge, channels), lambda a: (0, a, 0, 0)),
            pl.BlockSpec(memory_space=pl.ANY),
        ],
        out_specs=pl.BlockSpec((2, edge_group, edge, 2 * channels), lambda a: (0, a, 0, 0)),
        out_shape=out_shape,
        input_output_aliases={3: 0},
        cost_estimate=pl.CostEstimate(
            flops=4 * tap_count * edge * frames.size // spectra,
            transcendentals=0,
            bytes_accessed=8 * edge * frames.size // spectra,
        ),
    )(fir_taps, earlier, frames, whole)


def correlate_kernel(rows_ref, cols_ref, *refs):
    out_ref = refs[-1]
    row_count = out_ref.shape[2]
    for index in range(out_ref.shape[1]):
        left = rows_ref[index]
        right = cols_ref[index]
        product = jnp.dot(left, right, preferred_element_type=jnp.float32)
        right = right.astype(jnp.float32)
        rows = left[0:row_count].astype(jnp.float32)
        column_power = jnp.sum(right * right, axis=0, keepdims=True)
        row_power = jnp.sum(rows * rows, axis=1, keepdims=True)
        scale_row = lax.rsqrt(row_power + epsilon)
        scale_column = lax.rsqrt(column_power + epsilon)
        out_ref[0, index] = (product[0:row_count] * scale_row * scale_column).astype(out_ref.dtype)
        out_ref[1, index] = (product[row_count:] * scale_row * scale_column).astype(out_ref.dtype)


def correlate_chunk(left, right, previous, offset, local_channels):
    width, double_rows, depth = left.shape
    row_count = double_rows // 2
    stations = right.shape[2]
    step = 4 if width % 4 == 0 and offset % 4 == 0 else 1
    in_specs = [
        pl.BlockSpec((step, double_rows, depth), lambda k: (k, 0, 0)),
        pl.BlockSpec((step, depth, stations), lambda k: (k, 0, 0)),
    ]
    operands = [left, right]
    aliases = {}
    if previous is not None:
        in_specs.append(pl.BlockSpec(memory_space=pl.ANY))
        operands.append(previous)
        aliases = {2: 0}
    return pl.pallas_call(
        correlate_kernel,
        grid=(width // step,),
        in_specs=in_specs,
        out_specs=pl.BlockSpec(
            (2, step, row_count, stations), lambda k: (0, offset // step + k, 0, 0)
        ),
        out_shape=jax.ShapeDtypeStruct((2, local_channels, row_count, stations), jnp.bfloat16),
        input_output_aliases=aliases,
        cost_estimate=pl.CostEstimate(
            flops=2 * width * double_rows * depth * stations,
            transcendentals=width * (row_count + stations),
            bytes_accessed=2 * (left.size + right.size + width * double_rows * stations),
        ),
    )(*operands)


def correlate_rows_kernel(block_ref, rows_ref, cols_ref, *refs):
    out_ref = refs[-1]
    half = cols_ref.shape[1] // 2
    contract_first = (((0,), (0,)), ((), ()))
    for index in range(out_ref.shape[1]):
        rows = rows_ref[index]
        right = cols_ref[index]
        swapped = jnp.concatenate([rows[half:], -rows[:half]], axis=0)
        real_vis = lax.dot_general(rows, right, contract_first, preferred_element_type=jnp.float32)
        imag_vis = lax.dot_general(swapped, right, contract_first, preferred_element_type=jnp.float32)
        right = right.astype(jnp.float32)
        rows = rows.astype(jnp.float32)
        column_power = jnp.sum(right * right, axis=0, keepdims=True)
        row_power = jnp.sum(jnp.transpose(rows * rows), axis=1, keepdims=True)
        scale_row = lax.rsqrt(row_power + epsilon)
        scale_column = lax.rsqrt(column_power + epsilon)
        out_ref[0, index] = (real_vis * scale_row * scale_column).astype(out_ref.dtype)
        out_ref[1, index] = (imag_vis * scale_row * scale_column).astype(out_ref.dtype)


def correlate_rows_chunk(right, block, row_count, previous, offset, local_channels):
    width, depth, stations = right.shape
    step = 4 if width % 4 == 0 and offset % 4 == 0 else 1
    in_specs = [
        pl.BlockSpec((step, depth, row_count), lambda k, b: (k, 0, b[0])),
        pl.BlockSpec((step, depth, stations), lambda k, b: (k, 0, 0)),
    ]
    operands = [block, right, right]
    aliases = {}
    if previous is not None:
        in_specs.append(pl.BlockSpec(memory_space=pl.ANY))
        operands.append(previous)
        aliases = {3: 0}
    grid_spec = pltpu.PrefetchScalarGridSpec(
        num_scalar_prefetch=1,
        grid=(width // step,),
        in_specs=in_specs,
        out_specs=pl.BlockSpec(
            (2, step, row_count, stations), lambda k, b: (0, offset // step + k, 0, 0)
        ),
    )
    return pl.pallas_call(
        correlate_rows_kernel,
        grid_spec=grid_spec,
        out_shape=jax.ShapeDtypeStruct((2, local_channels, row_count, stations), jnp.bfloat16),
        input_output_aliases=aliases,
        cost_estimate=pl.CostEstimate(
            flops=4 * width * row_count * depth * stations,
            transcendentals=width * (row_count + stations),
            bytes_accessed=2 * (right.size + width * depth * row_count + 2 * width * row_count * stations),
        ),
    )(*operands)


def per_device(samples, fir_taps, station_order):
    tap_count = fir_taps.shape[0]
    channels = fir_taps.shape[1]
    stations_local = samples.shape[1]
    spectra_local = samples.shape[2] // channels
    stations = station_order.shape[0]
    groups = lax.axis_size("stn")
    blocks = lax.axis_size("blk")
    local_channels = channels // groups
    row_count = stations // blocks
    chunks = chunk_count(local_channels)
    width = local_channels // chunks

    earlier = samples[:, :, (spectra_local - (tap_count - 1)) * channels :].astype(jnp.bfloat16)
    earlier = earlier.reshape(2, stations_local, tap_count - 1, channels)
    frames = samples.astype(jnp.bfloat16).reshape(2, stations_local, spectra_local, channels)
    earlier = passed_along(earlier, "blk", 1)
    filtered = filter_frames(fir_taps, earlier, frames)
    filtered = filtered.reshape(2 * stations_local * spectra_local, 2 * channels)

    weights = dft_weights(channels, groups, chunks)
    selector = (
        station_order[None, :] == jnp.arange(stations, dtype=jnp.int32)[:, None]
    ).astype(jnp.bfloat16)
    selector = selector.reshape(groups, stations_local, stations)
    row_start = lax.axis_index("blk") * row_count

    block_index = jnp.reshape(lax.axis_index("blk"), (1,)).astype(jnp.int32)

    def correlate(chunk, gathered, result):
        if row_count % 128 == 0:
            right = gathered.reshape(width, -1, stations)
            return correlate_rows_chunk(
                right, block_index, row_count, result, chunk * width, local_channels
            )
        gathered = gathered.reshape(width, 2, -1, stations)
        row_block = lax.dynamic_slice_in_dim(gathered, row_start, row_count, 3)
        direct = jnp.transpose(row_block, (0, 3, 1, 2))
        swapped = jnp.stack([direct[:, :, 1], -direct[:, :, 0]], axis=2)
        left = jnp.concatenate([direct, swapped], axis=1).reshape(width, 2 * row_count, -1)
        right = gathered.reshape(width, -1, stations)
        return correlate_chunk(left, right, result, chunk * width, local_channels)

    result = None
    pending = []
    for chunk in range(chunks):
        source = filtered
        if chunk >= 2:
            result = correlate(chunk - 2, pending[chunk - 2], result)
            source, result = lax.optimization_barrier((filtered, result))
        spectra = jnp.einsum(
            "kj,nj->kn", weights[chunk], source, preferred_element_type=jnp.float32
        ).astype(jnp.bfloat16)
        spectra = spectra.reshape(groups, width, 2 * stations_local * spectra_local)
        turned = lax.all_to_all(spectra, "stn", split_axis=0, concat_axis=0, tiled=True)
        turned = turned.reshape(groups, width, 2, stations_local, spectra_local)
        ordered = jnp.einsum(
            "gkias,gar->kisr", turned, selector, preferred_element_type=jnp.float32
        ).astype(jnp.bfloat16)
        ordered = ordered.reshape(width * 2, spectra_local, stations)
        pending.append(gathered_along(ordered, "blk", 1))
    for chunk in range(max(0, chunks - 2), chunks):
        result = correlate(chunk, pending[chunk], result)
    return result


def solution(mesh):
    placed = (P(None, "stn", "blk"), P(), P())
    return jax.shard_map(
        per_device,
        mesh=mesh,
        in_specs=placed,
        out_specs=P(None, "stn", "blk", None),
        check_vma=False,
    )
```

```python
import math

import jax
import ml_dtypes
import numpy as np
import jax.numpy as jnp
from jax import lax
from jax.experimental import pallas as pl
from jax.experimental.pallas import tpu as pltpu
from jax.sharding import PartitionSpec as P

epsilon = 1e-06


def passed_along(value, axis, steps):
    count = lax.axis_size(axis)
    initial, last = (max(0, -steps), min(count, count - steps))
    return lax.ppermute(value, axis, [(source, source + steps) for source in range(initial, last)])


def gathered_along(value, axis, dimension):
    count = lax.axis_size(axis)
    parts = [value]
    for shift in range(1, count):
        pairs = [(source, (source + shift) % count) for source in range(count)]
        parts.append(lax.ppermute(value, axis, pairs))
    return jnp.concatenate(parts, axis=dimension)


def chunk_count(local_channels):
    for count in (4, 2):
        if local_channels % count == 0:
            return count
    return 1


def dft_weights(channels, groups, chunks):
    local = channels // groups
    width = local // chunks
    chunk = np.arange(chunks).reshape(chunks, 1, 1, 1)
    group = np.arange(groups).reshape(1, groups, 1, 1)
    inner = np.arange(width).reshape(1, 1, width, 1)
    column = np.arange(channels).reshape(1, 1, 1, channels)
    row = group * local + chunk * width + inner
    phase_index = (row * column % channels).astype(np.float32)
    angle = phase_index * np.float32(2.0 * math.pi / channels)
    cosine = np.cos(angle).astype(ml_dtypes.bfloat16)
    sine = np.sin(angle).astype(ml_dtypes.bfloat16)
    table = np.concatenate([cosine, sine], axis=3)
    return jnp.asarray(table.reshape(chunks, groups * width, 2 * channels))


def fir_rows(taps_ref, extended, count):
    total = taps_ref[0:1, :] * extended[0:count]
    for tap_index in range(1, taps_ref.shape[0]):
        total = total + taps_ref[tap_index : tap_index + 1, :] * extended[tap_index : tap_index + count]
    return total.astype(jnp.bfloat16)


def fir_store(out_ref, station, filtered, channels):
    out_ref[0, station, :, 0:channels] = filtered[0]
    out_ref[0, station, :, channels:] = filtered[1]
    out_ref[1, station, :, 0:channels] = filtered[1]
    out_ref[1, station, :, channels:] = -filtered[0]


def fir_kernel(taps_ref, frames_ref, out_ref):
    halo = taps_ref.shape[0] - 1
    spectra = frames_ref.shape[2]
    channels = frames_ref.shape[3]

    def body(station, carry):
        filtered = []
        for part in range(2):
            frames = frames_ref[part, station].astype(jnp.float32)
            extended = jnp.concatenate([jnp.zeros((halo, channels), jnp.float32), frames], axis=0)
            filtered.append(fir_rows(taps_ref, extended, spectra))
        fir_store(out_ref, station, filtered, channels)
        return carry

    lax.fori_loop(0, frames_ref.shape[1], body, 0)


def fir_edge_kernel(taps_ref, halo_ref, frames_ref, previous_ref, out_ref):
    count = frames_ref.shape[2]
    channels = frames_ref.shape[3]

    def body(station, carry):
        filtered = []
        for part in range(2):
            extended = jnp.concatenate(
                [
                    halo_ref[part, station].astype(jnp.float32),
                    frames_ref[part, station].astype(jnp.float32),
                ],
                axis=0,
            )
            filtered.append(fir_rows(taps_ref, extended, count))
        fir_store(out_ref, station, filtered, channels)
        return carry

    lax.fori_loop(0, frames_ref.shape[1], body, 0)


def filter_frames(fir_taps, earlier, frames):
    tap_count, channels = fir_taps.shape
    _, stations_local, spectra, _ = frames.shape
    out_shape = jax.ShapeDtypeStruct((2, stations_local, spectra, 2 * channels), jnp.bfloat16)
    group = 4 if stations_local % 4 == 0 else 1
    whole = pl.pallas_call(
        fir_kernel,
        grid=(stations_local // group,),
        in_specs=[
            pl.BlockSpec((tap_count, channels), lambda a: (0, 0)),
            pl.BlockSpec((2, group, spectra, channels), lambda a: (0, a, 0, 0)),
        ],
        out_specs=pl.BlockSpec((2, group, spectra, 2 * channels), lambda a: (0, a, 0, 0)),
        out_shape=out_shape,
        cost_estimate=pl.CostEstimate(
            flops=4 * tap_count * frames.size,
            transcendentals=0,
            bytes_accessed=2 * frames.size + 4 * frames.size,
        ),
    )(fir_taps, frames)
    edge = 8
    edge_group = stations_local // 4 if stations_local % 4 == 0 else stations_local
    return pl.pallas_call(
        fir_edge_kernel,
        grid=(stations_local // edge_group,),
        in_specs=[
            pl.BlockSpec((tap_count, channels), lambda a: (0, 0)),
            pl.BlockSpec((2, edge_group, tap_count - 1, channels), lambda a: (0, a, 0, 0)),
            pl.BlockSpec((2, edge_group, edge, channels), lambda a: (0, a, 0, 0)),
            pl.BlockSpec(memory_space=pl.ANY),
        ],
        out_specs=pl.BlockSpec((2, edge_group, edge, 2 * channels), lambda a: (0, a, 0, 0)),
        out_shape=out_shape,
        input_output_aliases={3: 0},
        cost_estimate=pl.CostEstimate(
            flops=4 * tap_count * edge * frames.size // spectra,
            transcendentals=0,
            bytes_accessed=8 * edge * frames.size // spectra,
        ),
    )(fir_taps, earlier, frames, whole)


def correlate_kernel(rows_ref, cols_ref, *refs):
    out_ref = refs[-1]
    row_count = out_ref.shape[2]
    for index in range(out_ref.shape[1]):
        left = rows_ref[index]
        right = cols_ref[index]
        product = jnp.dot(left, right, preferred_element_type=jnp.float32)
        right = right.astype(jnp.float32)
        rows = left[0:row_count].astype(jnp.float32)
        column_power = jnp.sum(right * right, axis=0, keepdims=True)
        row_power = jnp.sum(rows * rows, axis=1, keepdims=True)
        scale_row = lax.rsqrt(row_power + epsilon)
        scale_column = lax.rsqrt(column_power + epsilon)
        out_ref[0, index] = (product[0:row_count] * scale_row * scale_column).astype(out_ref.dtype)
        out_ref[1, index] = (product[row_count:] * scale_row * scale_column).astype(out_ref.dtype)


def correlate_chunk(left, right, previous, offset, local_channels):
    width, double_rows, depth = left.shape
    row_count = double_rows // 2
    stations = right.shape[2]
    step = 4 if width % 4 == 0 and offset % 4 == 0 else 1
    in_specs = [
        pl.BlockSpec((step, double_rows, depth), lambda k: (k, 0, 0)),
        pl.BlockSpec((step, depth, stations), lambda k: (k, 0, 0)),
    ]
    operands = [left, right]
    aliases = {}
    if previous is not None:
        in_specs.append(pl.BlockSpec(memory_space=pl.ANY))
        operands.append(previous)
        aliases = {2: 0}
    return pl.pallas_call(
        correlate_kernel,
        grid=(width // step,),
        in_specs=in_specs,
        out_specs=pl.BlockSpec(
            (2, step, row_count, stations), lambda k: (0, offset // step + k, 0, 0)
        ),
        out_shape=jax.ShapeDtypeStruct((2, local_channels, row_count, stations), jnp.bfloat16),
        input_output_aliases=aliases,
        cost_estimate=pl.CostEstimate(
            flops=2 * width * double_rows * depth * stations,
            transcendentals=width * (row_count + stations),
            bytes_accessed=2 * (left.size + right.size + width * double_rows * stations),
        ),
    )(*operands)


def correlate_rows_kernel(block_ref, rows_ref, cols_ref, *refs):
    out_ref = refs[-1]
    half = cols_ref.shape[1] // 2
    contract_first = (((0,), (0,)), ((), ()))
    for index in range(out_ref.shape[1]):
        rows = rows_ref[index]
        right = cols_ref[index]
        swapped = jnp.concatenate([rows[half:], -rows[:half]], axis=0)
        real_vis = lax.dot_general(rows, right, contract_first, preferred_element_type=jnp.float32)
        imag_vis = lax.dot_general(swapped, right, contract_first, preferred_element_type=jnp.float32)
        right = right.astype(jnp.float32)
        rows = rows.astype(jnp.float32)
        column_power = jnp.sum(right * right, axis=0, keepdims=True)
        row_power = jnp.sum(jnp.transpose(rows * rows), axis=1, keepdims=True)
        scale_row = lax.rsqrt(row_power + epsilon)
        scale_column = lax.rsqrt(column_power + epsilon)
        out_ref[0, index] = (real_vis * scale_row * scale_column).astype(out_ref.dtype)
        out_ref[1, index] = (imag_vis * scale_row * scale_column).astype(out_ref.dtype)


def correlate_rows_chunk(right, block, row_count, previous, offset, local_channels):
    width, depth, stations = right.shape
    step = 4 if width % 4 == 0 and offset % 4 == 0 else 1
    in_specs = [
        pl.BlockSpec((step, depth, row_count), lambda k, b: (k, 0, b[0])),
        pl.BlockSpec((step, depth, stations), lambda k, b: (k, 0, 0)),
    ]
    operands = [block, right, right]
    aliases = {}
    if previous is not None:
        in_specs.append(pl.BlockSpec(memory_space=pl.ANY))
        operands.append(previous)
        aliases = {3: 0}
    grid_spec = pltpu.PrefetchScalarGridSpec(
        num_scalar_prefetch=1,
        grid=(width // step,),
        in_specs=in_specs,
        out_specs=pl.BlockSpec(
            (2, step, row_count, stations), lambda k, b: (0, offset // step + k, 0, 0)
        ),
    )
    return pl.pallas_call(
        correlate_rows_kernel,
        grid_spec=grid_spec,
        out_shape=jax.ShapeDtypeStruct((2, local_channels, row_count, stations), jnp.bfloat16),
        input_output_aliases=aliases,
        cost_estimate=pl.CostEstimate(
            flops=4 * width * row_count * depth * stations,
            transcendentals=width * (row_count + stations),
            bytes_accessed=2 * (right.size + width * depth * row_count + 2 * width * row_count * stations),
        ),
    )(*operands)


def per_device(samples, fir_taps, station_order):
    tap_count = fir_taps.shape[0]
    channels = fir_taps.shape[1]
    stations_local = samples.shape[1]
    spectra_local = samples.shape[2] // channels
    stations = station_order.shape[0]
    groups = lax.axis_size("stn")
    blocks = lax.axis_size("blk")
    local_channels = channels // groups
    row_count = stations // blocks
    chunks = chunk_count(local_channels)
    width = local_channels // chunks

    earlier = samples[:, :, (spectra_local - (tap_count - 1)) * channels :].astype(jnp.bfloat16)
    earlier = earlier.reshape(2, stations_local, tap_count - 1, channels)
    frames = samples.astype(jnp.bfloat16).reshape(2, stations_local, spectra_local, channels)
    earlier = passed_along(earlier, "blk", 1)
    filtered = filter_frames(fir_taps, earlier, frames)
    filtered = filtered.reshape(2 * stations_local * spectra_local, 2 * channels)

    weights = dft_weights(channels, groups, chunks)
    selector = (
        station_order[None, :] == jnp.arange(stations, dtype=jnp.int32)[:, None]
    ).astype(jnp.bfloat16)
    selector = selector.reshape(groups, stations_local, stations)
    row_start = lax.axis_index("blk") * row_count

    block_index = jnp.reshape(lax.axis_index("blk"), (1,)).astype(jnp.int32)

    def correlate(chunk, gathered, result):
        if row_count % 128 == 0:
            right = gathered.reshape(width, -1, stations)
            return correlate_rows_chunk(
                right, block_index, row_count, result, chunk * width, local_channels
            )
        gathered = gathered.reshape(width, 2, -1, stations)
        row_block = lax.dynamic_slice_in_dim(gathered, row_start, row_count, 3)
        direct = jnp.transpose(row_block, (0, 3, 1, 2))
        swapped = jnp.stack([direct[:, :, 1], -direct[:, :, 0]], axis=2)
        left = jnp.concatenate([direct, swapped], axis=1).reshape(width, 2 * row_count, -1)
        right = gathered.reshape(width, -1, stations)
        return correlate_chunk(left, right, result, chunk * width, local_channels)

    def reorder(turned):
        turned = turned.reshape(groups, width, 2, stations_local, spectra_local)
        ordered = jnp.einsum(
            "gkias,gar->kisr", turned, selector, preferred_element_type=jnp.float32
        ).astype(jnp.bfloat16)
        return ordered.reshape(width * 2, spectra_local, stations)

    result = None
    pending = []
    finished = 0
    turned = None
    for chunk in range(chunks):
        source = filtered
        if chunk >= 3:
            result = correlate(finished, pending[finished], result)
            finished += 1
            source, result = lax.optimization_barrier((filtered, result))
        spectra = jnp.einsum(
            "kj,nj->kn", weights[chunk], source, preferred_element_type=jnp.float32
        ).astype(jnp.bfloat16)
        spectra = spectra.reshape(groups, width, 2 * stations_local * spectra_local)
        if chunk >= 1:
            turned, spectra = lax.optimization_barrier((turned, spectra))
            pending.append(gathered_along(reorder(turned), "blk", 1))
        turned = lax.all_to_all(spectra, "stn", split_axis=0, concat_axis=0, tiled=True)
    if finished + 3 <= chunks:
        result = correlate(finished, pending[finished], result)
        finished += 1
        turned, result = lax.optimization_barrier((turned, result))
    pending.append(gathered_along(reorder(turned), "blk", 1))
    for chunk in range(finished, chunks):
        result = correlate(chunk, pending[chunk], result)
    return result


def solution(mesh):
    placed = (P(None, "stn", "blk"), P(), P())
    return jax.shard_map(
        per_device,
        mesh=mesh,
        in_specs=placed,
        out_specs=P(None, "stn", "blk", None),
        check_vma=False,
    )
```

```python
import math

import jax
import ml_dtypes
import numpy as np
import jax.numpy as jnp
from jax import lax
from jax.experimental import pallas as pl
from jax.experimental.pallas import tpu as pltpu
from jax.sharding import PartitionSpec as P

epsilon = 1e-06


def passed_along(value, axis, steps):
    count = lax.axis_size(axis)
    initial, last = (max(0, -steps), min(count, count - steps))
    return lax.ppermute(value, axis, [(source, source + steps) for source in range(initial, last)])


def gathered_along(value, axis, dimension):
    count = lax.axis_size(axis)
    parts = [value]
    for shift in range(1, count):
        pairs = [(source, (source + shift) % count) for source in range(count)]
        parts.append(lax.ppermute(value, axis, pairs))
    return jnp.concatenate(parts, axis=dimension)


def chunk_count(local_channels):
    for count in (4, 2):
        if local_channels % count == 0:
            return count
    return 1


def dft_weights(channels, groups, chunks):
    local = channels // groups
    width = local // chunks
    chunk = np.arange(chunks).reshape(chunks, 1, 1, 1)
    group = np.arange(groups).reshape(1, groups, 1, 1)
    inner = np.arange(width).reshape(1, 1, width, 1)
    column = np.arange(channels).reshape(1, 1, 1, channels)
    row = group * local + chunk * width + inner
    phase_index = (row * column % channels).astype(np.float32)
    angle = phase_index * np.float32(2.0 * math.pi / channels)
    cosine = np.cos(angle).astype(ml_dtypes.bfloat16)
    sine = np.sin(angle).astype(ml_dtypes.bfloat16)
    table = np.concatenate([cosine, sine], axis=3)
    return jnp.asarray(table.reshape(chunks, groups * width, 2 * channels))


def fir_rows(taps_ref, extended, count):
    total = taps_ref[0:1, :] * extended[0:count]
    for tap_index in range(1, taps_ref.shape[0]):
        total = total + taps_ref[tap_index : tap_index + 1, :] * extended[tap_index : tap_index + count]
    return total.astype(jnp.bfloat16)


def fir_store(out_ref, station, filtered, channels):
    out_ref[0, station, :, 0:channels] = filtered[0]
    out_ref[0, station, :, channels:] = filtered[1]
    out_ref[1, station, :, 0:channels] = filtered[1]
    out_ref[1, station, :, channels:] = -filtered[0]


def fir_kernel(taps_ref, frames_ref, out_ref, scratch_ref):
    tap_count = taps_ref.shape[0]
    spectra = frames_ref.shape[2]
    channels = frames_ref.shape[3]
    edge = 8
    count = spectra - edge
    start = edge - (tap_count - 1)

    def body(station, carry):
        filtered = []
        for part in range(2):
            scratch_ref[...] = frames_ref[part, station].astype(jnp.float32)
            total = taps_ref[0:1, :] * scratch_ref[pl.ds(start, count), :]
            for tap_index in range(1, tap_count):
                total = total + taps_ref[tap_index : tap_index + 1, :] * scratch_ref[
                    pl.ds(start + tap_index, count), :
                ]
            filtered.append(total.astype(jnp.bfloat16))
        out_ref[0, station, edge:, 0:channels] = filtered[0]
        out_ref[0, station, edge:, channels:] = filtered[1]
        out_ref[1, station, edge:, 0:channels] = filtered[1]
        out_ref[1, station, edge:, channels:] = -filtered[0]
        return carry

    lax.fori_loop(0, frames_ref.shape[1], body, 0)


def fir_edge_kernel(taps_ref, halo_ref, frames_ref, previous_ref, out_ref):
    count = frames_ref.shape[2]
    channels = frames_ref.shape[3]

    def body(station, carry):
        filtered = []
        for part in range(2):
            extended = jnp.concatenate(
                [
                    halo_ref[part, station].astype(jnp.float32),
                    frames_ref[part, station].astype(jnp.float32),
                ],
                axis=0,
            )
            filtered.append(fir_rows(taps_ref, extended, count))
        fir_store(out_ref, station, filtered, channels)
        return carry

    lax.fori_loop(0, frames_ref.shape[1], body, 0)


def filter_frames(fir_taps, earlier, frames):
    tap_count, channels = fir_taps.shape
    _, stations_local, spectra, _ = frames.shape
    out_shape = jax.ShapeDtypeStruct((2, stations_local, spectra, 2 * channels), jnp.bfloat16)
    group = 4 if stations_local % 4 == 0 else 1
    whole = pl.pallas_call(
        fir_kernel,
        grid=(stations_local // group,),
        in_specs=[
            pl.BlockSpec((tap_count, channels), lambda a: (0, 0)),
            pl.BlockSpec((2, group, spectra, channels), lambda a: (0, a, 0, 0)),
        ],
        out_specs=pl.BlockSpec((2, group, spectra, 2 * channels), lambda a: (0, a, 0, 0)),
        out_shape=out_shape,
        scratch_shapes=[pltpu.VMEM((spectra, channels), jnp.float32)],
        cost_estimate=pl.CostEstimate(
            flops=4 * tap_count * frames.size,
            transcendentals=0,
            bytes_accessed=2 * frames.size + 4 * frames.size,
        ),
    )(fir_taps, frames)
    edge = 8
    edge_group = stations_local // 4 if stations_local % 4 == 0 else stations_local
    return pl.pallas_call(
        fir_edge_kernel,
        grid=(stations_local // edge_group,),
        in_specs=[
            pl.BlockSpec((tap_count, channels), lambda a: (0, 0)),
            pl.BlockSpec((2, edge_group, tap_count - 1, channels), lambda a: (0, a, 0, 0)),
            pl.BlockSpec((2, edge_group, edge, channels), lambda a: (0, a, 0, 0)),
            pl.BlockSpec(memory_space=pl.ANY),
        ],
        out_specs=pl.BlockSpec((2, edge_group, edge, 2 * channels), lambda a: (0, a, 0, 0)),
        out_shape=out_shape,
        input_output_aliases={3: 0},
        cost_estimate=pl.CostEstimate(
            flops=4 * tap_count * edge * frames.size // spectra,
            transcendentals=0,
            bytes_accessed=8 * edge * frames.size // spectra,
        ),
    )(fir_taps, earlier, frames, whole)


def correlate_kernel(rows_ref, cols_ref, *refs):
    out_ref = refs[-1]
    row_count = out_ref.shape[2]
    for index in range(out_ref.shape[1]):
        left = rows_ref[index]
        right = cols_ref[index]
        product = jnp.dot(left, right, preferred_element_type=jnp.float32)
        right = right.astype(jnp.float32)
        rows = left[0:row_count].astype(jnp.float32)
        column_power = jnp.sum(right * right, axis=0, keepdims=True)
        row_power = jnp.sum(rows * rows, axis=1, keepdims=True)
        scale_row = lax.rsqrt(row_power + epsilon)
        scale_column = lax.rsqrt(column_power + epsilon)
        out_ref[0, index] = (product[0:row_count] * scale_row * scale_column).astype(out_ref.dtype)
        out_ref[1, index] = (product[row_count:] * scale_row * scale_column).astype(out_ref.dtype)


def correlate_chunk(left, right, previous, offset, local_channels):
    width, double_rows, depth = left.shape
    row_count = double_rows // 2
    stations = right.shape[2]
    step = 4 if width % 4 == 0 and offset % 4 == 0 else 1
    in_specs = [
        pl.BlockSpec((step, double_rows, depth), lambda k: (k, 0, 0)),
        pl.BlockSpec((step, depth, stations), lambda k: (k, 0, 0)),
    ]
    operands = [left, right]
    aliases = {}
    if previous is not None:
        in_specs.append(pl.BlockSpec(memory_space=pl.ANY))
        operands.append(previous)
        aliases = {2: 0}
    return pl.pallas_call(
        correlate_kernel,
        grid=(width // step,),
        in_specs=in_specs,
        out_specs=pl.BlockSpec(
            (2, step, row_count, stations), lambda k: (0, offset // step + k, 0, 0)
        ),
        out_shape=jax.ShapeDtypeStruct((2, local_channels, row_count, stations), jnp.bfloat16),
        input_output_aliases=aliases,
        cost_estimate=pl.CostEstimate(
            flops=2 * width * double_rows * depth * stations,
            transcendentals=width * (row_count + stations),
            bytes_accessed=2 * (left.size + right.size + width * double_rows * stations),
        ),
    )(*operands)


def correlate_rows_kernel(block_ref, rows_ref, cols_ref, *refs):
    out_ref = refs[-1]
    half = cols_ref.shape[1] // 2
    contract_first = (((0,), (0,)), ((), ()))
    for index in range(out_ref.shape[1]):
        rows = rows_ref[index]
        right = cols_ref[index]
        swapped = jnp.concatenate([rows[half:], -rows[:half]], axis=0)
        real_vis = lax.dot_general(rows, right, contract_first, preferred_element_type=jnp.float32)
        imag_vis = lax.dot_general(swapped, right, contract_first, preferred_element_type=jnp.float32)
        right = right.astype(jnp.float32)
        rows = rows.astype(jnp.float32)
        column_power = jnp.sum(right * right, axis=0, keepdims=True)
        row_power = jnp.sum(jnp.transpose(rows * rows), axis=1, keepdims=True)
        scale_row = lax.rsqrt(row_power + epsilon)
        scale_column = lax.rsqrt(column_power + epsilon)
        out_ref[0, index] = (real_vis * scale_row * scale_column).astype(out_ref.dtype)
        out_ref[1, index] = (imag_vis * scale_row * scale_column).astype(out_ref.dtype)


def correlate_rows_chunk(right, block, row_count, previous, offset, local_channels):
    width, depth, stations = right.shape
    step = 4 if width % 4 == 0 and offset % 4 == 0 else 1
    in_specs = [
        pl.BlockSpec((step, depth, row_count), lambda k, b: (k, 0, b[0])),
        pl.BlockSpec((step, depth, stations), lambda k, b: (k, 0, 0)),
    ]
    operands = [block, right, right]
    aliases = {}
    if previous is not None:
        in_specs.append(pl.BlockSpec(memory_space=pl.ANY))
        operands.append(previous)
        aliases = {3: 0}
    grid_spec = pltpu.PrefetchScalarGridSpec(
        num_scalar_prefetch=1,
        grid=(width // step,),
        in_specs=in_specs,
        out_specs=pl.BlockSpec(
            (2, step, row_count, stations), lambda k, b: (0, offset // step + k, 0, 0)
        ),
    )
    return pl.pallas_call(
        correlate_rows_kernel,
        grid_spec=grid_spec,
        out_shape=jax.ShapeDtypeStruct((2, local_channels, row_count, stations), jnp.bfloat16),
        input_output_aliases=aliases,
        cost_estimate=pl.CostEstimate(
            flops=4 * width * row_count * depth * stations,
            transcendentals=width * (row_count + stations),
            bytes_accessed=2 * (right.size + width * depth * row_count + 2 * width * row_count * stations),
        ),
    )(*operands)


def per_device(samples, fir_taps, station_order):
    tap_count = fir_taps.shape[0]
    channels = fir_taps.shape[1]
    stations_local = samples.shape[1]
    spectra_local = samples.shape[2] // channels
    stations = station_order.shape[0]
    groups = lax.axis_size("stn")
    blocks = lax.axis_size("blk")
    local_channels = channels // groups
    row_count = stations // blocks
    chunks = chunk_count(local_channels)
    width = local_channels // chunks

    earlier = samples[:, :, (spectra_local - (tap_count - 1)) * channels :].astype(jnp.bfloat16)
    earlier = earlier.reshape(2, stations_local, tap_count - 1, channels)
    frames = samples.astype(jnp.bfloat16).reshape(2, stations_local, spectra_local, channels)
    earlier = passed_along(earlier, "blk", 1)
    filtered = filter_frames(fir_taps, earlier, frames)
    filtered = filtered.reshape(2 * stations_local * spectra_local, 2 * channels)

    weights = dft_weights(channels, groups, chunks)
    selector = (
        station_order[None, :] == jnp.arange(stations, dtype=jnp.int32)[:, None]
    ).astype(jnp.bfloat16)
    selector = selector.reshape(groups, stations_local, stations)
    row_start = lax.axis_index("blk") * row_count

    block_index = jnp.reshape(lax.axis_index("blk"), (1,)).astype(jnp.int32)

    def correlate(chunk, gathered, result):
        if row_count % 128 == 0:
            right = gathered.reshape(width, -1, stations)
            return correlate_rows_chunk(
                right, block_index, row_count, result, chunk * width, local_channels
            )
        gathered = gathered.reshape(width, 2, -1, stations)
        row_block = lax.dynamic_slice_in_dim(gathered, row_start, row_count, 3)
        direct = jnp.transpose(row_block, (0, 3, 1, 2))
        swapped = jnp.stack([direct[:, :, 1], -direct[:, :, 0]], axis=2)
        left = jnp.concatenate([direct, swapped], axis=1).reshape(width, 2 * row_count, -1)
        right = gathered.reshape(width, -1, stations)
        return correlate_chunk(left, right, result, chunk * width, local_channels)

    result = None
    pending = []
    for chunk in range(chunks):
        source = filtered
        if chunk >= 2:
            result = correlate(chunk - 2, pending[chunk - 2], result)
            source, result = lax.optimization_barrier((filtered, result))
        spectra = jnp.einsum(
            "kj,nj->kn", weights[chunk], source, preferred_element_type=jnp.float32
        ).astype(jnp.bfloat16)
        spectra = spectra.reshape(groups, width, 2 * stations_local * spectra_local)
        turned = lax.all_to_all(spectra, "stn", split_axis=0, concat_axis=0, tiled=True)
        turned = turned.reshape(groups, width, 2, stations_local, spectra_local)
        ordered = jnp.einsum(
            "gkias,gar->kisr", turned, selector, preferred_element_type=jnp.float32
        ).astype(jnp.bfloat16)
        ordered = ordered.reshape(width * 2, spectra_local, stations)
        pending.append(gathered_along(ordered, "blk", 1))
    for chunk in range(max(0, chunks - 2), chunks):
        result = correlate(chunk, pending[chunk], result)
    return result


def solution(mesh):
    placed = (P(None, "stn", "blk"), P(), P())
    return jax.shard_map(
        per_device,
        mesh=mesh,
        in_specs=placed,
        out_specs=P(None, "stn", "blk", None),
        check_vma=False,
    )
```

```python
import math

import jax
import ml_dtypes
import numpy as np
import jax.numpy as jnp
from jax import lax
from jax.experimental import pallas as pl
from jax.experimental.pallas import tpu as pltpu
from jax.sharding import PartitionSpec as P

epsilon = 1e-06


def passed_along(value, axis, steps):
    count = lax.axis_size(axis)
    initial, last = (max(0, -steps), min(count, count - steps))
    return lax.ppermute(value, axis, [(source, source + steps) for source in range(initial, last)])


def gathered_along(value, axis, dimension):
    count = lax.axis_size(axis)
    parts = [value]
    for shift in range(1, count):
        pairs = [(source, (source + shift) % count) for source in range(count)]
        parts.append(lax.ppermute(value, axis, pairs))
    return jnp.concatenate(parts, axis=dimension)


def chunk_count(local_channels):
    for count in (8, 4, 2):
        if local_channels % count == 0:
            return count
    return 1


def dft_weights(channels, groups, chunks):
    local = channels // groups
    width = local // chunks
    chunk = np.arange(chunks).reshape(chunks, 1, 1, 1)
    group = np.arange(groups).reshape(1, groups, 1, 1)
    inner = np.arange(width).reshape(1, 1, width, 1)
    column = np.arange(channels).reshape(1, 1, 1, channels)
    row = group * local + chunk * width + inner
    phase_index = (row * column % channels).astype(np.float32)
    angle = phase_index * np.float32(2.0 * math.pi / channels)
    cosine = np.cos(angle).astype(ml_dtypes.bfloat16)
    sine = np.sin(angle).astype(ml_dtypes.bfloat16)
    table = np.concatenate([cosine, sine], axis=3)
    return jnp.asarray(table.reshape(chunks, groups * width, 2 * channels))


def fir_rows(taps_ref, extended, count):
    total = taps_ref[0:1, :] * extended[0:count]
    for tap_index in range(1, taps_ref.shape[0]):
        total = total + taps_ref[tap_index : tap_index + 1, :] * extended[tap_index : tap_index + count]
    return total.astype(jnp.bfloat16)


def fir_store(out_ref, station, filtered, channels):
    out_ref[0, station, :, 0:channels] = filtered[0]
    out_ref[0, station, :, channels:] = filtered[1]
    out_ref[1, station, :, 0:channels] = filtered[1]
    out_ref[1, station, :, channels:] = -filtered[0]


def fir_kernel(taps_ref, frames_ref, out_ref, scratch_ref):
    tap_count = taps_ref.shape[0]
    spectra = frames_ref.shape[2]
    channels = frames_ref.shape[3]
    edge = 8
    count = spectra - edge
    start = edge - (tap_count - 1)

    def body(station, carry):
        filtered = []
        for part in range(2):
            scratch_ref[...] = frames_ref[part, station].astype(jnp.float32)
            total = taps_ref[0:1, :] * scratch_ref[pl.ds(start, count), :]
            for tap_index in range(1, tap_count):
                total = total + taps_ref[tap_index : tap_index + 1, :] * scratch_ref[
                    pl.ds(start + tap_index, count), :
                ]
            filtered.append(total.astype(jnp.bfloat16))
        out_ref[0, station, edge:, 0:channels] = filtered[0]
        out_ref[0, station, edge:, channels:] = filtered[1]
        out_ref[1, station, edge:, 0:channels] = filtered[1]
        out_ref[1, station, edge:, channels:] = -filtered[0]
        return carry

    lax.fori_loop(0, frames_ref.shape[1], body, 0)


def fir_edge_kernel(taps_ref, halo_ref, frames_ref, previous_ref, out_ref):
    count = frames_ref.shape[2]
    channels = frames_ref.shape[3]

    def body(station, carry):
        filtered = []
        for part in range(2):
            extended = jnp.concatenate(
                [
                    halo_ref[part, station].astype(jnp.float32),
                    frames_ref[part, station].astype(jnp.float32),
                ],
                axis=0,
            )
            filtered.append(fir_rows(taps_ref, extended, count))
        fir_store(out_ref, station, filtered, channels)
        return carry

    lax.fori_loop(0, frames_ref.shape[1], body, 0)


def filter_frames(fir_taps, earlier, frames):
    tap_count, channels = fir_taps.shape
    _, stations_local, spectra, _ = frames.shape
    out_shape = jax.ShapeDtypeStruct((2, stations_local, spectra, 2 * channels), jnp.bfloat16)
    group = 4 if stations_local % 4 == 0 else 1
    whole = pl.pallas_call(
        fir_kernel,
        grid=(stations_local // group,),
        in_specs=[
            pl.BlockSpec((tap_count, channels), lambda a: (0, 0)),
            pl.BlockSpec((2, group, spectra, channels), lambda a: (0, a, 0, 0)),
        ],
        out_specs=pl.BlockSpec((2, group, spectra, 2 * channels), lambda a: (0, a, 0, 0)),
        out_shape=out_shape,
        scratch_shapes=[pltpu.VMEM((spectra, channels), jnp.float32)],
        cost_estimate=pl.CostEstimate(
            flops=4 * tap_count * frames.size,
            transcendentals=0,
            bytes_accessed=2 * frames.size + 4 * frames.size,
        ),
    )(fir_taps, frames)
    edge = 8
    edge_group = stations_local // 4 if stations_local % 4 == 0 else stations_local
    return pl.pallas_call(
        fir_edge_kernel,
        grid=(stations_local // edge_group,),
        in_specs=[
            pl.BlockSpec((tap_count, channels), lambda a: (0, 0)),
            pl.BlockSpec((2, edge_group, tap_count - 1, channels), lambda a: (0, a, 0, 0)),
            pl.BlockSpec((2, edge_group, edge, channels), lambda a: (0, a, 0, 0)),
            pl.BlockSpec(memory_space=pl.ANY),
        ],
        out_specs=pl.BlockSpec((2, edge_group, edge, 2 * channels), lambda a: (0, a, 0, 0)),
        out_shape=out_shape,
        input_output_aliases={3: 0},
        cost_estimate=pl.CostEstimate(
            flops=4 * tap_count * edge * frames.size // spectra,
            transcendentals=0,
            bytes_accessed=8 * edge * frames.size // spectra,
        ),
    )(fir_taps, earlier, frames, whole)


def correlate_kernel(rows_ref, cols_ref, *refs):
    out_ref = refs[-1]
    row_count = out_ref.shape[2]
    for index in range(out_ref.shape[1]):
        left = rows_ref[index]
        right = cols_ref[index]
        product = jnp.dot(left, right, preferred_element_type=jnp.float32)
        right = right.astype(jnp.float32)
        rows = left[0:row_count].astype(jnp.float32)
        column_power = jnp.sum(right * right, axis=0, keepdims=True)
        row_power = jnp.sum(rows * rows, axis=1, keepdims=True)
        scale_row = lax.rsqrt(row_power + epsilon)
        scale_column = lax.rsqrt(column_power + epsilon)
        out_ref[0, index] = (product[0:row_count] * scale_row * scale_column).astype(out_ref.dtype)
        out_ref[1, index] = (product[row_count:] * scale_row * scale_column).astype(out_ref.dtype)


def correlate_chunk(left, right, previous, offset, local_channels):
    width, double_rows, depth = left.shape
    row_count = double_rows // 2
    stations = right.shape[2]
    step = 4 if width % 4 == 0 and offset % 4 == 0 else 1
    in_specs = [
        pl.BlockSpec((step, double_rows, depth), lambda k: (k, 0, 0)),
        pl.BlockSpec((step, depth, stations), lambda k: (k, 0, 0)),
    ]
    operands = [left, right]
    aliases = {}
    if previous is not None:
        in_specs.append(pl.BlockSpec(memory_space=pl.ANY))
        operands.append(previous)
        aliases = {2: 0}
    return pl.pallas_call(
        correlate_kernel,
        grid=(width // step,),
        in_specs=in_specs,
        out_specs=pl.BlockSpec(
            (2, step, row_count, stations), lambda k: (0, offset // step + k, 0, 0)
        ),
        out_shape=jax.ShapeDtypeStruct((2, local_channels, row_count, stations), jnp.bfloat16),
        input_output_aliases=aliases,
        cost_estimate=pl.CostEstimate(
            flops=2 * width * double_rows * depth * stations,
            transcendentals=width * (row_count + stations),
            bytes_accessed=2 * (left.size + right.size + width * double_rows * stations),
        ),
    )(*operands)


def correlate_rows_kernel(block_ref, rows_ref, cols_ref, *refs):
    out_ref = refs[-1]
    half = cols_ref.shape[1] // 2
    contract_first = (((0,), (0,)), ((), ()))
    for index in range(out_ref.shape[1]):
        rows = rows_ref[index]
        right = cols_ref[index]
        swapped = jnp.concatenate([rows[half:], -rows[:half]], axis=0)
        real_vis = lax.dot_general(rows, right, contract_first, preferred_element_type=jnp.float32)
        imag_vis = lax.dot_general(swapped, right, contract_first, preferred_element_type=jnp.float32)
        right = right.astype(jnp.float32)
        rows = rows.astype(jnp.float32)
        column_power = jnp.sum(right * right, axis=0, keepdims=True)
        row_power = jnp.sum(jnp.transpose(rows * rows), axis=1, keepdims=True)
        scale_row = lax.rsqrt(row_power + epsilon)
        scale_column = lax.rsqrt(column_power + epsilon)
        out_ref[0, index] = (real_vis * scale_row * scale_column).astype(out_ref.dtype)
        out_ref[1, index] = (imag_vis * scale_row * scale_column).astype(out_ref.dtype)


def correlate_rows_chunk(right, block, row_count, previous, offset, local_channels):
    width, depth, stations = right.shape
    step = 4 if width % 4 == 0 and offset % 4 == 0 else 1
    in_specs = [
        pl.BlockSpec((step, depth, row_count), lambda k, b: (k, 0, b[0])),
        pl.BlockSpec((step, depth, stations), lambda k, b: (k, 0, 0)),
    ]
    operands = [block, right, right]
    aliases = {}
    if previous is not None:
        in_specs.append(pl.BlockSpec(memory_space=pl.ANY))
        operands.append(previous)
        aliases = {3: 0}
    grid_spec = pltpu.PrefetchScalarGridSpec(
        num_scalar_prefetch=1,
        grid=(width // step,),
        in_specs=in_specs,
        out_specs=pl.BlockSpec(
            (2, step, row_count, stations), lambda k, b: (0, offset // step + k, 0, 0)
        ),
    )
    return pl.pallas_call(
        correlate_rows_kernel,
        grid_spec=grid_spec,
        out_shape=jax.ShapeDtypeStruct((2, local_channels, row_count, stations), jnp.bfloat16),
        input_output_aliases=aliases,
        cost_estimate=pl.CostEstimate(
            flops=4 * width * row_count * depth * stations,
            transcendentals=width * (row_count + stations),
            bytes_accessed=2 * (right.size + width * depth * row_count + 2 * width * row_count * stations),
        ),
    )(*operands)


def per_device(samples, fir_taps, station_order):
    tap_count = fir_taps.shape[0]
    channels = fir_taps.shape[1]
    stations_local = samples.shape[1]
    spectra_local = samples.shape[2] // channels
    stations = station_order.shape[0]
    groups = lax.axis_size("stn")
    blocks = lax.axis_size("blk")
    local_channels = channels // groups
    row_count = stations // blocks
    chunks = chunk_count(local_channels)
    width = local_channels // chunks

    earlier = samples[:, :, (spectra_local - (tap_count - 1)) * channels :].astype(jnp.bfloat16)
    earlier = earlier.reshape(2, stations_local, tap_count - 1, channels)
    frames = samples.astype(jnp.bfloat16).reshape(2, stations_local, spectra_local, channels)
    earlier = passed_along(earlier, "blk", 1)
    filtered = filter_frames(fir_taps, earlier, frames)
    filtered = filtered.reshape(2 * stations_local * spectra_local, 2 * channels)

    weights = dft_weights(channels, groups, chunks)
    selector = (
        station_order[None, :] == jnp.arange(stations, dtype=jnp.int32)[:, None]
    ).astype(jnp.bfloat16)
    selector = selector.reshape(groups, stations_local, stations)
    row_start = lax.axis_index("blk") * row_count

    block_index = jnp.reshape(lax.axis_index("blk"), (1,)).astype(jnp.int32)

    def correlate(chunk, gathered, result):
        if row_count % 128 == 0:
            right = gathered.reshape(width, -1, stations)
            return correlate_rows_chunk(
                right, block_index, row_count, result, chunk * width, local_channels
            )
        gathered = gathered.reshape(width, 2, -1, stations)
        row_block = lax.dynamic_slice_in_dim(gathered, row_start, row_count, 3)
        direct = jnp.transpose(row_block, (0, 3, 1, 2))
        swapped = jnp.stack([direct[:, :, 1], -direct[:, :, 0]], axis=2)
        left = jnp.concatenate([direct, swapped], axis=1).reshape(width, 2 * row_count, -1)
        right = gathered.reshape(width, -1, stations)
        return correlate_chunk(left, right, result, chunk * width, local_channels)

    result = None
    pending = []
    for chunk in range(chunks):
        source = filtered
        if chunk >= 2:
            result = correlate(chunk - 2, pending[chunk - 2], result)
            source, result = lax.optimization_barrier((filtered, result))
        spectra = jnp.einsum(
            "kj,nj->kn", weights[chunk], source, preferred_element_type=jnp.float32
        ).astype(jnp.bfloat16)
        spectra = spectra.reshape(groups, width, 2 * stations_local * spectra_local)
        turned = lax.all_to_all(spectra, "stn", split_axis=0, concat_axis=0, tiled=True)
        turned = turned.reshape(groups, width, 2, stations_local, spectra_local)
        ordered = jnp.einsum(
            "gkias,gar->kisr", turned, selector, preferred_element_type=jnp.float32
        ).astype(jnp.bfloat16)
        ordered = ordered.reshape(width * 2, spectra_local, stations)
        pending.append(gathered_along(ordered, "blk", 1))
    for chunk in range(max(0, chunks - 2), chunks):
        result = correlate(chunk, pending[chunk], result)
    return result


def solution(mesh):
    placed = (P(None, "stn", "blk"), P(), P())
    return jax.shard_map(
        per_device,
        mesh=mesh,
        in_specs=placed,
        out_specs=P(None, "stn", "blk", None),
        check_vma=False,
    )
```

```python
import math

import jax
import ml_dtypes
import numpy as np
import jax.numpy as jnp
from jax import lax
from jax.experimental import pallas as pl
from jax.experimental.pallas import tpu as pltpu
from jax.sharding import PartitionSpec as P

epsilon = 1e-06


def passed_along(value, axis, steps):
    count = lax.axis_size(axis)
    initial, last = (max(0, -steps), min(count, count - steps))
    return lax.ppermute(value, axis, [(source, source + steps) for source in range(initial, last)])


def gathered_along(value, axis, dimension):
    count = lax.axis_size(axis)
    parts = [value]
    for shift in range(1, count):
        pairs = [(source, (source + shift) % count) for source in range(count)]
        parts.append(lax.ppermute(value, axis, pairs))
    return jnp.concatenate(parts, axis=dimension)


def chunk_count(local_channels):
    for count in (4, 2):
        if local_channels % count == 0:
            return count
    return 1


def dft_weights(channels, groups, chunks):
    local = channels // groups
    width = local // chunks
    chunk = np.arange(chunks).reshape(chunks, 1, 1, 1)
    group = np.arange(groups).reshape(1, groups, 1, 1)
    inner = np.arange(width).reshape(1, 1, width, 1)
    column = np.arange(channels).reshape(1, 1, 1, channels)
    row = group * local + chunk * width + inner
    phase_index = (row * column % channels).astype(np.float32)
    angle = phase_index * np.float32(2.0 * math.pi / channels)
    cosine = np.cos(angle).astype(ml_dtypes.bfloat16)
    sine = np.sin(angle).astype(ml_dtypes.bfloat16)
    table = np.concatenate([cosine, sine], axis=3)
    return jnp.asarray(table.reshape(chunks, groups * width, 2 * channels))


def fir_rows(taps_ref, extended, count):
    total = taps_ref[0:1, :] * extended[0:count]
    for tap_index in range(1, taps_ref.shape[0]):
        total = total + taps_ref[tap_index : tap_index + 1, :] * extended[tap_index : tap_index + count]
    return total.astype(jnp.bfloat16)


def fir_store(out_ref, station, filtered, channels):
    out_ref[station, :, 0:channels] = filtered[0]
    out_ref[station, :, channels:] = filtered[1]


def fir_kernel(taps_ref, frames_ref, out_ref, scratch_ref):
    tap_count = taps_ref.shape[0]
    spectra = frames_ref.shape[2]
    channels = frames_ref.shape[3]
    edge = 8
    count = spectra - edge
    start = edge - (tap_count - 1)

    def body(station, carry):
        filtered = []
        for part in range(2):
            scratch_ref[...] = frames_ref[part, station].astype(jnp.float32)
            total = taps_ref[0:1, :] * scratch_ref[pl.ds(start, count), :]
            for tap_index in range(1, tap_count):
                total = total + taps_ref[tap_index : tap_index + 1, :] * scratch_ref[
                    pl.ds(start + tap_index, count), :
                ]
            filtered.append(total.astype(jnp.bfloat16))
        out_ref[station, edge:, 0:channels] = filtered[0]
        out_ref[station, edge:, channels:] = filtered[1]
        return carry

    lax.fori_loop(0, frames_ref.shape[1], body, 0)


def fir_edge_kernel(taps_ref, halo_ref, frames_ref, previous_ref, out_ref):
    count = frames_ref.shape[2]
    channels = frames_ref.shape[3]

    def body(station, carry):
        filtered = []
        for part in range(2):
            extended = jnp.concatenate(
                [
                    halo_ref[part, station].astype(jnp.float32),
                    frames_ref[part, station].astype(jnp.float32),
                ],
                axis=0,
            )
            filtered.append(fir_rows(taps_ref, extended, count))
        fir_store(out_ref, station, filtered, channels)
        return carry

    lax.fori_loop(0, frames_ref.shape[1], body, 0)


def filter_frames(fir_taps, earlier, frames):
    tap_count, channels = fir_taps.shape
    _, stations_local, spectra, _ = frames.shape
    out_shape = jax.ShapeDtypeStruct((stations_local, spectra, 2 * channels), jnp.bfloat16)
    group = 4 if stations_local % 4 == 0 else 1
    whole = pl.pallas_call(
        fir_kernel,
        grid=(stations_local // group,),
        in_specs=[
            pl.BlockSpec((tap_count, channels), lambda a: (0, 0)),
            pl.BlockSpec((2, group, spectra, channels), lambda a: (0, a, 0, 0)),
        ],
        out_specs=pl.BlockSpec((group, spectra, 2 * channels), lambda a: (a, 0, 0)),
        out_shape=out_shape,
        scratch_shapes=[pltpu.VMEM((spectra, channels), jnp.float32)],
        cost_estimate=pl.CostEstimate(
            flops=4 * tap_count * frames.size,
            transcendentals=0,
            bytes_accessed=2 * frames.size + 2 * frames.size,
        ),
    )(fir_taps, frames)
    edge = 8
    edge_group = stations_local // 4 if stations_local % 4 == 0 else stations_local
    return pl.pallas_call(
        fir_edge_kernel,
        grid=(stations_local // edge_group,),
        in_specs=[
            pl.BlockSpec((tap_count, channels), lambda a: (0, 0)),
            pl.BlockSpec((2, edge_group, tap_count - 1, channels), lambda a: (0, a, 0, 0)),
            pl.BlockSpec((2, edge_group, edge, channels), lambda a: (0, a, 0, 0)),
            pl.BlockSpec(memory_space=pl.ANY),
        ],
        out_specs=pl.BlockSpec((edge_group, edge, 2 * channels), lambda a: (a, 0, 0)),
        out_shape=out_shape,
        input_output_aliases={3: 0},
        cost_estimate=pl.CostEstimate(
            flops=4 * tap_count * edge * frames.size // spectra,
            transcendentals=0,
            bytes_accessed=6 * edge * frames.size // spectra,
        ),
    )(fir_taps, earlier, frames, whole)


def correlate_kernel(rows_ref, cols_ref, *refs):
    out_ref = refs[-1]
    row_count = out_ref.shape[2]
    for index in range(out_ref.shape[1]):
        left = rows_ref[index]
        right = cols_ref[index]
        product = jnp.dot(left, right, preferred_element_type=jnp.float32)
        right = right.astype(jnp.float32)
        rows = left[0:row_count].astype(jnp.float32)
        column_power = jnp.sum(right * right, axis=0, keepdims=True)
        row_power = jnp.sum(rows * rows, axis=1, keepdims=True)
        scale_row = lax.rsqrt(row_power + epsilon)
        scale_column = lax.rsqrt(column_power + epsilon)
        out_ref[0, index] = (product[0:row_count] * scale_row * scale_column).astype(out_ref.dtype)
        out_ref[1, index] = (product[row_count:] * scale_row * scale_column).astype(out_ref.dtype)


def correlate_chunk(left, right, previous, offset, local_channels):
    width, double_rows, depth = left.shape
    row_count = double_rows // 2
    stations = right.shape[2]
    step = 4 if width % 4 == 0 and offset % 4 == 0 else 1
    in_specs = [
        pl.BlockSpec((step, double_rows, depth), lambda k: (k, 0, 0)),
        pl.BlockSpec((step, depth, stations), lambda k: (k, 0, 0)),
    ]
    operands = [left, right]
    aliases = {}
    if previous is not None:
        in_specs.append(pl.BlockSpec(memory_space=pl.ANY))
        operands.append(previous)
        aliases = {2: 0}
    return pl.pallas_call(
        correlate_kernel,
        grid=(width // step,),
        in_specs=in_specs,
        out_specs=pl.BlockSpec(
            (2, step, row_count, stations), lambda k: (0, offset // step + k, 0, 0)
        ),
        out_shape=jax.ShapeDtypeStruct((2, local_channels, row_count, stations), jnp.bfloat16),
        input_output_aliases=aliases,
        cost_estimate=pl.CostEstimate(
            flops=2 * width * double_rows * depth * stations,
            transcendentals=width * (row_count + stations),
            bytes_accessed=2 * (left.size + right.size + width * double_rows * stations),
        ),
    )(*operands)


def correlate_rows_kernel(block_ref, rows_ref, cols_ref, *refs):
    out_ref = refs[-1]
    half = cols_ref.shape[1] // 2
    contract_first = (((0,), (0,)), ((), ()))
    for index in range(out_ref.shape[1]):
        rows = rows_ref[index]
        right = cols_ref[index]
        swapped = jnp.concatenate([rows[half:], -rows[:half]], axis=0)
        real_vis = lax.dot_general(rows, right, contract_first, preferred_element_type=jnp.float32)
        imag_vis = lax.dot_general(swapped, right, contract_first, preferred_element_type=jnp.float32)
        right = right.astype(jnp.float32)
        rows = rows.astype(jnp.float32)
        column_power = jnp.sum(right * right, axis=0, keepdims=True)
        row_power = jnp.sum(jnp.transpose(rows * rows), axis=1, keepdims=True)
        scale_row = lax.rsqrt(row_power + epsilon)
        scale_column = lax.rsqrt(column_power + epsilon)
        out_ref[0, index] = (real_vis * scale_row * scale_column).astype(out_ref.dtype)
        out_ref[1, index] = (imag_vis * scale_row * scale_column).astype(out_ref.dtype)


def correlate_rows_chunk(right, block, row_count, previous, offset, local_channels):
    width, depth, stations = right.shape
    step = 4 if width % 4 == 0 and offset % 4 == 0 else 1
    in_specs = [
        pl.BlockSpec((step, depth, row_count), lambda k, b: (k, 0, b[0])),
        pl.BlockSpec((step, depth, stations), lambda k, b: (k, 0, 0)),
    ]
    operands = [block, right, right]
    aliases = {}
    if previous is not None:
        in_specs.append(pl.BlockSpec(memory_space=pl.ANY))
        operands.append(previous)
        aliases = {3: 0}
    grid_spec = pltpu.PrefetchScalarGridSpec(
        num_scalar_prefetch=1,
        grid=(width // step,),
        in_specs=in_specs,
        out_specs=pl.BlockSpec(
            (2, step, row_count, stations), lambda k, b: (0, offset // step + k, 0, 0)
        ),
    )
    return pl.pallas_call(
        correlate_rows_kernel,
        grid_spec=grid_spec,
        out_shape=jax.ShapeDtypeStruct((2, local_channels, row_count, stations), jnp.bfloat16),
        input_output_aliases=aliases,
        cost_estimate=pl.CostEstimate(
            flops=4 * width * row_count * depth * stations,
            transcendentals=width * (row_count + stations),
            bytes_accessed=2 * (right.size + width * depth * row_count + 2 * width * row_count * stations),
        ),
    )(*operands)


def per_device(samples, fir_taps, station_order):
    tap_count = fir_taps.shape[0]
    channels = fir_taps.shape[1]
    stations_local = samples.shape[1]
    spectra_local = samples.shape[2] // channels
    stations = station_order.shape[0]
    groups = lax.axis_size("stn")
    blocks = lax.axis_size("blk")
    local_channels = channels // groups
    row_count = stations // blocks
    chunks = chunk_count(local_channels)
    width = local_channels // chunks

    earlier = samples[:, :, (spectra_local - (tap_count - 1)) * channels :].astype(jnp.bfloat16)
    earlier = earlier.reshape(2, stations_local, tap_count - 1, channels)
    frames = samples.astype(jnp.bfloat16).reshape(2, stations_local, spectra_local, channels)
    earlier = passed_along(earlier, "blk", 1)
    filtered = filter_frames(fir_taps, earlier, frames)
    filtered = filtered.reshape(stations_local * spectra_local, 2 * channels)

    table = dft_weights(channels, groups, chunks).reshape(chunks, groups, 1, width, 2 * channels)
    table = lax.optimization_barrier(table)
    rotated = jnp.concatenate([-table[..., channels:], table[..., :channels]], axis=-1)
    weights = jnp.concatenate([table, rotated], axis=2).reshape(chunks, groups * 2 * width, -1)
    selector = (
        station_order[None, :] == jnp.arange(stations, dtype=jnp.int32)[:, None]
    ).astype(jnp.bfloat16)
    selector = selector.reshape(groups, stations_local, stations)
    row_start = lax.axis_index("blk") * row_count

    block_index = jnp.reshape(lax.axis_index("blk"), (1,)).astype(jnp.int32)

    def correlate(chunk, gathered, result):
        if row_count % 128 == 0:
            right = gathered.reshape(width, -1, stations)
            return correlate_rows_chunk(
                right, block_index, row_count, result, chunk * width, local_channels
            )
        gathered = gathered.reshape(width, 2, -1, stations)
        row_block = lax.dynamic_slice_in_dim(gathered, row_start, row_count, 3)
        direct = jnp.transpose(row_block, (0, 3, 1, 2))
        swapped = jnp.stack([direct[:, :, 1], -direct[:, :, 0]], axis=2)
        left = jnp.concatenate([direct, swapped], axis=1).reshape(width, 2 * row_count, -1)
        right = gathered.reshape(width, -1, stations)
        return correlate_chunk(left, right, result, chunk * width, local_channels)

    result = None
    pending = []
    for chunk in range(chunks):
        source = filtered
        if chunk >= 2:
            result = correlate(chunk - 2, pending[chunk - 2], result)
            source, result = lax.optimization_barrier((filtered, result))
        spectra = jnp.einsum(
            "kj,nj->kn", weights[chunk], source, preferred_element_type=jnp.float32
        ).astype(jnp.bfloat16)
        spectra = spectra.reshape(groups, 2 * width, stations_local * spectra_local)
        turned = lax.all_to_all(spectra, "stn", split_axis=0, concat_axis=0, tiled=True)
        turned = turned.reshape(groups, 2, width, stations_local, spectra_local)
        ordered = jnp.einsum(
            "gikas,gar->kisr", turned, selector, preferred_element_type=jnp.float32
        ).astype(jnp.bfloat16)
        ordered = ordered.reshape(width * 2, spectra_local, stations)
        pending.append(gathered_along(ordered, "blk", 1))
    for chunk in range(max(0, chunks - 2), chunks):
        result = correlate(chunk, pending[chunk], result)
    return result


def solution(mesh):
    placed = (P(None, "stn", "blk"), P(), P())
    return jax.shard_map(
        per_device,
        mesh=mesh,
        in_specs=placed,
        out_specs=P(None, "stn", "blk", None),
        check_vma=False,
    )
```

```python
import math

import jax
import ml_dtypes
import numpy as np
import jax.numpy as jnp
from jax import lax
from jax.experimental import pallas as pl
from jax.experimental.pallas import tpu as pltpu
from jax.sharding import PartitionSpec as P

epsilon = 1e-06


def passed_along(value, axis, steps):
    count = lax.axis_size(axis)
    initial, last = (max(0, -steps), min(count, count - steps))
    return lax.ppermute(value, axis, [(source, source + steps) for source in range(initial, last)])


def gathered_along(value, axis, dimension):
    count = lax.axis_size(axis)
    parts = [value]
    for shift in range(1, count):
        pairs = [(source, (source + shift) % count) for source in range(count)]
        parts.append(lax.ppermute(value, axis, pairs))
    return jnp.concatenate(parts, axis=dimension)


def chunk_count(local_channels):
    for count in (4, 2):
        if local_channels % count == 0:
            return count
    return 1


def dft_weights(channels, groups, chunks):
    local = channels // groups
    width = local // chunks
    chunk = np.arange(chunks).reshape(chunks, 1, 1, 1)
    group = np.arange(groups).reshape(1, groups, 1, 1)
    inner = np.arange(width).reshape(1, 1, width, 1)
    column = np.arange(channels).reshape(1, 1, 1, channels)
    row = group * local + chunk * width + inner
    phase_index = (row * column % channels).astype(np.float32)
    angle = phase_index * np.float32(2.0 * math.pi / channels)
    cosine = np.cos(angle).astype(ml_dtypes.bfloat16)
    sine = np.sin(angle).astype(ml_dtypes.bfloat16)
    table = np.concatenate([cosine, sine], axis=3)
    return jnp.asarray(table.reshape(chunks, groups * width, 2 * channels))


def fir_rows(taps_ref, extended, count):
    total = taps_ref[0:1, :] * extended[0:count]
    for tap_index in range(1, taps_ref.shape[0]):
        total = total + taps_ref[tap_index : tap_index + 1, :] * extended[tap_index : tap_index + count]
    return total.astype(jnp.bfloat16)


def fir_store(out_ref, station, filtered, channels):
    out_ref[0, station, :, 0:channels] = filtered[0]
    out_ref[0, station, :, channels:] = filtered[1]
    out_ref[1, station, :, 0:channels] = filtered[1]
    out_ref[1, station, :, channels:] = -filtered[0]


def fir_kernel(taps_ref, frames_ref, out_ref):
    halo = taps_ref.shape[0] - 1
    spectra = frames_ref.shape[2]
    channels = frames_ref.shape[3]

    def body(station, carry):
        filtered = []
        for part in range(2):
            frames = frames_ref[part, station].astype(jnp.float32)
            extended = jnp.concatenate([jnp.zeros((halo, channels), jnp.float32), frames], axis=0)
            filtered.append(fir_rows(taps_ref, extended, spectra))
        fir_store(out_ref, station, filtered, channels)
        return carry

    lax.fori_loop(0, frames_ref.shape[1], body, 0)


def fir_edge_kernel(taps_ref, halo_ref, frames_ref, previous_ref, out_ref):
    count = frames_ref.shape[2]
    channels = frames_ref.shape[3]

    def body(station, carry):
        filtered = []
        for part in range(2):
            extended = jnp.concatenate(
                [
                    halo_ref[part, station].astype(jnp.float32),
                    frames_ref[part, station].astype(jnp.float32),
                ],
                axis=0,
            )
            filtered.append(fir_rows(taps_ref, extended, count))
        fir_store(out_ref, station, filtered, channels)
        return carry

    lax.fori_loop(0, frames_ref.shape[1], body, 0)


def filter_frames(fir_taps, earlier, frames):
    tap_count, channels = fir_taps.shape
    _, stations_local, spectra, _ = frames.shape
    out_shape = jax.ShapeDtypeStruct((2, stations_local, spectra, 2 * channels), jnp.bfloat16)
    group = 4 if stations_local % 4 == 0 else 1
    whole = pl.pallas_call(
        fir_kernel,
        grid=(stations_local // group,),
        in_specs=[
            pl.BlockSpec((tap_count, channels), lambda a: (0, 0)),
            pl.BlockSpec((2, group, spectra, channels), lambda a: (0, a, 0, 0)),
        ],
        out_specs=pl.BlockSpec((2, group, spectra, 2 * channels), lambda a: (0, a, 0, 0)),
        out_shape=out_shape,
        cost_estimate=pl.CostEstimate(
            flops=4 * tap_count * frames.size,
            transcendentals=0,
            bytes_accessed=2 * frames.size + 4 * frames.size,
        ),
    )(fir_taps, frames)
    edge = 8
    edge_group = stations_local // 4 if stations_local % 4 == 0 else stations_local
    return pl.pallas_call(
        fir_edge_kernel,
        grid=(stations_local // edge_group,),
        in_specs=[
            pl.BlockSpec((tap_count, channels), lambda a: (0, 0)),
            pl.BlockSpec((2, edge_group, tap_count - 1, channels), lambda a: (0, a, 0, 0)),
            pl.BlockSpec((2, edge_group, edge, channels), lambda a: (0, a, 0, 0)),
            pl.BlockSpec(memory_space=pl.ANY),
        ],
        out_specs=pl.BlockSpec((2, edge_group, edge, 2 * channels), lambda a: (0, a, 0, 0)),
        out_shape=out_shape,
        input_output_aliases={3: 0},
        cost_estimate=pl.CostEstimate(
            flops=4 * tap_count * edge * frames.size // spectra,
            transcendentals=0,
            bytes_accessed=8 * edge * frames.size // spectra,
        ),
    )(fir_taps, earlier, frames, whole)


def correlate_kernel(rows_ref, cols_ref, *refs):
    out_ref = refs[-1]
    row_count = out_ref.shape[2]
    for index in range(out_ref.shape[1]):
        left = rows_ref[index]
        right = cols_ref[index]
        product = jnp.dot(left, right, preferred_element_type=jnp.float32)
        right = right.astype(jnp.float32)
        rows = left[0:row_count].astype(jnp.float32)
        column_power = jnp.sum(right * right, axis=0, keepdims=True)
        row_power = jnp.sum(rows * rows, axis=1, keepdims=True)
        scale_row = lax.rsqrt(row_power + epsilon)
        scale_column = lax.rsqrt(column_power + epsilon)
        out_ref[0, index] = (product[0:row_count] * scale_row * scale_column).astype(out_ref.dtype)
        out_ref[1, index] = (product[row_count:] * scale_row * scale_column).astype(out_ref.dtype)


def correlate_chunk(left, right, previous, offset, local_channels):
    width, double_rows, depth = left.shape
    row_count = double_rows // 2
    stations = right.shape[2]
    step = 4 if width % 4 == 0 and offset % 4 == 0 else 1
    in_specs = [
        pl.BlockSpec((step, double_rows, depth), lambda k: (k, 0, 0)),
        pl.BlockSpec((step, depth, stations), lambda k: (k, 0, 0)),
    ]
    operands = [left, right]
    aliases = {}
    if previous is not None:
        in_specs.append(pl.BlockSpec(memory_space=pl.ANY))
        operands.append(previous)
        aliases = {2: 0}
    return pl.pallas_call(
        correlate_kernel,
        grid=(width // step,),
        in_specs=in_specs,
        out_specs=pl.BlockSpec(
            (2, step, row_count, stations), lambda k: (0, offset // step + k, 0, 0)
        ),
        out_shape=jax.ShapeDtypeStruct((2, local_channels, row_count, stations), jnp.bfloat16),
        input_output_aliases=aliases,
        cost_estimate=pl.CostEstimate(
            flops=2 * width * double_rows * depth * stations,
            transcendentals=width * (row_count + stations),
            bytes_accessed=2 * (left.size + right.size + width * double_rows * stations),
        ),
    )(*operands)


def correlate_rows_kernel(block_ref, rows_ref, cols_ref, *refs):
    out_ref = refs[-1]
    half = cols_ref.shape[1] // 2
    contract_first = (((0,), (0,)), ((), ()))
    for index in range(out_ref.shape[1]):
        rows = rows_ref[index]
        right = cols_ref[index]
        swapped = jnp.concatenate([rows[half:], -rows[:half]], axis=0)
        real_vis = lax.dot_general(rows, right, contract_first, preferred_element_type=jnp.float32)
        imag_vis = lax.dot_general(swapped, right, contract_first, preferred_element_type=jnp.float32)
        right = right.astype(jnp.float32)
        rows = rows.astype(jnp.float32)
        column_power = jnp.sum(right * right, axis=0, keepdims=True)
        row_power = jnp.sum(jnp.transpose(rows * rows), axis=1, keepdims=True)
        scale_row = lax.rsqrt(row_power + epsilon)
        scale_column = lax.rsqrt(column_power + epsilon)
        out_ref[0, index] = (real_vis * scale_row * scale_column).astype(out_ref.dtype)
        out_ref[1, index] = (imag_vis * scale_row * scale_column).astype(out_ref.dtype)


def correlate_rows_chunk(right, block, row_count, previous, offset, local_channels):
    width, depth, stations = right.shape
    step = 4 if width % 4 == 0 and offset % 4 == 0 else 1
    in_specs = [
        pl.BlockSpec((step, depth, row_count), lambda k, b: (k, 0, b[0])),
        pl.BlockSpec((step, depth, stations), lambda k, b: (k, 0, 0)),
    ]
    operands = [block, right, right]
    aliases = {}
    if previous is not None:
        in_specs.append(pl.BlockSpec(memory_space=pl.ANY))
        operands.append(previous)
        aliases = {3: 0}
    grid_spec = pltpu.PrefetchScalarGridSpec(
        num_scalar_prefetch=1,
        grid=(width // step,),
        in_specs=in_specs,
        out_specs=pl.BlockSpec(
            (2, step, row_count, stations), lambda k, b: (0, offset // step + k, 0, 0)
        ),
    )
    return pl.pallas_call(
        correlate_rows_kernel,
        grid_spec=grid_spec,
        out_shape=jax.ShapeDtypeStruct((2, local_channels, row_count, stations), jnp.bfloat16),
        input_output_aliases=aliases,
        cost_estimate=pl.CostEstimate(
            flops=4 * width * row_count * depth * stations,
            transcendentals=width * (row_count + stations),
            bytes_accessed=2 * (right.size + width * depth * row_count + 2 * width * row_count * stations),
        ),
    )(*operands)


def per_device(samples, fir_taps, station_order):
    tap_count = fir_taps.shape[0]
    channels = fir_taps.shape[1]
    stations_local = samples.shape[1]
    spectra_local = samples.shape[2] // channels
    stations = station_order.shape[0]
    groups = lax.axis_size("stn")
    blocks = lax.axis_size("blk")
    local_channels = channels // groups
    row_count = stations // blocks
    chunks = chunk_count(local_channels)
    width = local_channels // chunks

    earlier = samples[:, :, (spectra_local - (tap_count - 1)) * channels :].astype(jnp.bfloat16)
    earlier = earlier.reshape(2, stations_local, tap_count - 1, channels)
    earlier, samples = lax.optimization_barrier((earlier, samples))
    frames = samples.astype(jnp.bfloat16).reshape(2, stations_local, spectra_local, channels)
    earlier = passed_along(earlier, "blk", 1)
    filtered = filter_frames(fir_taps, earlier, frames)
    filtered = filtered.reshape(2 * stations_local * spectra_local, 2 * channels)

    weights = dft_weights(channels, groups, chunks)
    selector = (
        station_order[None, :] == jnp.arange(stations, dtype=jnp.int32)[:, None]
    ).astype(jnp.bfloat16)
    selector = selector.reshape(groups, stations_local, stations)
    row_start = lax.axis_index("blk") * row_count

    block_index = jnp.reshape(lax.axis_index("blk"), (1,)).astype(jnp.int32)

    def correlate(chunk, gathered, result):
        if row_count % 128 == 0:
            right = gathered.reshape(width, -1, stations)
            return correlate_rows_chunk(
                right, block_index, row_count, result, chunk * width, local_channels
            )
        gathered = gathered.reshape(width, 2, -1, stations)
        row_block = lax.dynamic_slice_in_dim(gathered, row_start, row_count, 3)
        direct = jnp.transpose(row_block, (0, 3, 1, 2))
        swapped = jnp.stack([direct[:, :, 1], -direct[:, :, 0]], axis=2)
        left = jnp.concatenate([direct, swapped], axis=1).reshape(width, 2 * row_count, -1)
        right = gathered.reshape(width, -1, stations)
        return correlate_chunk(left, right, result, chunk * width, local_channels)

    result = None
    pending = []
    for chunk in range(chunks):
        source = filtered
        if chunk >= 2:
            result = correlate(chunk - 2, pending[chunk - 2], result)
            source, result = lax.optimization_barrier((filtered, result))
        spectra = jnp.einsum(
            "kj,nj->kn", weights[chunk], source, preferred_element_type=jnp.float32
        ).astype(jnp.bfloat16)
        spectra = spectra.reshape(groups, width, 2 * stations_local * spectra_local)
        turned = lax.all_to_all(spectra, "stn", split_axis=0, concat_axis=0, tiled=True)
        turned = turned.reshape(groups, width, 2, stations_local, spectra_local)
        ordered = jnp.einsum(
            "gkias,gar->kisr", turned, selector, preferred_element_type=jnp.float32
        ).astype(jnp.bfloat16)
        ordered = ordered.reshape(width * 2, spectra_local, stations)
        pending.append(gathered_along(ordered, "blk", 1))
    for chunk in range(max(0, chunks - 2), chunks):
        result = correlate(chunk, pending[chunk], result)
    return result


def solution(mesh):
    placed = (P(None, "stn", "blk"), P(), P())
    return jax.shard_map(
        per_device,
        mesh=mesh,
        in_specs=placed,
        out_specs=P(None, "stn", "blk", None),
        check_vma=False,
    )
```

```python
import math

import jax
import ml_dtypes
import numpy as np
import jax.numpy as jnp
from jax import lax
from jax.experimental import pallas as pl
from jax.experimental.pallas import tpu as pltpu
from jax.sharding import PartitionSpec as P

epsilon = 1e-06


def passed_along(value, axis, steps):
    count = lax.axis_size(axis)
    initial, last = (max(0, -steps), min(count, count - steps))
    return lax.ppermute(value, axis, [(source, source + steps) for source in range(initial, last)])


def gathered_along(value, axis, dimension):
    count = lax.axis_size(axis)
    parts = [value]
    for shift in range(1, count):
        pairs = [(source, (source + shift) % count) for source in range(count)]
        parts.append(lax.ppermute(value, axis, pairs))
    return jnp.concatenate(parts, axis=dimension)


def chunk_count(local_channels):
    for count in (4, 2):
        if local_channels % count == 0:
            return count
    return 1


def dft_weights(channels, groups, chunks):
    local = channels // groups
    width = local // chunks
    chunk = np.arange(chunks).reshape(chunks, 1, 1, 1)
    group = np.arange(groups).reshape(1, groups, 1, 1)
    inner = np.arange(width).reshape(1, 1, width, 1)
    column = np.arange(channels).reshape(1, 1, 1, channels)
    row = group * local + chunk * width + inner
    phase_index = (row * column % channels).astype(np.float32)
    angle = phase_index * np.float32(2.0 * math.pi / channels)
    cosine = np.cos(angle).astype(ml_dtypes.bfloat16)
    sine = np.sin(angle).astype(ml_dtypes.bfloat16)
    table = np.concatenate([cosine, sine], axis=3)
    return jnp.asarray(table.reshape(chunks, groups * width, 2 * channels))


def fir_rows(taps_ref, extended, count):
    total = taps_ref[0:1, :] * extended[0:count]
    for tap_index in range(1, taps_ref.shape[0]):
        total = total + taps_ref[tap_index : tap_index + 1, :] * extended[tap_index : tap_index + count]
    return total.astype(jnp.bfloat16)


def fir_store(out_ref, station, filtered, channels):
    out_ref[0, station, :, 0:channels] = filtered[0]
    out_ref[0, station, :, channels:] = filtered[1]
    out_ref[1, station, :, 0:channels] = filtered[1]
    out_ref[1, station, :, channels:] = -filtered[0]


def fir_kernel(taps_ref, frames_ref, out_ref):
    halo = taps_ref.shape[0] - 1
    spectra = frames_ref.shape[2]
    channels = frames_ref.shape[3]

    def body(station, carry):
        filtered = []
        for part in range(2):
            frames = frames_ref[part, station].astype(jnp.float32)
            extended = jnp.concatenate([jnp.zeros((halo, channels), jnp.float32), frames], axis=0)
            filtered.append(fir_rows(taps_ref, extended, spectra))
        fir_store(out_ref, station, filtered, channels)
        return carry

    lax.fori_loop(0, frames_ref.shape[1], body, 0)


def fir_edge_kernel(taps_ref, halo_ref, frames_ref, previous_ref, out_ref):
    count = frames_ref.shape[2]
    channels = frames_ref.shape[3]

    def body(station, carry):
        filtered = []
        for part in range(2):
            extended = jnp.concatenate(
                [
                    halo_ref[part, station].astype(jnp.float32),
                    frames_ref[part, station].astype(jnp.float32),
                ],
                axis=0,
            )
            filtered.append(fir_rows(taps_ref, extended, count))
        fir_store(out_ref, station, filtered, channels)
        return carry

    lax.fori_loop(0, frames_ref.shape[1], body, 0)


def filter_frames(fir_taps, earlier, frames):
    tap_count, channels = fir_taps.shape
    _, stations_local, spectra, _ = frames.shape
    out_shape = jax.ShapeDtypeStruct((2, stations_local, spectra, 2 * channels), jnp.bfloat16)
    group = 4 if stations_local % 4 == 0 else 1
    whole = pl.pallas_call(
        fir_kernel,
        grid=(stations_local // group,),
        in_specs=[
            pl.BlockSpec((tap_count, channels), lambda a: (0, 0)),
            pl.BlockSpec((2, group, spectra, channels), lambda a: (0, a, 0, 0)),
        ],
        out_specs=pl.BlockSpec((2, group, spectra, 2 * channels), lambda a: (0, a, 0, 0)),
        out_shape=out_shape,
        cost_estimate=pl.CostEstimate(
            flops=4 * tap_count * frames.size,
            transcendentals=0,
            bytes_accessed=2 * frames.size + 4 * frames.size,
        ),
    )(fir_taps, frames)
    edge = 8
    edge_group = stations_local // 4 if stations_local % 4 == 0 else stations_local
    return pl.pallas_call(
        fir_edge_kernel,
        grid=(stations_local // edge_group,),
        in_specs=[
            pl.BlockSpec((tap_count, channels), lambda a: (0, 0)),
            pl.BlockSpec((2, edge_group, tap_count - 1, channels), lambda a: (0, a, 0, 0)),
            pl.BlockSpec((2, edge_group, edge, channels), lambda a: (0, a, 0, 0)),
            pl.BlockSpec(memory_space=pl.ANY),
        ],
        out_specs=pl.BlockSpec((2, edge_group, edge, 2 * channels), lambda a: (0, a, 0, 0)),
        out_shape=out_shape,
        input_output_aliases={3: 0},
        cost_estimate=pl.CostEstimate(
            flops=4 * tap_count * edge * frames.size // spectra,
            transcendentals=0,
            bytes_accessed=8 * edge * frames.size // spectra,
        ),
    )(fir_taps, earlier, frames, whole)


def correlate_kernel(rows_ref, cols_ref, *refs):
    out_ref = refs[-1]
    row_count = out_ref.shape[2]
    for index in range(out_ref.shape[1]):
        left = rows_ref[index]
        right = cols_ref[index]
        product = jnp.dot(left, right, preferred_element_type=jnp.float32)
        right = right.astype(jnp.float32)
        rows = left[0:row_count].astype(jnp.float32)
        column_power = jnp.sum(right * right, axis=0, keepdims=True)
        row_power = jnp.sum(rows * rows, axis=1, keepdims=True)
        scale_row = lax.rsqrt(row_power + epsilon)
        scale_column = lax.rsqrt(column_power + epsilon)
        out_ref[0, index] = (product[0:row_count] * scale_row * scale_column).astype(out_ref.dtype)
        out_ref[1, index] = (product[row_count:] * scale_row * scale_column).astype(out_ref.dtype)


def correlate_chunk(left, right, previous, offset, local_channels):
    width, double_rows, depth = left.shape
    row_count = double_rows // 2
    stations = right.shape[2]
    step = 4 if width % 4 == 0 and offset % 4 == 0 else 1
    in_specs = [
        pl.BlockSpec((step, double_rows, depth), lambda k: (k, 0, 0)),
        pl.BlockSpec((step, depth, stations), lambda k: (k, 0, 0)),
    ]
    operands = [left, right]
    aliases = {}
    if previous is not None:
        in_specs.append(pl.BlockSpec(memory_space=pl.ANY))
        operands.append(previous)
        aliases = {2: 0}
    return pl.pallas_call(
        correlate_kernel,
        grid=(width // step,),
        in_specs=in_specs,
        out_specs=pl.BlockSpec(
            (2, step, row_count, stations), lambda k: (0, offset // step + k, 0, 0)
        ),
        out_shape=jax.ShapeDtypeStruct((2, local_channels, row_count, stations), jnp.bfloat16),
        input_output_aliases=aliases,
        cost_estimate=pl.CostEstimate(
            flops=2 * width * double_rows * depth * stations,
            transcendentals=width * (row_count + stations),
            bytes_accessed=2 * (left.size + right.size + width * double_rows * stations),
        ),
    )(*operands)


def correlate_rows_kernel(block_ref, rows_ref, cols_ref, *refs):
    out_ref = refs[-1]
    half = cols_ref.shape[1] // 2
    contract_first = (((0,), (0,)), ((), ()))
    for index in range(out_ref.shape[1]):
        rows = rows_ref[index]
        right = cols_ref[index]
        swapped = jnp.concatenate([rows[half:], -rows[:half]], axis=0)
        real_vis = lax.dot_general(rows, right, contract_first, preferred_element_type=jnp.float32)
        imag_vis = lax.dot_general(swapped, right, contract_first, preferred_element_type=jnp.float32)
        right = right.astype(jnp.float32)
        rows = rows.astype(jnp.float32)
        column_power = jnp.sum(right * right, axis=0, keepdims=True)
        row_power = jnp.sum(jnp.transpose(rows * rows), axis=1, keepdims=True)
        scale_row = lax.rsqrt(row_power + epsilon)
        scale_column = lax.rsqrt(column_power + epsilon)
        out_ref[0, index] = (real_vis * scale_row * scale_column).astype(out_ref.dtype)
        out_ref[1, index] = (imag_vis * scale_row * scale_column).astype(out_ref.dtype)


def correlate_rows_chunk(right, block, row_count, previous, offset, local_channels):
    width, depth, stations = right.shape
    step = 8 if width % 8 == 0 and offset % 8 == 0 else 1
    in_specs = [
        pl.BlockSpec((step, depth, row_count), lambda k, b: (k, 0, b[0])),
        pl.BlockSpec((step, depth, stations), lambda k, b: (k, 0, 0)),
    ]
    operands = [block, right, right]
    aliases = {}
    if previous is not None:
        in_specs.append(pl.BlockSpec(memory_space=pl.ANY))
        operands.append(previous)
        aliases = {3: 0}
    grid_spec = pltpu.PrefetchScalarGridSpec(
        num_scalar_prefetch=1,
        grid=(width // step,),
        in_specs=in_specs,
        out_specs=pl.BlockSpec(
            (2, step, row_count, stations), lambda k, b: (0, offset // step + k, 0, 0)
        ),
    )
    return pl.pallas_call(
        correlate_rows_kernel,
        grid_spec=grid_spec,
        out_shape=jax.ShapeDtypeStruct((2, local_channels, row_count, stations), jnp.bfloat16),
        input_output_aliases=aliases,
        cost_estimate=pl.CostEstimate(
            flops=4 * width * row_count * depth * stations,
            transcendentals=width * (row_count + stations),
            bytes_accessed=2 * (right.size + width * depth * row_count + 2 * width * row_count * stations),
        ),
    )(*operands)


def per_device(samples, fir_taps, station_order):
    tap_count = fir_taps.shape[0]
    channels = fir_taps.shape[1]
    stations_local = samples.shape[1]
    spectra_local = samples.shape[2] // channels
    stations = station_order.shape[0]
    groups = lax.axis_size("stn")
    blocks = lax.axis_size("blk")
    local_channels = channels // groups
    row_count = stations // blocks
    chunks = chunk_count(local_channels)
    width = local_channels // chunks

    earlier = samples[:, :, (spectra_local - (tap_count - 1)) * channels :].astype(jnp.bfloat16)
    earlier = earlier.reshape(2, stations_local, tap_count - 1, channels)
    frames = samples.astype(jnp.bfloat16).reshape(2, stations_local, spectra_local, channels)
    earlier = passed_along(earlier, "blk", 1)
    filtered = filter_frames(fir_taps, earlier, frames)
    filtered = filtered.reshape(2 * stations_local * spectra_local, 2 * channels)

    weights = dft_weights(channels, groups, chunks)
    selector = (
        station_order[None, :] == jnp.arange(stations, dtype=jnp.int32)[:, None]
    ).astype(jnp.bfloat16)
    selector = selector.reshape(groups, stations_local, stations)
    row_start = lax.axis_index("blk") * row_count

    block_index = jnp.reshape(lax.axis_index("blk"), (1,)).astype(jnp.int32)

    def correlate(chunk, gathered, result):
        if row_count % 128 == 0:
            right = gathered.reshape(width, -1, stations)
            return correlate_rows_chunk(
                right, block_index, row_count, result, chunk * width, local_channels
            )
        gathered = gathered.reshape(width, 2, -1, stations)
        row_block = lax.dynamic_slice_in_dim(gathered, row_start, row_count, 3)
        direct = jnp.transpose(row_block, (0, 3, 1, 2))
        swapped = jnp.stack([direct[:, :, 1], -direct[:, :, 0]], axis=2)
        left = jnp.concatenate([direct, swapped], axis=1).reshape(width, 2 * row_count, -1)
        right = gathered.reshape(width, -1, stations)
        return correlate_chunk(left, right, result, chunk * width, local_channels)

    result = None
    pending = []
    for chunk in range(chunks):
        source = filtered
        if chunk >= 2:
            result = correlate(chunk - 2, pending[chunk - 2], result)
            source, result = lax.optimization_barrier((filtered, result))
        spectra = jnp.einsum(
            "kj,nj->kn", weights[chunk], source, preferred_element_type=jnp.float32
        ).astype(jnp.bfloat16)
        spectra = spectra.reshape(groups, width, 2 * stations_local * spectra_local)
        turned = lax.all_to_all(spectra, "stn", split_axis=0, concat_axis=0, tiled=True)
        turned = turned.reshape(groups, width, 2, stations_local, spectra_local)
        ordered = jnp.einsum(
            "gkias,gar->kisr", turned, selector, preferred_element_type=jnp.float32
        ).astype(jnp.bfloat16)
        ordered = ordered.reshape(width * 2, spectra_local, stations)
        pending.append(gathered_along(ordered, "blk", 1))
    for chunk in range(max(0, chunks - 2), chunks):
        result = correlate(chunk, pending[chunk], result)
    return result


def solution(mesh):
    placed = (P(None, "stn", "blk"), P(), P())
    return jax.shard_map(
        per_device,
        mesh=mesh,
        in_specs=placed,
        out_specs=P(None, "stn", "blk", None),
        check_vma=False,
    )
```

```python
import math

import jax
import ml_dtypes
import numpy as np
import jax.numpy as jnp
from jax import lax
from jax.experimental import pallas as pl
from jax.experimental.pallas import tpu as pltpu
from jax.sharding import PartitionSpec as P

epsilon = 1e-06


def passed_along(value, axis, steps):
    count = lax.axis_size(axis)
    initial, last = (max(0, -steps), min(count, count - steps))
    return lax.ppermute(value, axis, [(source, source + steps) for source in range(initial, last)])


def gathered_along(value, axis, dimension):
    count = lax.axis_size(axis)
    parts = [value]
    for shift in range(1, count):
        pairs = [(source, (source + shift) % count) for source in range(count)]
        parts.append(lax.ppermute(value, axis, pairs))
    if dimension is None:
        return parts
    return jnp.concatenate(parts, axis=dimension)


def chunk_count(local_channels):
    for count in (4, 2):
        if local_channels % count == 0:
            return count
    return 1


def dft_weights(channels, groups, chunks):
    local = channels // groups
    width = local // chunks
    chunk = np.arange(chunks).reshape(chunks, 1, 1, 1)
    group = np.arange(groups).reshape(1, groups, 1, 1)
    inner = np.arange(width).reshape(1, 1, width, 1)
    column = np.arange(channels).reshape(1, 1, 1, channels)
    row = group * local + chunk * width + inner
    phase_index = (row * column % channels).astype(np.float32)
    angle = phase_index * np.float32(2.0 * math.pi / channels)
    cosine = np.cos(angle).astype(ml_dtypes.bfloat16)
    sine = np.sin(angle).astype(ml_dtypes.bfloat16)
    table = np.concatenate([cosine, sine], axis=3)
    return jnp.asarray(table.reshape(chunks, groups * width, 2 * channels))


def fir_rows(taps_ref, extended, count):
    total = taps_ref[0:1, :] * extended[0:count]
    for tap_index in range(1, taps_ref.shape[0]):
        total = total + taps_ref[tap_index : tap_index + 1, :] * extended[tap_index : tap_index + count]
    return total.astype(jnp.bfloat16)


def fir_store(out_ref, station, filtered, channels):
    out_ref[0, station, :, 0:channels] = filtered[0]
    out_ref[0, station, :, channels:] = filtered[1]
    out_ref[1, station, :, 0:channels] = filtered[1]
    out_ref[1, station, :, channels:] = -filtered[0]


def fir_kernel(taps_ref, frames_ref, out_ref):
    halo = taps_ref.shape[0] - 1
    spectra = frames_ref.shape[2]
    channels = frames_ref.shape[3]

    def body(station, carry):
        filtered = []
        for part in range(2):
            frames = frames_ref[part, station].astype(jnp.float32)
            extended = jnp.concatenate([jnp.zeros((halo, channels), jnp.float32), frames], axis=0)
            filtered.append(fir_rows(taps_ref, extended, spectra))
        fir_store(out_ref, station, filtered, channels)
        return carry

    lax.fori_loop(0, frames_ref.shape[1], body, 0)


def fir_edge_kernel(taps_ref, halo_ref, frames_ref, previous_ref, out_ref):
    count = frames_ref.shape[2]
    channels = frames_ref.shape[3]

    def body(station, carry):
        filtered = []
        for part in range(2):
            extended = jnp.concatenate(
                [
                    halo_ref[part, station].astype(jnp.float32),
                    frames_ref[part, station].astype(jnp.float32),
                ],
                axis=0,
            )
            filtered.append(fir_rows(taps_ref, extended, count))
        fir_store(out_ref, station, filtered, channels)
        return carry

    lax.fori_loop(0, frames_ref.shape[1], body, 0)


def filter_frames(fir_taps, earlier, frames):
    tap_count, channels = fir_taps.shape
    _, stations_local, spectra, _ = frames.shape
    out_shape = jax.ShapeDtypeStruct((2, stations_local, spectra, 2 * channels), jnp.bfloat16)
    group = 4 if stations_local % 4 == 0 else 1
    whole = pl.pallas_call(
        fir_kernel,
        grid=(stations_local // group,),
        in_specs=[
            pl.BlockSpec((tap_count, channels), lambda a: (0, 0)),
            pl.BlockSpec((2, group, spectra, channels), lambda a: (0, a, 0, 0)),
        ],
        out_specs=pl.BlockSpec((2, group, spectra, 2 * channels), lambda a: (0, a, 0, 0)),
        out_shape=out_shape,
        cost_estimate=pl.CostEstimate(
            flops=4 * tap_count * frames.size,
            transcendentals=0,
            bytes_accessed=2 * frames.size + 4 * frames.size,
        ),
    )(fir_taps, frames)
    edge = 8
    edge_group = stations_local // 4 if stations_local % 4 == 0 else stations_local
    return pl.pallas_call(
        fir_edge_kernel,
        grid=(stations_local // edge_group,),
        in_specs=[
            pl.BlockSpec((tap_count, channels), lambda a: (0, 0)),
            pl.BlockSpec((2, edge_group, tap_count - 1, channels), lambda a: (0, a, 0, 0)),
            pl.BlockSpec((2, edge_group, edge, channels), lambda a: (0, a, 0, 0)),
            pl.BlockSpec(memory_space=pl.ANY),
        ],
        out_specs=pl.BlockSpec((2, edge_group, edge, 2 * channels), lambda a: (0, a, 0, 0)),
        out_shape=out_shape,
        input_output_aliases={3: 0},
        cost_estimate=pl.CostEstimate(
            flops=4 * tap_count * edge * frames.size // spectra,
            transcendentals=0,
            bytes_accessed=8 * edge * frames.size // spectra,
        ),
    )(fir_taps, earlier, frames, whole)


def correlate_kernel(rows_ref, cols_ref, *refs):
    out_ref = refs[-1]
    row_count = out_ref.shape[2]
    for index in range(out_ref.shape[1]):
        left = rows_ref[index]
        right = cols_ref[index]
        product = jnp.dot(left, right, preferred_element_type=jnp.float32)
        right = right.astype(jnp.float32)
        rows = left[0:row_count].astype(jnp.float32)
        column_power = jnp.sum(right * right, axis=0, keepdims=True)
        row_power = jnp.sum(rows * rows, axis=1, keepdims=True)
        scale_row = lax.rsqrt(row_power + epsilon)
        scale_column = lax.rsqrt(column_power + epsilon)
        out_ref[0, index] = (product[0:row_count] * scale_row * scale_column).astype(out_ref.dtype)
        out_ref[1, index] = (product[row_count:] * scale_row * scale_column).astype(out_ref.dtype)


def correlate_chunk(left, right, previous, offset, local_channels):
    width, double_rows, depth = left.shape
    row_count = double_rows // 2
    stations = right.shape[2]
    step = 4 if width % 4 == 0 and offset % 4 == 0 else 1
    in_specs = [
        pl.BlockSpec((step, double_rows, depth), lambda k: (k, 0, 0)),
        pl.BlockSpec((step, depth, stations), lambda k: (k, 0, 0)),
    ]
    operands = [left, right]
    aliases = {}
    if previous is not None:
        in_specs.append(pl.BlockSpec(memory_space=pl.ANY))
        operands.append(previous)
        aliases = {2: 0}
    return pl.pallas_call(
        correlate_kernel,
        grid=(width // step,),
        in_specs=in_specs,
        out_specs=pl.BlockSpec(
            (2, step, row_count, stations), lambda k: (0, offset // step + k, 0, 0)
        ),
        out_shape=jax.ShapeDtypeStruct((2, local_channels, row_count, stations), jnp.bfloat16),
        input_output_aliases=aliases,
        cost_estimate=pl.CostEstimate(
            flops=2 * width * double_rows * depth * stations,
            transcendentals=width * (row_count + stations),
            bytes_accessed=2 * (left.size + right.size + width * double_rows * stations),
        ),
    )(*operands)


def correlate_rows_kernel(block_ref, rows_ref, cols_ref, *refs):
    out_ref = refs[-1]
    half = cols_ref.shape[1] // 2
    contract_first = (((0,), (0,)), ((), ()))
    for index in range(out_ref.shape[1]):
        rows = rows_ref[index]
        right = cols_ref[index]
        swapped = jnp.concatenate([rows[half:], -rows[:half]], axis=0)
        real_vis = lax.dot_general(rows, right, contract_first, preferred_element_type=jnp.float32)
        imag_vis = lax.dot_general(swapped, right, contract_first, preferred_element_type=jnp.float32)
        right = right.astype(jnp.float32)
        rows = rows.astype(jnp.float32)
        column_power = jnp.sum(right * right, axis=0, keepdims=True)
        row_power = jnp.sum(jnp.transpose(rows * rows), axis=1, keepdims=True)
        scale_row = lax.rsqrt(row_power + epsilon)
        scale_column = lax.rsqrt(column_power + epsilon)
        out_ref[0, index] = (real_vis * scale_row * scale_column).astype(out_ref.dtype)
        out_ref[1, index] = (imag_vis * scale_row * scale_column).astype(out_ref.dtype)


def correlate_rows_chunk(right, block, row_count, previous, offset, local_channels):
    width, depth, stations = right.shape
    step = 8 if width % 8 == 0 and offset % 8 == 0 else 1
    in_specs = [
        pl.BlockSpec((step, depth, row_count), lambda k, b: (k, 0, b[0])),
        pl.BlockSpec((step, depth, stations), lambda k, b: (k, 0, 0)),
    ]
    operands = [block, right, right]
    aliases = {}
    if previous is not None:
        in_specs.append(pl.BlockSpec(memory_space=pl.ANY))
        operands.append(previous)
        aliases = {3: 0}
    grid_spec = pltpu.PrefetchScalarGridSpec(
        num_scalar_prefetch=1,
        grid=(width // step,),
        in_specs=in_specs,
        out_specs=pl.BlockSpec(
            (2, step, row_count, stations), lambda k, b: (0, offset // step + k, 0, 0)
        ),
    )
    return pl.pallas_call(
        correlate_rows_kernel,
        grid_spec=grid_spec,
        out_shape=jax.ShapeDtypeStruct((2, local_channels, row_count, stations), jnp.bfloat16),
        input_output_aliases=aliases,
        cost_estimate=pl.CostEstimate(
            flops=4 * width * row_count * depth * stations,
            transcendentals=width * (row_count + stations),
            bytes_accessed=2 * (right.size + width * depth * row_count + 2 * width * row_count * stations),
        ),
    )(*operands)


def correlate_pieces_kernel(block_ref, *refs):
    out_ref = refs[-1]
    pieces = (len(refs) - 1) // 2
    rows_refs = refs[0:pieces]
    cols_refs = refs[pieces : 2 * pieces]
    contract_first = (((0,), (0,)), ((), ()))
    for index in range(out_ref.shape[1]):
        rows = jnp.concatenate(
            [ref[index, part] for part in range(2) for ref in rows_refs], axis=0
        )
        right = jnp.concatenate(
            [ref[index, part] for part in range(2) for ref in cols_refs], axis=0
        )
        half = rows.shape[0] // 2
        swapped = jnp.concatenate([rows[half:], -rows[:half]], axis=0)
        real_vis = lax.dot_general(rows, right, contract_first, preferred_element_type=jnp.float32)
        imag_vis = lax.dot_general(swapped, right, contract_first, preferred_element_type=jnp.float32)
        right = right.astype(jnp.float32)
        rows = rows.astype(jnp.float32)
        column_power = jnp.sum(right * right, axis=0, keepdims=True)
        row_power = jnp.sum(jnp.transpose(rows * rows), axis=1, keepdims=True)
        scale_row = lax.rsqrt(row_power + epsilon)
        scale_column = lax.rsqrt(column_power + epsilon)
        out_ref[0, index] = (real_vis * scale_row * scale_column).astype(out_ref.dtype)
        out_ref[1, index] = (imag_vis * scale_row * scale_column).astype(out_ref.dtype)


def correlate_pieces_chunk(parts, block, row_count, previous, offset, local_channels):
    width, _, spectra, stations = parts[0].shape
    step = 4 if width % 4 == 0 and offset % 4 == 0 else 1
    rows_spec = pl.BlockSpec((step, 2, spectra, row_count), lambda k, b: (k, 0, 0, b[0]))
    cols_spec = pl.BlockSpec((step, 2, spectra, stations), lambda k, b: (k, 0, 0, 0))
    in_specs = [rows_spec] * len(parts) + [cols_spec] * len(parts)
    operands = [block] + list(parts) + list(parts)
    aliases = {}
    if previous is not None:
        in_specs.append(pl.BlockSpec(memory_space=pl.ANY))
        operands.append(previous)
        aliases = {len(operands) - 1: 0}
    grid_spec = pltpu.PrefetchScalarGridSpec(
        num_scalar_prefetch=1,
        grid=(width // step,),
        in_specs=in_specs,
        out_specs=pl.BlockSpec(
            (2, step, row_count, stations), lambda k, b: (0, offset // step + k, 0, 0)
        ),
    )
    depth = 2 * spectra * len(parts)
    return pl.pallas_call(
        correlate_pieces_kernel,
        grid_spec=grid_spec,
        out_shape=jax.ShapeDtypeStruct((2, local_channels, row_count, stations), jnp.bfloat16),
        input_output_aliases=aliases,
        cost_estimate=pl.CostEstimate(
            flops=4 * width * row_count * depth * stations,
            transcendentals=width * (row_count + stations),
            bytes_accessed=2 * width * depth * (stations + row_count)
            + 4 * width * row_count * stations,
        ),
    )(*operands)


def per_device(samples, fir_taps, station_order):
    tap_count = fir_taps.shape[0]
    channels = fir_taps.shape[1]
    stations_local = samples.shape[1]
    spectra_local = samples.shape[2] // channels
    stations = station_order.shape[0]
    groups = lax.axis_size("stn")
    blocks = lax.axis_size("blk")
    local_channels = channels // groups
    row_count = stations // blocks
    chunks = chunk_count(local_channels)
    width = local_channels // chunks

    earlier = samples[:, :, (spectra_local - (tap_count - 1)) * channels :].astype(jnp.bfloat16)
    earlier = earlier.reshape(2, stations_local, tap_count - 1, channels)
    frames = samples.astype(jnp.bfloat16).reshape(2, stations_local, spectra_local, channels)
    earlier = passed_along(earlier, "blk", 1)
    filtered = filter_frames(fir_taps, earlier, frames)
    filtered = filtered.reshape(2 * stations_local * spectra_local, 2 * channels)

    weights = dft_weights(channels, groups, chunks)
    selector = (
        station_order[None, :] == jnp.arange(stations, dtype=jnp.int32)[:, None]
    ).astype(jnp.bfloat16)
    selector = selector.reshape(groups, stations_local, stations)
    row_start = lax.axis_index("blk") * row_count

    block_index = jnp.reshape(lax.axis_index("blk"), (1,)).astype(jnp.int32)

    def correlate(chunk, gathered, result):
        if isinstance(gathered, list):
            if row_count % 128 == 0:
                parts = [part.reshape(width, 2, spectra_local, stations) for part in gathered]
                return correlate_pieces_chunk(
                    parts, block_index, row_count, result, chunk * width, local_channels
                )
            gathered = jnp.concatenate(gathered, axis=1)
        if row_count % 128 == 0:
            right = gathered.reshape(width, -1, stations)
            return correlate_rows_chunk(
                right, block_index, row_count, result, chunk * width, local_channels
            )
        gathered = gathered.reshape(width, 2, -1, stations)
        row_block = lax.dynamic_slice_in_dim(gathered, row_start, row_count, 3)
        direct = jnp.transpose(row_block, (0, 3, 1, 2))
        swapped = jnp.stack([direct[:, :, 1], -direct[:, :, 0]], axis=2)
        left = jnp.concatenate([direct, swapped], axis=1).reshape(width, 2 * row_count, -1)
        right = gathered.reshape(width, -1, stations)
        return correlate_chunk(left, right, result, chunk * width, local_channels)

    result = None
    pending = []
    for chunk in range(chunks):
        source = filtered
        if chunk >= 2:
            result = correlate(chunk - 2, pending[chunk - 2], result)
            source, result = lax.optimization_barrier((filtered, result))
        spectra = jnp.einsum(
            "kj,nj->kn", weights[chunk], source, preferred_element_type=jnp.float32
        ).astype(jnp.bfloat16)
        spectra = spectra.reshape(groups, width, 2 * stations_local * spectra_local)
        turned = lax.all_to_all(spectra, "stn", split_axis=0, concat_axis=0, tiled=True)
        turned = turned.reshape(groups, width, 2, stations_local, spectra_local)
        ordered = jnp.einsum(
            "gkias,gar->kisr", turned, selector, preferred_element_type=jnp.float32
        ).astype(jnp.bfloat16)
        ordered = ordered.reshape(width * 2, spectra_local, stations)
        last = chunk == chunks - 1
        pending.append(gathered_along(ordered, "blk", None if last else 1))
    for chunk in range(max(0, chunks - 2), chunks):
        result = correlate(chunk, pending[chunk], result)
    return result


def solution(mesh):
    placed = (P(None, "stn", "blk"), P(), P())
    return jax.shard_map(
        per_device,
        mesh=mesh,
        in_specs=placed,
        out_specs=P(None, "stn", "blk", None),
        check_vma=False,
    )
```

```python
import math

import jax
import ml_dtypes
import numpy as np
import jax.numpy as jnp
from jax import lax
from jax.experimental import pallas as pl
from jax.experimental.pallas import tpu as pltpu
from jax.sharding import PartitionSpec as P

epsilon = 1e-06


def passed_along(value, axis, steps):
    count = lax.axis_size(axis)
    initial, last = (max(0, -steps), min(count, count - steps))
    return lax.ppermute(value, axis, [(source, source + steps) for source in range(initial, last)])


def gathered_along(value, axis, dimension):
    count = lax.axis_size(axis)
    parts = [value]
    for shift in range(1, count):
        pairs = [(source, (source + shift) % count) for source in range(count)]
        parts.append(lax.ppermute(value, axis, pairs))
    if dimension is None:
        return parts
    return jnp.concatenate(parts, axis=dimension)


def chunk_count(local_channels):
    for count in (4, 2):
        if local_channels % count == 0:
            return count
    return 1


def dft_weights(channels, groups, chunks):
    local = channels // groups
    width = local // chunks
    chunk = np.arange(chunks).reshape(chunks, 1, 1, 1)
    group = np.arange(groups).reshape(1, groups, 1, 1)
    inner = np.arange(width).reshape(1, 1, width, 1)
    column = np.arange(channels).reshape(1, 1, 1, channels)
    row = group * local + chunk * width + inner
    phase_index = (row * column % channels).astype(np.float32)
    angle = phase_index * np.float32(2.0 * math.pi / channels)
    cosine = np.cos(angle).astype(ml_dtypes.bfloat16)
    sine = np.sin(angle).astype(ml_dtypes.bfloat16)
    table = np.concatenate([cosine, sine], axis=3)
    return jnp.asarray(table.reshape(chunks, groups * width, 2 * channels))


def fir_rows(taps_ref, extended, count):
    total = taps_ref[0:1, :] * extended[0:count]
    for tap_index in range(1, taps_ref.shape[0]):
        total = total + taps_ref[tap_index : tap_index + 1, :] * extended[tap_index : tap_index + count]
    return total.astype(jnp.bfloat16)


def fir_store(out_ref, station, filtered, channels):
    out_ref[0, station, :, 0:channels] = filtered[0]
    out_ref[0, station, :, channels:] = filtered[1]
    out_ref[1, station, :, 0:channels] = filtered[1]
    out_ref[1, station, :, channels:] = -filtered[0]


def fir_kernel(taps_ref, frames_ref, out_ref):
    halo = taps_ref.shape[0] - 1
    spectra = frames_ref.shape[2]
    channels = frames_ref.shape[3]

    def body(station, carry):
        filtered = []
        for part in range(2):
            frames = frames_ref[part, station].astype(jnp.float32)
            extended = jnp.concatenate([jnp.zeros((halo, channels), jnp.float32), frames], axis=0)
            filtered.append(fir_rows(taps_ref, extended, spectra))
        fir_store(out_ref, station, filtered, channels)
        return carry

    lax.fori_loop(0, frames_ref.shape[1], body, 0)


def fir_edge_kernel(taps_ref, halo_ref, frames_ref, previous_ref, out_ref):
    count = frames_ref.shape[2]
    channels = frames_ref.shape[3]

    def body(station, carry):
        filtered = []
        for part in range(2):
            extended = jnp.concatenate(
                [
                    halo_ref[part, station].astype(jnp.float32),
                    frames_ref[part, station].astype(jnp.float32),
                ],
                axis=0,
            )
            filtered.append(fir_rows(taps_ref, extended, count))
        fir_store(out_ref, station, filtered, channels)
        return carry

    lax.fori_loop(0, frames_ref.shape[1], body, 0)


def filter_frames(fir_taps, earlier, frames):
    tap_count, channels = fir_taps.shape
    _, stations_local, spectra, _ = frames.shape
    out_shape = jax.ShapeDtypeStruct((2, stations_local, spectra, 2 * channels), jnp.bfloat16)
    group = 4 if stations_local % 4 == 0 else 1
    whole = pl.pallas_call(
        fir_kernel,
        grid=(stations_local // group,),
        in_specs=[
            pl.BlockSpec((tap_count, channels), lambda a: (0, 0)),
            pl.BlockSpec((2, group, spectra, channels), lambda a: (0, a, 0, 0)),
        ],
        out_specs=pl.BlockSpec((2, group, spectra, 2 * channels), lambda a: (0, a, 0, 0)),
        out_shape=out_shape,
        cost_estimate=pl.CostEstimate(
            flops=4 * tap_count * frames.size,
            transcendentals=0,
            bytes_accessed=2 * frames.size + 4 * frames.size,
        ),
    )(fir_taps, frames)
    edge = 8
    edge_group = stations_local // 4 if stations_local % 4 == 0 else stations_local
    return pl.pallas_call(
        fir_edge_kernel,
        grid=(stations_local // edge_group,),
        in_specs=[
            pl.BlockSpec((tap_count, channels), lambda a: (0, 0)),
            pl.BlockSpec((2, edge_group, tap_count - 1, channels), lambda a: (0, a, 0, 0)),
            pl.BlockSpec((2, edge_group, edge, channels), lambda a: (0, a, 0, 0)),
            pl.BlockSpec(memory_space=pl.ANY),
        ],
        out_specs=pl.BlockSpec((2, edge_group, edge, 2 * channels), lambda a: (0, a, 0, 0)),
        out_shape=out_shape,
        input_output_aliases={3: 0},
        cost_estimate=pl.CostEstimate(
            flops=4 * tap_count * edge * frames.size // spectra,
            transcendentals=0,
            bytes_accessed=8 * edge * frames.size // spectra,
        ),
    )(fir_taps, earlier, frames, whole)


def correlate_kernel(rows_ref, cols_ref, *refs):
    out_ref = refs[-1]
    row_count = out_ref.shape[2]
    for index in range(out_ref.shape[1]):
        left = rows_ref[index]
        right = cols_ref[index]
        product = jnp.dot(left, right, preferred_element_type=jnp.float32)
        right = right.astype(jnp.float32)
        rows = left[0:row_count].astype(jnp.float32)
        column_power = jnp.sum(right * right, axis=0, keepdims=True)
        row_power = jnp.sum(rows * rows, axis=1, keepdims=True)
        scale_row = lax.rsqrt(row_power + epsilon)
        scale_column = lax.rsqrt(column_power + epsilon)
        out_ref[0, index] = (product[0:row_count] * scale_row * scale_column).astype(out_ref.dtype)
        out_ref[1, index] = (product[row_count:] * scale_row * scale_column).astype(out_ref.dtype)


def correlate_chunk(left, right, previous, offset, local_channels):
    width, double_rows, depth = left.shape
    row_count = double_rows // 2
    stations = right.shape[2]
    step = 4 if width % 4 == 0 and offset % 4 == 0 else 1
    in_specs = [
        pl.BlockSpec((step, double_rows, depth), lambda k: (k, 0, 0)),
        pl.BlockSpec((step, depth, stations), lambda k: (k, 0, 0)),
    ]
    operands = [left, right]
    aliases = {}
    if previous is not None:
        in_specs.append(pl.BlockSpec(memory_space=pl.ANY))
        operands.append(previous)
        aliases = {2: 0}
    return pl.pallas_call(
        correlate_kernel,
        grid=(width // step,),
        in_specs=in_specs,
        out_specs=pl.BlockSpec(
            (2, step, row_count, stations), lambda k: (0, offset // step + k, 0, 0)
        ),
        out_shape=jax.ShapeDtypeStruct((2, local_channels, row_count, stations), jnp.bfloat16),
        input_output_aliases=aliases,
        cost_estimate=pl.CostEstimate(
            flops=2 * width * double_rows * depth * stations,
            transcendentals=width * (row_count + stations),
            bytes_accessed=2 * (left.size + right.size + width * double_rows * stations),
        ),
    )(*operands)


def correlate_rows_kernel(block_ref, rows_ref, cols_ref, *refs):
    out_ref = refs[-1]
    half = cols_ref.shape[1] // 2
    contract_first = (((0,), (0,)), ((), ()))
    for index in range(out_ref.shape[1]):
        rows = rows_ref[index]
        right = cols_ref[index]
        swapped = jnp.concatenate([rows[half:], -rows[:half]], axis=0)
        real_vis = lax.dot_general(rows, right, contract_first, preferred_element_type=jnp.float32)
        imag_vis = lax.dot_general(swapped, right, contract_first, preferred_element_type=jnp.float32)
        right = right.astype(jnp.float32)
        rows = rows.astype(jnp.float32)
        column_power = jnp.sum(right * right, axis=0, keepdims=True)
        row_power = jnp.sum(jnp.transpose(rows * rows), axis=1, keepdims=True)
        scale_row = lax.rsqrt(row_power + epsilon)
        scale_column = lax.rsqrt(column_power + epsilon)
        out_ref[0, index] = (real_vis * scale_row * scale_column).astype(out_ref.dtype)
        out_ref[1, index] = (imag_vis * scale_row * scale_column).astype(out_ref.dtype)


def correlate_rows_chunk(right, block, row_count, previous, offset, local_channels):
    width, depth, stations = right.shape
    step = 8 if width % 8 == 0 and offset % 8 == 0 else 1
    in_specs = [
        pl.BlockSpec((step, depth, row_count), lambda k, b: (k, 0, b[0])),
        pl.BlockSpec((step, depth, stations), lambda k, b: (k, 0, 0)),
    ]
    operands = [block, right, right]
    aliases = {}
    if previous is not None:
        in_specs.append(pl.BlockSpec(memory_space=pl.ANY))
        operands.append(previous)
        aliases = {3: 0}
    grid_spec = pltpu.PrefetchScalarGridSpec(
        num_scalar_prefetch=1,
        grid=(width // step,),
        in_specs=in_specs,
        out_specs=pl.BlockSpec(
            (2, step, row_count, stations), lambda k, b: (0, offset // step + k, 0, 0)
        ),
    )
    return pl.pallas_call(
        correlate_rows_kernel,
        grid_spec=grid_spec,
        out_shape=jax.ShapeDtypeStruct((2, local_channels, row_count, stations), jnp.bfloat16),
        input_output_aliases=aliases,
        cost_estimate=pl.CostEstimate(
            flops=4 * width * row_count * depth * stations,
            transcendentals=width * (row_count + stations),
            bytes_accessed=2 * (right.size + width * depth * row_count + 2 * width * row_count * stations),
        ),
    )(*operands)


def correlate_pieces_kernel(block_ref, *refs):
    out_ref = refs[-1]
    pieces = (len(refs) - 1) // 2
    rows_refs = refs[0:pieces]
    cols_refs = refs[pieces : 2 * pieces]
    contract_first = (((0,), (0,)), ((), ()))
    for index in range(out_ref.shape[1]):
        rows = jnp.concatenate(
            [ref[index, part] for part in range(2) for ref in rows_refs], axis=0
        )
        right = jnp.concatenate(
            [ref[index, part] for part in range(2) for ref in cols_refs], axis=0
        )
        half = rows.shape[0] // 2
        swapped = jnp.concatenate([rows[half:], -rows[:half]], axis=0)
        real_vis = lax.dot_general(rows, right, contract_first, preferred_element_type=jnp.float32)
        imag_vis = lax.dot_general(swapped, right, contract_first, preferred_element_type=jnp.float32)
        right = right.astype(jnp.float32)
        rows = rows.astype(jnp.float32)
        column_power = jnp.sum(right * right, axis=0, keepdims=True)
        row_power = jnp.sum(jnp.transpose(rows * rows), axis=1, keepdims=True)
        scale_row = lax.rsqrt(row_power + epsilon)
        scale_column = lax.rsqrt(column_power + epsilon)
        out_ref[0, index] = (real_vis * scale_row * scale_column).astype(out_ref.dtype)
        out_ref[1, index] = (imag_vis * scale_row * scale_column).astype(out_ref.dtype)


def correlate_pieces_chunk(parts, block, row_count, previous, offset, local_channels):
    width, _, spectra, stations = parts[0].shape
    step = 8 if width % 8 == 0 and offset % 8 == 0 else 1
    rows_spec = pl.BlockSpec((step, 2, spectra, row_count), lambda k, b: (k, 0, 0, b[0]))
    cols_spec = pl.BlockSpec((step, 2, spectra, stations), lambda k, b: (k, 0, 0, 0))
    in_specs = [rows_spec] * len(parts) + [cols_spec] * len(parts)
    operands = [block] + list(parts) + list(parts)
    aliases = {}
    if previous is not None:
        in_specs.append(pl.BlockSpec(memory_space=pl.ANY))
        operands.append(previous)
        aliases = {len(operands) - 1: 0}
    grid_spec = pltpu.PrefetchScalarGridSpec(
        num_scalar_prefetch=1,
        grid=(width // step,),
        in_specs=in_specs,
        out_specs=pl.BlockSpec(
            (2, step, row_count, stations), lambda k, b: (0, offset // step + k, 0, 0)
        ),
    )
    depth = 2 * spectra * len(parts)
    return pl.pallas_call(
        correlate_pieces_kernel,
        grid_spec=grid_spec,
        out_shape=jax.ShapeDtypeStruct((2, local_channels, row_count, stations), jnp.bfloat16),
        input_output_aliases=aliases,
        cost_estimate=pl.CostEstimate(
            flops=4 * width * row_count * depth * stations,
            transcendentals=width * (row_count + stations),
            bytes_accessed=2 * width * depth * (stations + row_count)
            + 4 * width * row_count * stations,
        ),
    )(*operands)


def per_device(samples, fir_taps, station_order):
    tap_count = fir_taps.shape[0]
    channels = fir_taps.shape[1]
    stations_local = samples.shape[1]
    spectra_local = samples.shape[2] // channels
    stations = station_order.shape[0]
    groups = lax.axis_size("stn")
    blocks = lax.axis_size("blk")
    local_channels = channels // groups
    row_count = stations // blocks
    chunks = chunk_count(local_channels)
    width = local_channels // chunks

    earlier = samples[:, :, (spectra_local - (tap_count - 1)) * channels :].astype(jnp.bfloat16)
    earlier = earlier.reshape(2, stations_local, tap_count - 1, channels)
    frames = samples.astype(jnp.bfloat16).reshape(2, stations_local, spectra_local, channels)
    earlier = passed_along(earlier, "blk", 1)
    filtered = filter_frames(fir_taps, earlier, frames)
    filtered = filtered.reshape(2 * stations_local * spectra_local, 2 * channels)

    weights = dft_weights(channels, groups, chunks)
    selector = (
        station_order[None, :] == jnp.arange(stations, dtype=jnp.int32)[:, None]
    ).astype(jnp.bfloat16)
    selector = selector.reshape(groups, stations_local, stations)
    row_start = lax.axis_index("blk") * row_count

    block_index = jnp.reshape(lax.axis_index("blk"), (1,)).astype(jnp.int32)

    def correlate(chunk, gathered, result):
        if isinstance(gathered, list):
            if row_count % 128 == 0:
                parts = [part.reshape(width, 2, spectra_local, stations) for part in gathered]
                return correlate_pieces_chunk(
                    parts, block_index, row_count, result, chunk * width, local_channels
                )
            gathered = jnp.concatenate(gathered, axis=1)
        if row_count % 128 == 0:
            right = gathered.reshape(width, -1, stations)
            return correlate_rows_chunk(
                right, block_index, row_count, result, chunk * width, local_channels
            )
        gathered = gathered.reshape(width, 2, -1, stations)
        row_block = lax.dynamic_slice_in_dim(gathered, row_start, row_count, 3)
        direct = jnp.transpose(row_block, (0, 3, 1, 2))
        swapped = jnp.stack([direct[:, :, 1], -direct[:, :, 0]], axis=2)
        left = jnp.concatenate([direct, swapped], axis=1).reshape(width, 2 * row_count, -1)
        right = gathered.reshape(width, -1, stations)
        return correlate_chunk(left, right, result, chunk * width, local_channels)

    result = None
    pending = []
    for chunk in range(chunks):
        source = filtered
        if chunk >= 2:
            result = correlate(chunk - 2, pending[chunk - 2], result)
            source, result = lax.optimization_barrier((filtered, result))
        spectra = jnp.einsum(
            "kj,nj->kn", weights[chunk], source, preferred_element_type=jnp.float32
        ).astype(jnp.bfloat16)
        spectra = spectra.reshape(groups, width, 2 * stations_local * spectra_local)
        turned = lax.all_to_all(spectra, "stn", split_axis=0, concat_axis=0, tiled=True)
        turned = turned.reshape(groups, width, 2, stations_local, spectra_local)
        ordered = jnp.einsum(
            "gkias,gar->kisr", turned, selector, preferred_element_type=jnp.float32
        ).astype(jnp.bfloat16)
        ordered = ordered.reshape(width * 2, spectra_local, stations)
        last = chunk == chunks - 1
        pending.append(gathered_along(ordered, "blk", None if last else 1))
    for chunk in range(max(0, chunks - 2), chunks):
        result = correlate(chunk, pending[chunk], result)
    return result


def solution(mesh):
    placed = (P(None, "stn", "blk"), P(), P())
    return jax.shard_map(
        per_device,
        mesh=mesh,
        in_specs=placed,
        out_specs=P(None, "stn", "blk", None),
        check_vma=False,
    )
```
